32 devices in a mesh: ctx: 8 (over z, y), tp: 4 (over x, core).
Axes of the slice: x: 2, y: 2, z: 4, core: 2. Of those that a mesh axis runs over, the one named last changes fastest.
Arguments:
- tokens: bfloat16 [6144, 4096], P('ctx'), may hold values from -6 to 6
- in_weight: bfloat16 [4096, 3, 4096], P('ctx', None, 'tp'), may hold values from -0.09375 to 0.09375
- short_taps: float32 [3, 4096, 7], P(None, 'tp'), may hold values from -2.5 to 2.5
- medium_taps: float32 [4096, 128], P('tp'), may hold values from -2 to 2
- medium_decay: float32 [4096], P('tp'), may hold values from 0.01 to 0.3
- skip_gain: float32 [4096], P('tp'), may hold values from 0.5 to 1.5
- out_weight: bfloat16 [4096, 4096], P('tp'), may hold values from -0.09375 to 0.09375
Outputs:
- mixed: bfloat16 [6144, 4096], P('ctx', 'tp')
The draws below stay inside these ranges and needn't reach their ends.
All inputs are finite; a program needn't handle non-finite values.
Results may differ from the reference program's by a relative error of at most 0.0072.
Values may be sent and summed in bfloat16 or wider, within the bound.
No kernel may reach another device: no remote copies, remote signals or barrier semaphores. Data moves between devices by JAX's collectives and lax.ppermute only.
A program may use at most 192 MiB of HBM per device.

```python
import math
import jax
import jax.numpy as jnp
from jax import lax

D = 4096
C = 4096
SLEN = 7
MLEN = 128
TOKENS = 6144


def shard_levels(rng, dims, pieces, least, top_value):
    loudness = 1.0
    for axis_at, shards_of in pieces:
        draws = jax.random.uniform(jax.random.fold_in(jax.random.fold_in(rng, 6), axis_at), (shards_of,), jnp.float32, least / len(pieces), top_value / len(pieces))
        loudness = loudness * jnp.repeat(jnp.exp(draws), dims[axis_at] // shards_of).reshape((-1,) + (1,) * (len(dims) - 1 - axis_at))
    return loudness


def gaussian(own_key, shape, scale, bound, shards=(), held_as=jnp.bfloat16):
    factor_of = shard_levels(own_key, shape, shards, -0.22, 0.18) if shards else 1.0
    result = jax.random.normal(own_key, shape, jnp.float32) * scale * factor_of
    return jnp.minimum(jnp.maximum(result, -bound), bound).astype(held_as)


def setup_inputs(seed: int = 0) -> dict:
    splits = jax.random.split(jax.random.key(seed), 8)
    tokens = gaussian(splits[0], (TOKENS, D), 1.0, 6.0, ((0, 8),))
    in_weight = gaussian(splits[1], (D, 3, C), D ** -0.5, 0.09375, ((0, 8), (2, 4)))
    short_taps = gaussian(splits[2], (3, C, SLEN), 0.4, 2.5, ((1, 4),), jnp.float32)
    medium_taps = gaussian(splits[3], (C, MLEN), 0.3, 2.0, ((0, 4),), jnp.float32)
    medium_decay = jnp.clip(jnp.exp(math.log(0.3) - 3.4011974 * jax.random.uniform(splits[4], (C,), jnp.float32) ** shard_levels(splits[4], (C,), ((0, 4),), -0.2, 0.2)), 0.01, 0.3)
    skip_gain = jnp.clip(0.5 + 1.0 * jax.random.uniform(splits[5], (C,), jnp.float32) ** shard_levels(splits[5], (C,), ((0, 4),), -0.2, 0.2), 0.5, 1.5)
    out_weight = gaussian(splits[6], (C, D), C ** -0.5, 0.09375, ((0, 4),))
    return {"tokens": tokens, "in_weight": in_weight, "short_taps": short_taps, "medium_taps": medium_taps, "medium_decay": medium_decay, "skip_gain": skip_gain, "out_weight": out_weight}


def reference(tokens, in_weight, short_taps, medium_taps, medium_decay, skip_gain, out_weight):
    features = jnp.dot(tokens, in_weight.reshape(D, 3 * C), preferred_element_type=jnp.float32)
    features = features.astype(jnp.bfloat16).reshape(TOKENS, 3, C)
    widened = jnp.pad(features.astype(jnp.float32), ((SLEN - 1, 0), (0, 0), (0, 0)))
    smoothed = jnp.zeros((TOKENS, 3, C), jnp.float32)
    for lag_step in range(SLEN):
        start_row = SLEN - 1 - lag_step
        smoothed = smoothed + short_taps[:, :, lag_step][None, :, :] * widened[start_row:start_row + TOKENS]
    product = smoothed[:, 1, :] * smoothed[:, 2, :]
    lag_values = jnp.arange(MLEN).astype(jnp.float32)
    filters = medium_taps * jnp.exp(-medium_decay[:, None] * lag_values[None, :])
    product_padded = jnp.pad(product, ((MLEN - 1, 0), (0, 0)))

    def add_lag(lag_step, total):
        shifted = lax.dynamic_slice_in_dim(product_padded, (MLEN - 1 - lag_step).astype(jnp.int32), TOKENS, 0)
        weight_row = lax.dynamic_slice_in_dim(filters, lag_step.astype(jnp.int32), 1, 1)[:, 0]
        return total + weight_row[None, :] * shifted

    response = lax.fori_loop(jnp.int32(0), jnp.int32(MLEN), add_lag, skip_gain[None, :] * product)
    gated = (smoothed[:, 0, :] * response).astype(jnp.bfloat16)
    return jnp.dot(gated, out_weight, preferred_element_type=jnp.float32).astype(jnp.bfloat16)
```

```python
import jax
import jax.numpy as jnp
from jax import lax
from jax.sharding import PartitionSpec as P


def skewed(extended):
    group_size = extended.shape[0]
    width = extended.shape[1] // 2
    reverse = extended[:, ::-1]
    tiled = jnp.tile(reverse, (1, width))
    flat = tiled[:, width - 1 : width - 1 + width * (2 * width - 1)]
    return flat.reshape(group_size, width, 2 * width - 1)[:, :, :width]


def toeplitz_pair(filters):
    blank = jnp.zeros(filters.shape, jnp.float32)
    lower = skewed(jnp.concatenate([blank, filters], axis=1))
    upper = skewed(jnp.concatenate([filters, blank], axis=1))
    return (lower, upper)


def channel_filter(fields, short_weights, filters, skip_weights):
    group_size = fields.shape[1]
    length = fields.shape[2]
    short_count = short_weights.shape[2]
    medium_count = filters.shape[1]
    widened = jnp.pad(fields.astype(jnp.float32), ((0, 0), (0, 0), (short_count - 1, 0)))
    smoothed = jnp.zeros(fields.shape, jnp.float32)
    for lag_step in range(short_count):
        start_col = short_count - 1 - lag_step
        smoothed = (
            smoothed
            + short_weights[:, :, lag_step : lag_step + 1]
            * widened[:, :, start_col : start_col + length]
        )
    product = smoothed[1] * smoothed[2]
    blocks = product.reshape(group_size, -1, medium_count)
    earlier = jnp.concatenate(
        [jnp.zeros((group_size, 1, medium_count), jnp.float32), blocks[:, :-1]], axis=1
    )
    lower, upper = toeplitz_pair(filters)
    response = jnp.einsum("cbj,cij->cbi", blocks, lower, precision=lax.Precision.HIGHEST)
    response = response + jnp.einsum(
        "cbj,cij->cbi", earlier, upper, precision=lax.Precision.HIGHEST
    )
    response = response.reshape(group_size, -1)
    return (smoothed[0] * (response + skip_weights[:, None] * product)).astype(jnp.bfloat16)


def ring_order(count):
    if count % 2:
        return list(range(count))
    return list(range(0, count, 2)) + list(range(count - 1, 0, -2))


def ring_projection(tokens, in_weight):
    count = lax.axis_size("ctx")
    rows = in_weight.shape[0]
    order = ring_order(count)
    place = [0] * count
    for at, member in enumerate(order):
        place[member] = at
    forward = [(order[k], order[(k + 1) % count]) for k in range(count)]
    backward = [(order[k], order[(k - 1) % count]) for k in range(count)]
    me = lax.axis_index("ctx")
    order_table = jnp.array(order, jnp.int32)
    my_place = jnp.array(place, jnp.int32)[me]

    def partial(block, source, start, width):
        cols = lax.dynamic_slice_in_dim(tokens, source * rows + start, width, 1)
        return jnp.einsum("rd,dkc->rkc", cols, block, preferred_element_type=jnp.float32)

    total = partial(in_weight, me, 0, rows)
    full_steps = (count - 1) // 2
    half = rows // 2

    def sources(step):
        return (
            order_table[(my_place - step) % count],
            order_table[(my_place + step) % count],
        )

    def add_pair(total, ahead, behind, step):
        from_behind, from_ahead = sources(step)
        total = total + partial(ahead, from_behind, 0, rows)
        return total + partial(behind, from_ahead, 0, rows)

    def ring_step(step, carry):
        ahead, behind, total = carry
        moved_ahead = lax.ppermute(ahead, "ctx", forward)
        moved_behind = lax.ppermute(behind, "ctx", backward)
        total = add_pair(total, ahead, behind, step - 1)
        return (moved_ahead, moved_behind, total)

    if full_steps == 0:
        return total
    ahead = lax.ppermute(in_weight, "ctx", forward)
    behind = lax.ppermute(in_weight, "ctx", backward)
    ahead, behind, total = lax.fori_loop(
        2, full_steps + 1, ring_step, (ahead, behind, total)
    )
    if count % 2 == 0:
        last_ahead = lax.ppermute(ahead[:half], "ctx", forward)
        last_behind = lax.ppermute(behind[half:], "ctx", backward)
        total = add_pair(total, ahead, behind, full_steps)
        from_behind, from_ahead = sources(full_steps + 1)
        total = total + partial(last_ahead, from_behind, 0, half)
        total = total + partial(last_behind, from_ahead, half, rows - half)
    else:
        total = add_pair(total, ahead, behind, full_steps)
    return total


def per_device(tokens, in_weight, short_taps, medium_taps, medium_decay, skip_gain, out_weight):
    row_count = tokens.shape[0]
    channel_count = in_weight.shape[2]
    ctx_count = lax.axis_size("ctx")
    group_size = channel_count // ctx_count
    medium_count = medium_taps.shape[1]
    features = ring_projection(tokens, in_weight).astype(jnp.bfloat16)
    lag_values = lax.broadcasted_iota(jnp.float32, (1, medium_count), 1)
    filters = medium_taps * jnp.exp(-medium_decay[:, None] * lag_values)
    tilted = jnp.transpose(features, (1, 2, 0))
    spread = lax.all_to_all(tilted, "ctx", split_axis=1, concat_axis=2, tiled=True)
    offset = lax.axis_index("ctx") * group_size
    short_local = lax.dynamic_slice_in_dim(short_taps, offset, group_size, 1)
    filter_local = lax.dynamic_slice_in_dim(filters, offset, group_size, 0)
    skip_local = lax.dynamic_slice_in_dim(skip_gain, offset, group_size, 0)
    filtered = channel_filter(spread, short_local, filter_local, skip_local)
    filtered = filtered.reshape(group_size, ctx_count, row_count)
    returned = lax.all_to_all(filtered, "ctx", split_axis=1, concat_axis=0, tiled=True)
    gated = returned.reshape(channel_count, row_count)
    summed = lax.psum_scatter(
        lax.dot_general(
            out_weight, gated, (((0,), (0,)), ((), ())), preferred_element_type=jnp.float32
        ),
        "tp",
        scatter_dimension=0,
        tiled=True,
    )
    return jnp.transpose(summed).astype(jnp.bfloat16)


def solution(mesh):
    return jax.shard_map(
        per_device,
        mesh=mesh,
        in_specs=(
            P("ctx", None),
            P("ctx", None, "tp"),
            P(None, "tp", None),
            P("tp", None),
            P("tp"),
            P("tp"),
            P("tp", None),
        ),
        out_specs=P("ctx", "tp"),
        check_vma=False,
    )
```

```python
import jax
import jax.numpy as jnp
from jax import lax
from jax.sharding import PartitionSpec as P


from jax.experimental import pallas as pl
from jax.experimental.pallas import tpu as pltpu

HALO = 136
CHUNK = 64
LANES = 128


def filter_kernel(halo_q, halo_k, halo_v, own_q, own_k, own_v, taps, medium, skip, out,
                  raw, prod, shifted, smooth_q):
    local = own_q.shape[0]
    ext = HALO + local
    taps_count = 7
    short_count = taps.shape[0] // 3

    def load_field(halo_ref, own_ref, slot):
        raw[slot, 0:HALO, :] = halo_ref[...].astype(jnp.float32)
        raw[slot, HALO:ext, :] = own_ref[...].astype(jnp.float32)

    load_field(halo_q, own_q, 0)
    load_field(halo_k, own_k, 1)
    load_field(halo_v, own_v, 2)

    def smooth(slot, first):
        total = jnp.zeros((ext - first, LANES), jnp.float32)
        for lag in range(taps_count):
            weight = taps[pl.ds(slot * short_count + lag, 1), :]
            total = total + weight * raw[slot, pl.ds(first - lag, ext - first), :]
        return total

    smooth_q[...] = smooth(0, HALO)
    prod[8:ext, :] = smooth(1, 8) * smooth(2, 8)
    for shift in range(8):
        shifted[shift, 16:ext, :] = prod[pl.ds(16 - shift, ext - 16), :]

    def chunk_body(index, carry):
        row = pl.multiple_of(index * CHUNK, CHUNK)
        at = pl.multiple_of(row + HALO, 8)
        total = skip[...] * prod[pl.ds(at, CHUNK), :]
        for group in range(medium.shape[0] // 8):
            base = pl.multiple_of(at - 8 * group, 8)
            for shift in range(8):
                weight = medium[pl.ds(8 * group + shift, 1), :]
                total = total + weight * shifted[shift, pl.ds(base, CHUNK), :]
        out[pl.ds(row, CHUNK), :] = (smooth_q[pl.ds(row, CHUNK), :] * total).astype(out.dtype)
        return carry

    lax.fori_loop(0, local // CHUNK, chunk_body, 0)


def channel_filter(halo, own, taps, medium, skip):
    local = own.shape[0]
    channels = own.shape[1] // 3
    tiles = channels // LANES
    ext = HALO + local

    def field_spec(rows, field):
        return pl.BlockSpec((rows, LANES), lambda t: (0, field * tiles + t))

    return pl.pallas_call(
        filter_kernel,
        grid=(tiles,),
        in_specs=[
            field_spec(HALO, 0),
            field_spec(HALO, 1),
            field_spec(HALO, 2),
            field_spec(local, 0),
            field_spec(local, 1),
            field_spec(local, 2),
            pl.BlockSpec((taps.shape[0], LANES), lambda t: (0, t)),
            pl.BlockSpec((medium.shape[0], LANES), lambda t: (0, t)),
            pl.BlockSpec((1, LANES), lambda t: (0, t)),
        ],
        out_specs=pl.BlockSpec((local, LANES), lambda t: (0, t)),
        out_shape=jax.ShapeDtypeStruct((local, channels), jnp.bfloat16),
        scratch_shapes=[
            pltpu.VMEM((3, ext, LANES), jnp.float32),
            pltpu.VMEM((ext, LANES), jnp.float32),
            pltpu.VMEM((8, ext, LANES), jnp.float32),
            pltpu.VMEM((local, LANES), jnp.float32),
        ],
    )(halo, halo, halo, own, own, own, taps, medium, skip)


def ring_order(count):
    if count % 2:
        return list(range(count))
    return list(range(0, count, 2)) + list(range(count - 1, 0, -2))


def ring_projection(tokens, in_weight):
    count = lax.axis_size("ctx")
    rows = in_weight.shape[0]
    order = ring_order(count)
    place = [0] * count
    for at, member in enumerate(order):
        place[member] = at
    forward = [(order[k], order[(k + 1) % count]) for k in range(count)]
    backward = [(order[k], order[(k - 1) % count]) for k in range(count)]
    me = lax.axis_index("ctx")
    order_table = jnp.array(order, jnp.int32)
    my_place = jnp.array(place, jnp.int32)[me]

    def partial(block, source, start, width):
        cols = lax.dynamic_slice_in_dim(tokens, source * rows + start, width, 1)
        return jnp.einsum("rd,dkc->rkc", cols, block, preferred_element_type=jnp.float32)

    total = partial(in_weight, me, 0, rows)
    full_steps = (count - 1) // 2
    half = rows // 2

    def sources(step):
        return (
            order_table[(my_place - step) % count],
            order_table[(my_place + step) % count],
        )

    def add_pair(total, ahead, behind, step):
        from_behind, from_ahead = sources(step)
        total = total + partial(ahead, from_behind, 0, rows)
        return total + partial(behind, from_ahead, 0, rows)

    def ring_step(step, carry):
        ahead, behind, total = carry
        moved_ahead = lax.ppermute(ahead, "ctx", forward)
        moved_behind = lax.ppermute(behind, "ctx", backward)
        total = add_pair(total, ahead, behind, step - 1)
        return (moved_ahead, moved_behind, total)

    if full_steps == 0:
        return total
    ahead = lax.ppermute(in_weight, "ctx", forward)
    behind = lax.ppermute(in_weight, "ctx", backward)
    ahead, behind, total = lax.fori_loop(
        2, full_steps + 1, ring_step, (ahead, behind, total)
    )
    if count % 2 == 0:
        last_ahead = lax.ppermute(ahead[:half], "ctx", forward)
        last_behind = lax.ppermute(behind[half:], "ctx", backward)
        total = add_pair(total, ahead, behind, full_steps)
        from_behind, from_ahead = sources(full_steps + 1)
        total = total + partial(last_ahead, from_behind, 0, half)
        total = total + partial(last_behind, from_ahead, half, rows - half)
    else:
        total = add_pair(total, ahead, behind, full_steps)
    return total


def per_device(tokens, in_weight, short_taps, medium_taps, medium_decay, skip_gain, out_weight):
    row_count = tokens.shape[0]
    channel_count = in_weight.shape[2]
    ctx_count = lax.axis_size("ctx")
    medium_count = medium_taps.shape[1]
    short_count = short_taps.shape[2]
    features = ring_projection(tokens, in_weight).astype(jnp.bfloat16)
    features = features.reshape(row_count, 3 * channel_count)
    halo = lax.ppermute(
        features[row_count - HALO :],
        "ctx",
        [(k, k + 1) for k in range(ctx_count - 1)],
    )
    lag_values = lax.broadcasted_iota(jnp.float32, (1, medium_count), 1)
    filters = medium_taps * jnp.exp(-medium_decay[:, None] * lag_values)
    taps = jnp.pad(
        jnp.transpose(short_taps, (0, 2, 1)), ((0, 0), (0, 8 - short_count), (0, 0))
    ).reshape(3 * 8, channel_count)
    gated = channel_filter(
        halo, features, taps, jnp.transpose(filters), skip_gain.reshape(1, channel_count)
    )
    summed = lax.psum_scatter(
        jnp.dot(gated, out_weight, preferred_element_type=jnp.float32),
        "tp",
        scatter_dimension=1,
        tiled=True,
    )
    return summed.astype(jnp.bfloat16)

def solution(mesh):
    return jax.shard_map(
        per_device,
        mesh=mesh,
        in_specs=(
            P("ctx", None),
            P("ctx", None, "tp"),
            P(None, "tp", None),
            P("tp", None),
            P("tp"),
            P("tp"),
            P("tp", None),
        ),
        out_specs=P("ctx", "tp"),
        check_vma=False,
    )
```

```python
import jax
import jax.numpy as jnp
from jax import lax
from jax.sharding import PartitionSpec as P


from jax.experimental import pallas as pl
from jax.experimental.pallas import tpu as pltpu

HALO = 136
CHUNK = 64
LANES = 128


def filter_kernel(halo_q, halo_k, halo_v, own_q, own_k, own_v, taps, medium, skip, out,
                  raw, prod, shifted, smooth_q):
    local = own_q.shape[0]
    ext = HALO + local
    taps_count = 7
    short_count = taps.shape[0] // 3

    def load_field(halo_ref, own_ref, slot):
        raw[slot, 0:HALO, :] = halo_ref[...].astype(jnp.float32)
        raw[slot, HALO:ext, :] = own_ref[...].astype(jnp.float32)

    load_field(halo_q, own_q, 0)
    load_field(halo_k, own_k, 1)
    load_field(halo_v, own_v, 2)

    def smooth(slot, first):
        total = jnp.zeros((ext - first, LANES), jnp.float32)
        for lag in range(taps_count):
            weight = taps[pl.ds(slot * short_count + lag, 1), :]
            total = total + weight * raw[slot, pl.ds(first - lag, ext - first), :]
        return total

    smooth_q[...] = smooth(0, HALO)
    prod[8:ext, :] = smooth(1, 8) * smooth(2, 8)
    for shift in range(8):
        shifted[shift, 16:ext, :] = prod[pl.ds(16 - shift, ext - 16), :]

    def chunk_body(index, carry):
        row = pl.multiple_of(index * CHUNK, CHUNK)
        at = pl.multiple_of(row + HALO, 8)
        total = skip[...] * prod[pl.ds(at, CHUNK), :]
        for group in range(medium.shape[0] // 8):
            base = pl.multiple_of(at - 8 * group, 8)
            for shift in range(8):
                weight = medium[pl.ds(8 * group + shift, 1), :]
                total = total + weight * shifted[shift, pl.ds(base, CHUNK), :]
        out[pl.ds(row, CHUNK), :] = (smooth_q[pl.ds(row, CHUNK), :] * total).astype(out.dtype)
        return carry

    lax.fori_loop(0, local // CHUNK, chunk_body, 0)


def channel_filter(halo, own, taps, medium, skip):
    local = own.shape[0]
    channels = own.shape[1] // 3
    tiles = channels // LANES
    ext = HALO + local

    def field_spec(rows, field):
        return pl.BlockSpec((rows, LANES), lambda t: (0, field * tiles + t))

    return pl.pallas_call(
        filter_kernel,
        grid=(tiles,),
        in_specs=[
            field_spec(HALO, 0),
            field_spec(HALO, 1),
            field_spec(HALO, 2),
            field_spec(local, 0),
            field_spec(local, 1),
            field_spec(local, 2),
            pl.BlockSpec((taps.shape[0], LANES), lambda t: (0, t)),
            pl.BlockSpec((medium.shape[0], LANES), lambda t: (0, t)),
            pl.BlockSpec((1, LANES), lambda t: (0, t)),
        ],
        out_specs=pl.BlockSpec((local, LANES), lambda t: (0, t)),
        out_shape=jax.ShapeDtypeStruct((local, channels), jnp.bfloat16),
        scratch_shapes=[
            pltpu.VMEM((3, ext, LANES), jnp.float32),
            pltpu.VMEM((ext, LANES), jnp.float32),
            pltpu.VMEM((8, ext, LANES), jnp.float32),
            pltpu.VMEM((local, LANES), jnp.float32),
        ],
    )(halo, halo, halo, own, own, own, taps, medium, skip)


def ring_order(count):
    if count % 2:
        return list(range(count))
    return list(range(0, count, 2)) + list(range(count - 1, 0, -2))


def ring_projection(tokens, in_weight, riders):
    count = lax.axis_size("ctx")
    rows = in_weight.shape[0]
    order = ring_order(count)
    place = [0] * count
    for at, member in enumerate(order):
        place[member] = at
    forward = [(order[k], order[(k + 1) % count]) for k in range(count)]
    backward = [(order[k], order[(k - 1) % count]) for k in range(count)]
    me = lax.axis_index("ctx")
    order_table = jnp.array(order, jnp.int32)
    my_place = jnp.array(place, jnp.int32)[me]

    def partial(block, source, start, width):
        cols = lax.dynamic_slice_in_dim(tokens, source * rows + start, width, 1)
        return jnp.einsum("rd,dkc->rkc", cols, block, preferred_element_type=jnp.float32)

    total = partial(in_weight, me, 0, rows)
    full_steps = (count - 1) // 2
    half = rows // 2

    def sources(step):
        return (
            order_table[(my_place - step) % count],
            order_table[(my_place + step) % count],
        )

    def add_pair(total, ahead, behind, step):
        from_behind, from_ahead = sources(step)
        total = total + partial(ahead, from_behind, 0, rows)
        return total + partial(behind, from_ahead, 0, rows)

    def ring_step(step, carry):
        ahead, behind, total = carry
        moved_ahead = lax.ppermute(ahead, "ctx", forward)
        moved_behind = lax.ppermute(behind, "ctx", backward)
        total = add_pair(total, ahead, behind, step - 1)
        return (moved_ahead, moved_behind, total)

    if full_steps == 0:
        return total, riders
    ahead = lax.ppermute(in_weight, "ctx", forward)
    behind = lax.ppermute(in_weight, "ctx", backward)
    carry = (ahead, behind, total)
    if full_steps >= 2:
        carry = ring_step(2, carry)
    carry, riders = lax.optimization_barrier((carry, riders))

    def carried_step(step, state):
        return (ring_step(step, state[0]), state[1])

    carry, riders = lax.fori_loop(3, full_steps + 1, carried_step, (carry, riders))
    ahead, behind, total = carry
    if count % 2 == 0:
        last_ahead = lax.ppermute(ahead[:half], "ctx", forward)
        last_behind = lax.ppermute(behind[half:], "ctx", backward)
        total = add_pair(total, ahead, behind, full_steps)
        from_behind, from_ahead = sources(full_steps + 1)
        total = total + partial(last_ahead, from_behind, 0, half)
        total = total + partial(last_behind, from_ahead, half, rows - half)
    else:
        total = add_pair(total, ahead, behind, full_steps)
    return total, riders


def tp_bits(count):
    bits = []
    bit = 1
    while bit < count:
        bits.append(bit)
        bit *= 2
    return bits


def spread_weights(out_weight):
    count = lax.axis_size("tp")
    me = lax.axis_index("tp")
    width = out_weight.shape[1] // count
    weights = [lax.dynamic_slice_in_dim(out_weight, me * width, width, 1)]
    for partner in range(1, count):
        pairs = [(k, k ^ partner) for k in range(count)]
        sent = lax.dynamic_slice_in_dim(out_weight, (me ^ partner) * width, width, 1)
        weights.append(lax.ppermute(sent, "tp", pairs))
    return tuple(weights)


def output_projection(gated, weights):
    count = lax.axis_size("tp")
    pieces = {0: gated}
    for bit in reversed(tp_bits(count)):
        pairs = [(k, k ^ bit) for k in range(count)]
        moved = {key ^ bit: lax.ppermute(piece, "tp", pairs) for key, piece in pieces.items()}
        pieces.update(moved)
    total = None
    for key in sorted(pieces):
        part = jnp.dot(pieces[key], weights[key], preferred_element_type=jnp.float32)
        total = part if total is None else total + part
    return total

def per_device(tokens, in_weight, short_taps, medium_taps, medium_decay, skip_gain, out_weight):
    row_count = tokens.shape[0]
    channel_count = in_weight.shape[2]
    ctx_count = lax.axis_size("ctx")
    medium_count = medium_taps.shape[1]
    short_count = short_taps.shape[2]
    features, weights = ring_projection(tokens, in_weight, spread_weights(out_weight))
    features = features.astype(jnp.bfloat16)
    features = features.reshape(row_count, 3 * channel_count)
    halo = lax.ppermute(
        features[row_count - HALO :],
        "ctx",
        [(k, k + 1) for k in range(ctx_count - 1)],
    )
    lag_values = lax.broadcasted_iota(jnp.float32, (1, medium_count), 1)
    filters = medium_taps * jnp.exp(-medium_decay[:, None] * lag_values)
    taps = jnp.pad(
        jnp.transpose(short_taps, (0, 2, 1)), ((0, 0), (0, 8 - short_count), (0, 0))
    ).reshape(3 * 8, channel_count)
    gated = channel_filter(
        halo, features, taps, jnp.transpose(filters), skip_gain.reshape(1, channel_count)
    )
    return output_projection(gated, weights).astype(jnp.bfloat16)

def solution(mesh):
    return jax.shard_map(
        per_device,
        mesh=mesh,
        in_specs=(
            P("ctx", None),
            P("ctx", None, "tp"),
            P(None, "tp", None),
            P("tp", None),
            P("tp"),
            P("tp"),
            P("tp", None),
        ),
        out_specs=P("ctx", "tp"),
        check_vma=False,
    )
```

```python
import jax
import jax.numpy as jnp
from jax import lax
from jax.sharding import PartitionSpec as P


from jax.experimental import pallas as pl
from jax.experimental.pallas import tpu as pltpu

HALO = 136
CHUNK = 64
LANES = 128


def filter_kernel(field_q, field_k, field_v, taps, medium, skip, out,
                  raw, prod, shifted, smooth_q):
    ext = field_q.shape[0]
    local = ext - HALO
    taps_count = 7
    short_count = taps.shape[0] // 3
    raw[0] = field_q[...].astype(jnp.float32)
    raw[1] = field_k[...].astype(jnp.float32)
    raw[2] = field_v[...].astype(jnp.float32)

    def smooth(slot, first):
        total = jnp.zeros((ext - first, LANES), jnp.float32)
        for lag in range(taps_count):
            weight = taps[pl.ds(slot * short_count + lag, 1), :]
            total = total + weight * raw[slot, pl.ds(first - lag, ext - first), :]
        return total

    smooth_q[...] = smooth(0, HALO)
    prod[8:ext, :] = smooth(1, 8) * smooth(2, 8)
    for shift in range(8):
        shifted[shift, 16:ext, :] = prod[pl.ds(16 - shift, ext - 16), :]

    def chunk_body(index, carry):
        row = pl.multiple_of(index * CHUNK, CHUNK)
        at = pl.multiple_of(row + HALO, 8)
        total = skip[...] * prod[pl.ds(at, CHUNK), :]
        for group in range(medium.shape[0] // 8):
            base = pl.multiple_of(at - 8 * group, 8)
            for shift in range(8):
                weight = medium[pl.ds(8 * group + shift, 1), :]
                total = total + weight * shifted[shift, pl.ds(base, CHUNK), :]
        out[pl.ds(row, CHUNK), :] = (smooth_q[pl.ds(row, CHUNK), :] * total).astype(out.dtype)
        return carry

    lax.fori_loop(0, local // CHUNK, chunk_body, 0)


def channel_filter(fields, taps, medium, skip):
    ext = fields.shape[1]
    local = ext - HALO
    channels = fields.shape[2]
    tiles = channels // LANES

    def field_spec(field):
        return pl.BlockSpec((None, ext, LANES), lambda t: (field, 0, t))

    return pl.pallas_call(
        filter_kernel,
        grid=(tiles,),
        in_specs=[
            field_spec(0),
            field_spec(1),
            field_spec(2),
            pl.BlockSpec((taps.shape[0], LANES), lambda t: (0, t)),
            pl.BlockSpec((medium.shape[0], LANES), lambda t: (0, t)),
            pl.BlockSpec((1, LANES), lambda t: (0, t)),
        ],
        out_specs=pl.BlockSpec((local, LANES), lambda t: (0, t)),
        out_shape=jax.ShapeDtypeStruct((local, channels), jnp.bfloat16),
        scratch_shapes=[
            pltpu.VMEM((3, ext, LANES), jnp.float32),
            pltpu.VMEM((ext, LANES), jnp.float32),
            pltpu.VMEM((8, ext, LANES), jnp.float32),
            pltpu.VMEM((local, LANES), jnp.float32),
        ],
    )(fields, fields, fields, taps, medium, skip)

def ring_order(count):
    if count % 2:
        return list(range(count))
    return list(range(0, count, 2)) + list(range(count - 1, 0, -2))


def ring_projection(tokens, in_weight, riders):
    count = lax.axis_size("ctx")
    rows = in_weight.shape[0]
    order = ring_order(count)
    place = [0] * count
    for at, member in enumerate(order):
        place[member] = at
    forward = [(order[k], order[(k + 1) % count]) for k in range(count)]
    backward = [(order[k], order[(k - 1) % count]) for k in range(count)]
    me = lax.axis_index("ctx")
    order_table = jnp.array(order, jnp.int32)
    my_place = jnp.array(place, jnp.int32)[me]

    def partial(block, source, start, width):
        cols = lax.dynamic_slice_in_dim(tokens, source * rows + start, width, 1)
        return jnp.einsum("rd,dkc->krc", cols, block, preferred_element_type=jnp.float32)

    total = partial(in_weight, me, 0, rows)
    full_steps = (count - 1) // 2
    half = rows // 2

    def sources(step):
        return (
            order_table[(my_place - step) % count],
            order_table[(my_place + step) % count],
        )

    def add_pair(total, ahead, behind, step):
        from_behind, from_ahead = sources(step)
        total = total + partial(ahead, from_behind, 0, rows)
        return total + partial(behind, from_ahead, 0, rows)

    def ring_step(step, carry):
        ahead, behind, total = carry
        moved_ahead = lax.ppermute(ahead, "ctx", forward)
        moved_behind = lax.ppermute(behind, "ctx", backward)
        total = add_pair(total, ahead, behind, step - 1)
        return (moved_ahead, moved_behind, total)

    if full_steps == 0:
        return total, riders
    ahead = lax.ppermute(in_weight, "ctx", forward)
    behind = lax.ppermute(in_weight, "ctx", backward)
    carry = (ahead, behind, total)
    if full_steps >= 2:
        carry = ring_step(2, carry)
    carry, riders = lax.optimization_barrier((carry, riders))

    def carried_step(step, state):
        return (ring_step(step, state[0]), state[1])

    carry, riders = lax.fori_loop(3, full_steps + 1, carried_step, (carry, riders))
    ahead, behind, total = carry
    if count % 2 == 0:
        last_ahead = lax.ppermute(ahead[:half], "ctx", forward)
        last_behind = lax.ppermute(behind[half:], "ctx", backward)
        total = add_pair(total, ahead, behind, full_steps)
        from_behind, from_ahead = sources(full_steps + 1)
        total = total + partial(last_ahead, from_behind, 0, half)
        total = total + partial(last_behind, from_ahead, half, rows - half)
    else:
        total = add_pair(total, ahead, behind, full_steps)
    return total, riders


def tp_bits(count):
    bits = []
    bit = 1
    while bit < count:
        bits.append(bit)
        bit *= 2
    return bits


def spread_weights(out_weight):
    count = lax.axis_size("tp")
    me = lax.axis_index("tp")
    width = out_weight.shape[1] // count
    weights = [lax.dynamic_slice_in_dim(out_weight, me * width, width, 1)]
    for partner in range(1, count):
        pairs = [(k, k ^ partner) for k in range(count)]
        sent = lax.dynamic_slice_in_dim(out_weight, (me ^ partner) * width, width, 1)
        weights.append(lax.ppermute(sent, "tp", pairs))
    return tuple(weights)


def output_projection(gated, weights):
    count = lax.axis_size("tp")
    pieces = {0: gated}
    for bit in reversed(tp_bits(count)):
        pairs = [(k, k ^ bit) for k in range(count)]
        moved = {key ^ bit: lax.ppermute(piece, "tp", pairs) for key, piece in pieces.items()}
        pieces.update(moved)
    total = None
    for key in sorted(pieces):
        part = jnp.dot(pieces[key], weights[key], preferred_element_type=jnp.float32)
        total = part if total is None else total + part
    return total

def per_device(tokens, in_weight, short_taps, medium_taps, medium_decay, skip_gain, out_weight):
    row_count = tokens.shape[0]
    channel_count = in_weight.shape[2]
    ctx_count = lax.axis_size("ctx")
    medium_count = medium_taps.shape[1]
    short_count = short_taps.shape[2]
    earlier = lax.ppermute(
        tokens[row_count - HALO :],
        "ctx",
        [(k, k + 1) for k in range(ctx_count - 1)],
    )
    widened = jnp.concatenate([earlier, tokens], axis=0)
    features, weights = ring_projection(widened, in_weight, spread_weights(out_weight))
    features = features.astype(jnp.bfloat16)
    lag_values = lax.broadcasted_iota(jnp.float32, (1, medium_count), 1)
    filters = medium_taps * jnp.exp(-medium_decay[:, None] * lag_values)
    taps = jnp.pad(
        jnp.transpose(short_taps, (0, 2, 1)), ((0, 0), (0, 8 - short_count), (0, 0))
    ).reshape(3 * 8, channel_count)
    gated = channel_filter(
        features, taps, jnp.transpose(filters), skip_gain.reshape(1, channel_count)
    )
    return output_projection(gated, weights).astype(jnp.bfloat16)

def solution(mesh):
    return jax.shard_map(
        per_device,
        mesh=mesh,
        in_specs=(
            P("ctx", None),
            P("ctx", None, "tp"),
            P(None, "tp", None),
            P("tp", None),
            P("tp"),
            P("tp"),
            P("tp", None),
        ),
        out_specs=P("ctx", "tp"),
        check_vma=False,
    )
```

```python
import jax
import jax.numpy as jnp
from jax import lax
from jax.sharding import PartitionSpec as P


from jax.experimental import pallas as pl
from jax.experimental.pallas import tpu as pltpu

HALO = 136
CHUNK = 64
LANES = 128


def filter_kernel(field_q, field_k, field_v, taps, medium, skip, out,
                  raw, prod, shifted, smooth_q):
    ext = field_q.shape[0]
    local = ext - HALO
    taps_count = 7
    short_count = taps.shape[0] // 3
    raw[0] = field_q[...].astype(jnp.float32)
    raw[1] = field_k[...].astype(jnp.float32)
    raw[2] = field_v[...].astype(jnp.float32)

    def smooth(slot, first):
        total = jnp.zeros((ext - first, LANES), jnp.float32)
        for lag in range(taps_count):
            weight = taps[pl.ds(slot * short_count + lag, 1), :]
            total = total + weight * raw[slot, pl.ds(first - lag, ext - first), :]
        return total

    smooth_q[...] = smooth(0, HALO)
    prod[8:ext, :] = smooth(1, 8) * smooth(2, 8)
    for shift in range(8):
        shifted[shift, 16:ext, :] = prod[pl.ds(16 - shift, ext - 16), :]

    def chunk_body(index, carry):
        row = pl.multiple_of(index * CHUNK, CHUNK)
        at = pl.multiple_of(row + HALO, 8)
        total = skip[...] * prod[pl.ds(at, CHUNK), :]
        for group in range(medium.shape[0] // 8):
            base = pl.multiple_of(at - 8 * group, 8)
            for shift in range(8):
                weight = medium[pl.ds(8 * group + shift, 1), :]
                total = total + weight * shifted[shift, pl.ds(base, CHUNK), :]
        out[pl.ds(row, CHUNK), :] = (smooth_q[pl.ds(row, CHUNK), :] * total).astype(out.dtype)
        return carry

    lax.fori_loop(0, local // CHUNK, chunk_body, 0)


def channel_filter(fields, taps, medium, skip):
    ext = fields[0].shape[0]
    local = ext - HALO
    channels = fields[0].shape[1]
    tiles = channels // LANES

    def field_spec(field):
        return pl.BlockSpec((ext, LANES), lambda t: (0, t))

    return pl.pallas_call(
        filter_kernel,
        grid=(tiles,),
        in_specs=[
            field_spec(0),
            field_spec(1),
            field_spec(2),
            pl.BlockSpec((taps.shape[0], LANES), lambda t: (0, t)),
            pl.BlockSpec((medium.shape[0], LANES), lambda t: (0, t)),
            pl.BlockSpec((1, LANES), lambda t: (0, t)),
        ],
        out_specs=pl.BlockSpec((local, LANES), lambda t: (0, t)),
        out_shape=jax.ShapeDtypeStruct((local, channels), jnp.bfloat16),
        scratch_shapes=[
            pltpu.VMEM((3, ext, LANES), jnp.float32),
            pltpu.VMEM((ext, LANES), jnp.float32),
            pltpu.VMEM((8, ext, LANES), jnp.float32),
            pltpu.VMEM((local, LANES), jnp.float32),
        ],
    )(*fields, taps, medium, skip)

def ring_order(count):
    if count % 2:
        return list(range(count))
    return list(range(0, count, 2)) + list(range(count - 1, 0, -2))


def ring_projection(tokens, in_weight, riders):
    count = lax.axis_size("ctx")
    rows = in_weight.shape[0]
    order = ring_order(count)
    place = [0] * count
    for at, member in enumerate(order):
        place[member] = at
    forward = [(order[k], order[(k + 1) % count]) for k in range(count)]
    backward = [(order[k], order[(k - 1) % count]) for k in range(count)]
    me = lax.axis_index("ctx")
    order_table = jnp.array(order, jnp.int32)
    my_place = jnp.array(place, jnp.int32)[me]

    def product(cols, block):
        return tuple(
            jnp.dot(cols, block[:, field, :], preferred_element_type=jnp.float32)
            for field in range(block.shape[1])
        )

    def plus(left, right):
        return tuple(a + b for a, b in zip(left, right))

    def partial(block, source, start, width):
        cols = lax.dynamic_slice_in_dim(tokens, source * rows + start, width, 1)
        return product(cols, block)

    total = partial(in_weight, me, 0, rows)
    full_steps = (count - 1) // 2
    half = rows // 2

    def sources(step):
        return (
            order_table[(my_place - step) % count],
            order_table[(my_place + step) % count],
        )

    def add_pair(total, ahead, behind, step):
        from_behind, from_ahead = sources(step)
        total = plus(total, partial(ahead, from_behind, 0, rows))
        return plus(total, partial(behind, from_ahead, 0, rows))

    def ring_step(step, carry):
        ahead, behind, total = carry
        moved_ahead = lax.ppermute(ahead, "ctx", forward)
        moved_behind = lax.ppermute(behind, "ctx", backward)
        total = add_pair(total, ahead, behind, step - 1)
        return (moved_ahead, moved_behind, total)

    if full_steps == 0:
        return total, riders
    ahead = lax.ppermute(in_weight, "ctx", forward)
    behind = lax.ppermute(in_weight, "ctx", backward)
    carry = (ahead, behind, total)
    if full_steps >= 2:
        carry = ring_step(2, carry)
    carry, riders = lax.optimization_barrier((carry, riders))

    def carried_step(step, state):
        return (ring_step(step, state[0]), state[1])

    carry, riders = lax.fori_loop(3, full_steps + 1, carried_step, (carry, riders))
    ahead, behind, total = carry
    if count % 2 == 0:
        last_ahead = lax.ppermute(ahead[:half], "ctx", forward)
        last_behind = lax.ppermute(behind[half:], "ctx", backward)
        total = add_pair(total, ahead, behind, full_steps)
        from_behind, from_ahead = sources(full_steps + 1)
        cols = jnp.concatenate(
            [
                lax.dynamic_slice_in_dim(tokens, from_behind * rows, half, 1),
                lax.dynamic_slice_in_dim(tokens, from_ahead * rows + half, rows - half, 1),
            ],
            axis=1,
        )
        block = jnp.concatenate([last_ahead, last_behind], axis=0)
        total = plus(total, product(cols, block))
    else:
        total = add_pair(total, ahead, behind, full_steps)
    return total, riders


def tp_bits(count):
    bits = []
    bit = 1
    while bit < count:
        bits.append(bit)
        bit *= 2
    return bits


def spread_weights(out_weight):
    count = lax.axis_size("tp")
    me = lax.axis_index("tp")
    width = out_weight.shape[1] // count
    weights = [lax.dynamic_slice_in_dim(out_weight, me * width, width, 1)]
    for partner in range(1, count):
        pairs = [(k, k ^ partner) for k in range(count)]
        sent = lax.dynamic_slice_in_dim(out_weight, (me ^ partner) * width, width, 1)
        weights.append(lax.ppermute(sent, "tp", pairs))
    return tuple(weights)


def output_projection(gated, weights):
    count = lax.axis_size("tp")
    pieces = {0: gated}
    for bit in reversed(tp_bits(count)):
        pairs = [(k, k ^ bit) for k in range(count)]
        moved = {key ^ bit: lax.ppermute(piece, "tp", pairs) for key, piece in pieces.items()}
        pieces.update(moved)
    total = None
    for key in sorted(pieces):
        part = jnp.dot(pieces[key], weights[key], preferred_element_type=jnp.float32)
        total = part if total is None else total + part
    return total

def per_device(tokens, in_weight, short_taps, medium_taps, medium_decay, skip_gain, out_weight):
    row_count = tokens.shape[0]
    channel_count = in_weight.shape[2]
    ctx_count = lax.axis_size("ctx")
    medium_count = medium_taps.shape[1]
    short_count = short_taps.shape[2]
    earlier = lax.ppermute(
        tokens[row_count - HALO :],
        "ctx",
        [(k, k + 1) for k in range(ctx_count - 1)],
    )
    earlier, in_weight = lax.optimization_barrier((earlier, in_weight))
    widened = jnp.concatenate([earlier, tokens], axis=0)
    features, weights = ring_projection(widened, in_weight, spread_weights(out_weight))
    features = tuple(part.astype(jnp.bfloat16) for part in features)
    lag_values = lax.broadcasted_iota(jnp.float32, (1, medium_count), 1)
    filters = medium_taps * jnp.exp(-medium_decay[:, None] * lag_values)
    taps = jnp.pad(
        jnp.transpose(short_taps, (0, 2, 1)), ((0, 0), (0, 8 - short_count), (0, 0))
    ).reshape(3 * 8, channel_count)
    gated = channel_filter(
        features, taps, jnp.transpose(filters), skip_gain.reshape(1, channel_count)
    )
    return output_projection(gated, weights).astype(jnp.bfloat16)

def solution(mesh):
    return jax.shard_map(
        per_device,
        mesh=mesh,
        in_specs=(
            P("ctx", None),
            P("ctx", None, "tp"),
            P(None, "tp", None),
            P("tp", None),
            P("tp"),
            P("tp"),
            P("tp", None),
        ),
        out_specs=P("ctx", "tp"),
        check_vma=False,
    )
```

```python
import jax
import jax.numpy as jnp
from jax import lax
from jax.sharding import PartitionSpec as P


from jax.experimental import pallas as pl
from jax.experimental.pallas import tpu as pltpu

HALO = 136
CHUNK = 64
LANES = 128


def filter_kernel(field_q, field_k, field_v, taps, medium, skip, out,
                  raw, prod, shifted, smooth_q):
    ext = field_q.shape[0]
    local = ext - HALO
    taps_count = 7
    short_count = taps.shape[0] // 3
    raw[0] = field_q[...].astype(jnp.float32)
    raw[1] = field_k[...].astype(jnp.float32)
    raw[2] = field_v[...].astype(jnp.float32)

    def smooth(slot, first):
        total = jnp.zeros((ext - first, LANES), jnp.float32)
        for lag in range(taps_count):
            weight = taps[pl.ds(slot * short_count + lag, 1), :]
            total = total + weight * raw[slot, pl.ds(first - lag, ext - first), :]
        return total

    smooth_q[...] = smooth(0, HALO)
    prod[8:ext, :] = smooth(1, 8) * smooth(2, 8)
    for shift in range(8):
        shifted[shift, 16:ext, :] = prod[pl.ds(16 - shift, ext - 16), :]

    def chunk_body(index, carry):
        row = pl.multiple_of(index * CHUNK, CHUNK)
        at = pl.multiple_of(row + HALO, 8)
        total = skip[...] * prod[pl.ds(at, CHUNK), :]
        for group in range(medium.shape[0] // 8):
            base = pl.multiple_of(at - 8 * group, 8)
            for shift in range(8):
                weight = medium[pl.ds(8 * group + shift, 1), :]
                total = total + weight * shifted[shift, pl.ds(base, CHUNK), :]
        out[pl.ds(row, CHUNK), :] = (smooth_q[pl.ds(row, CHUNK), :] * total).astype(out.dtype)
        return carry

    lax.fori_loop(0, local // CHUNK, chunk_body, 0)


def channel_filter(fields, taps, medium, skip, first, tiles):
    ext = fields[0].shape[0]
    local = ext - HALO
    channels = tiles * LANES

    def field_spec(field):
        return pl.BlockSpec((ext, LANES), lambda t: (0, first + t))

    return pl.pallas_call(
        filter_kernel,
        grid=(tiles,),
        in_specs=[
            field_spec(0),
            field_spec(1),
            field_spec(2),
            pl.BlockSpec((taps.shape[0], LANES), lambda t: (0, first + t)),
            pl.BlockSpec((medium.shape[0], LANES), lambda t: (0, first + t)),
            pl.BlockSpec((1, LANES), lambda t: (0, first + t)),
        ],
        out_specs=pl.BlockSpec((local, LANES), lambda t: (0, t)),
        out_shape=jax.ShapeDtypeStruct((local, channels), jnp.bfloat16),
        scratch_shapes=[
            pltpu.VMEM((3, ext, LANES), jnp.float32),
            pltpu.VMEM((ext, LANES), jnp.float32),
            pltpu.VMEM((8, ext, LANES), jnp.float32),
            pltpu.VMEM((local, LANES), jnp.float32),
        ],
    )(*fields, taps, medium, skip)

def ring_order(count):
    if count % 2:
        return list(range(count))
    return list(range(0, count, 2)) + list(range(count - 1, 0, -2))


def ring_projection(tokens, in_weight, riders):
    count = lax.axis_size("ctx")
    rows = in_weight.shape[0]
    order = ring_order(count)
    place = [0] * count
    for at, member in enumerate(order):
        place[member] = at
    forward = [(order[k], order[(k + 1) % count]) for k in range(count)]
    backward = [(order[k], order[(k - 1) % count]) for k in range(count)]
    me = lax.axis_index("ctx")
    order_table = jnp.array(order, jnp.int32)
    my_place = jnp.array(place, jnp.int32)[me]

    def product(cols, block):
        return tuple(
            jnp.dot(cols, block[:, field, :], preferred_element_type=jnp.float32)
            for field in range(block.shape[1])
        )

    def plus(left, right):
        return tuple(a + b for a, b in zip(left, right))

    def partial(block, source, start, width):
        cols = lax.dynamic_slice_in_dim(tokens, source * rows + start, width, 1)
        return product(cols, block)

    total = partial(in_weight, me, 0, rows)
    full_steps = (count - 1) // 2
    half = rows // 2

    def sources(step):
        return (
            order_table[(my_place - step) % count],
            order_table[(my_place + step) % count],
        )

    def add_pair(total, ahead, behind, step):
        from_behind, from_ahead = sources(step)
        total = plus(total, partial(ahead, from_behind, 0, rows))
        return plus(total, partial(behind, from_ahead, 0, rows))

    def ring_step(step, carry):
        ahead, behind, total = carry
        moved_ahead = lax.ppermute(ahead, "ctx", forward)
        moved_behind = lax.ppermute(behind, "ctx", backward)
        total = add_pair(total, ahead, behind, step - 1)
        return (moved_ahead, moved_behind, total)

    if full_steps == 0:
        return total, riders
    ahead = lax.ppermute(in_weight, "ctx", forward)
    behind = lax.ppermute(in_weight, "ctx", backward)
    carry = (ahead, behind, total)
    if full_steps >= 2:
        carry = ring_step(2, carry)
    carry, riders = lax.optimization_barrier((carry, riders))

    def carried_step(step, state):
        return (ring_step(step, state[0]), state[1])

    carry, riders = lax.fori_loop(3, full_steps + 1, carried_step, (carry, riders))
    ahead, behind, total = carry
    if count % 2 == 0:
        last_ahead = lax.ppermute(ahead[:half], "ctx", forward)
        last_behind = lax.ppermute(behind[half:], "ctx", backward)
        total = add_pair(total, ahead, behind, full_steps)
        from_behind, from_ahead = sources(full_steps + 1)
        cols = jnp.concatenate(
            [
                lax.dynamic_slice_in_dim(tokens, from_behind * rows, half, 1),
                lax.dynamic_slice_in_dim(tokens, from_ahead * rows + half, rows - half, 1),
            ],
            axis=1,
        )
        block = jnp.concatenate([last_ahead, last_behind], axis=0)
        total = plus(total, product(cols, block))
    else:
        total = add_pair(total, ahead, behind, full_steps)
    return total, riders


def tp_bits(count):
    bits = []
    bit = 1
    while bit < count:
        bits.append(bit)
        bit *= 2
    return bits


def spread_weights(out_weight):
    count = lax.axis_size("tp")
    me = lax.axis_index("tp")
    width = out_weight.shape[1] // count
    weights = [lax.dynamic_slice_in_dim(out_weight, me * width, width, 1)]
    for partner in range(1, count):
        pairs = [(k, k ^ partner) for k in range(count)]
        sent = lax.dynamic_slice_in_dim(out_weight, (me ^ partner) * width, width, 1)
        weights.append(lax.ppermute(sent, "tp", pairs))
    return tuple(weights)


def output_projection(gated, weights):
    count = lax.axis_size("tp")
    pieces = {0: gated}
    for bit in reversed(tp_bits(count)):
        pairs = [(k, k ^ bit) for k in range(count)]
        moved = {key ^ bit: lax.ppermute(piece, "tp", pairs) for key, piece in pieces.items()}
        pieces.update(moved)
    total = None
    for key in sorted(pieces):
        part = jnp.dot(pieces[key], weights[key], preferred_element_type=jnp.float32)
        total = part if total is None else total + part
    return total

def per_device(tokens, in_weight, short_taps, medium_taps, medium_decay, skip_gain, out_weight):
    row_count = tokens.shape[0]
    channel_count = in_weight.shape[2]
    ctx_count = lax.axis_size("ctx")
    medium_count = medium_taps.shape[1]
    short_count = short_taps.shape[2]
    earlier = lax.ppermute(
        tokens[row_count - HALO :],
        "ctx",
        [(k, k + 1) for k in range(ctx_count - 1)],
    )
    earlier, in_weight = lax.optimization_barrier((earlier, in_weight))
    widened = jnp.concatenate([earlier, tokens], axis=0)
    features, weights = ring_projection(widened, in_weight, spread_weights(out_weight))
    features = tuple(part.astype(jnp.bfloat16) for part in features)
    lag_values = lax.broadcasted_iota(jnp.float32, (1, medium_count), 1)
    filters = medium_taps * jnp.exp(-medium_decay[:, None] * lag_values)
    taps = jnp.pad(
        jnp.transpose(short_taps, (0, 2, 1)), ((0, 0), (0, 8 - short_count), (0, 0))
    ).reshape(3 * 8, channel_count)
    tiles = channel_count // LANES
    parts = 2 if tiles % 2 == 0 else 1
    share = tiles // parts
    medium = jnp.transpose(filters)
    skip = skip_gain.reshape(1, channel_count)
    total = None
    for part in range(parts):
        gated = channel_filter(features, taps, medium, skip, part * share, share)
        rows = slice(part * share * LANES, (part + 1) * share * LANES)
        piece = output_projection(gated, tuple(w[rows] for w in weights))
        total = piece if total is None else total + piece
    return total.astype(jnp.bfloat16)

def solution(mesh):
    return jax.shard_map(
        per_device,
        mesh=mesh,
        in_specs=(
            P("ctx", None),
            P("ctx", None, "tp"),
            P(None, "tp", None),
            P("tp", None),
            P("tp"),
            P("tp"),
            P("tp", None),
        ),
        out_specs=P("ctx", "tp"),
        check_vma=False,
    )
```

```python
import jax
import jax.numpy as jnp
from jax import lax
from jax.sharding import PartitionSpec as P


from jax.experimental import pallas as pl
from jax.experimental.pallas import tpu as pltpu

HALO = 136
CHUNK = 64
LANES = 128


def filter_kernel(field_q, field_k, field_v, taps, medium, skip, out,
                  raw, prod, shifted, smooth_q):
    ext = field_q.shape[0]
    local = ext - HALO
    taps_count = 7
    short_count = taps.shape[0] // 3
    raw[0] = field_q[...].astype(jnp.float32)
    raw[1] = field_k[...].astype(jnp.float32)
    raw[2] = field_v[...].astype(jnp.float32)

    def smooth(slot, first):
        total = jnp.zeros((ext - first, LANES), jnp.float32)
        for lag in range(taps_count):
            weight = taps[pl.ds(slot * short_count + lag, 1), :]
            total = total + weight * raw[slot, pl.ds(first - lag, ext - first), :]
        return total

    smooth_q[...] = smooth(0, HALO)
    prod[8:ext, :] = smooth(1, 8) * smooth(2, 8)
    for shift in range(8):
        shifted[shift, 16:ext, :] = prod[pl.ds(16 - shift, ext - 16), :]

    def chunk_body(index, carry):
        row = pl.multiple_of(index * CHUNK, CHUNK)
        at = pl.multiple_of(row + HALO, 8)
        total = skip[...] * prod[pl.ds(at, CHUNK), :]
        for group in range(medium.shape[0] // 8):
            base = pl.multiple_of(at - 8 * group, 8)
            for shift in range(8):
                weight = medium[pl.ds(8 * group + shift, 1), :]
                total = total + weight * shifted[shift, pl.ds(base, CHUNK), :]
        out[pl.ds(row, CHUNK), :] = (smooth_q[pl.ds(row, CHUNK), :] * total).astype(out.dtype)
        return carry

    lax.fori_loop(0, local // CHUNK, chunk_body, 0)


def channel_filter(fields, taps, medium, skip, first, tiles):
    ext = fields[0].shape[0]
    local = ext - HALO
    channels = tiles * LANES

    def field_spec(field):
        return pl.BlockSpec((ext, LANES), lambda t: (0, first + t))

    return pl.pallas_call(
        filter_kernel,
        grid=(tiles,),
        in_specs=[
            field_spec(0),
            field_spec(1),
            field_spec(2),
            pl.BlockSpec((taps.shape[0], LANES), lambda t: (0, first + t)),
            pl.BlockSpec((medium.shape[0], LANES), lambda t: (0, first + t)),
            pl.BlockSpec((1, LANES), lambda t: (0, first + t)),
        ],
        out_specs=pl.BlockSpec((local, LANES), lambda t: (0, t)),
        out_shape=jax.ShapeDtypeStruct((local, channels), jnp.bfloat16),
        scratch_shapes=[
            pltpu.VMEM((3, ext, LANES), jnp.float32),
            pltpu.VMEM((ext, LANES), jnp.float32),
            pltpu.VMEM((8, ext, LANES), jnp.float32),
            pltpu.VMEM((local, LANES), jnp.float32),
        ],
    )(*fields, taps, medium, skip)

def ring_order(count):
    if count % 2:
        return list(range(count))
    return list(range(0, count, 2)) + list(range(count - 1, 0, -2))


def ring_projection(tokens, in_weight, riders):
    count = lax.axis_size("ctx")
    rows = in_weight.shape[0]
    order = ring_order(count)
    place = [0] * count
    for at, member in enumerate(order):
        place[member] = at
    forward = [(order[k], order[(k + 1) % count]) for k in range(count)]
    backward = [(order[k], order[(k - 1) % count]) for k in range(count)]
    me = lax.axis_index("ctx")
    order_table = jnp.array(order, jnp.int32)
    my_place = jnp.array(place, jnp.int32)[me]

    def product(cols, block):
        return tuple(
            jnp.dot(cols, block[:, field, :], preferred_element_type=jnp.float32)
            for field in range(block.shape[1])
        )

    def plus(left, right):
        return tuple(a + b for a, b in zip(left, right))

    def partial(block, source, start, width):
        cols = lax.dynamic_slice_in_dim(tokens, source * rows + start, width, 1)
        return product(cols, block)

    total = partial(in_weight, me, 0, rows)
    full_steps = (count - 1) // 2
    half = rows // 2

    def sources(step):
        return (
            order_table[(my_place - step) % count],
            order_table[(my_place + step) % count],
        )

    def add_pair(total, ahead, behind, step):
        from_behind, from_ahead = sources(step)
        total = plus(total, partial(ahead, from_behind, 0, rows))
        return plus(total, partial(behind, from_ahead, 0, rows))

    def ring_step(step, carry):
        ahead, behind, total = carry
        moved_ahead = lax.ppermute(ahead, "ctx", forward)
        moved_behind = lax.ppermute(behind, "ctx", backward)
        total = add_pair(total, ahead, behind, step - 1)
        return (moved_ahead, moved_behind, total)

    if full_steps == 0:
        return total, riders
    ahead = lax.ppermute(in_weight, "ctx", forward)
    behind = lax.ppermute(in_weight, "ctx", backward)
    carry = (ahead, behind, total)
    if full_steps >= 2:
        carry = ring_step(2, carry)
    carry, riders = lax.optimization_barrier((carry, riders))

    def carried_step(step, state):
        return (ring_step(step, state[0]), state[1])

    carry, riders = lax.fori_loop(3, full_steps + 1, carried_step, (carry, riders))
    ahead, behind, total = carry
    if count % 2 == 0:
        last_ahead = lax.ppermute(ahead[:half], "ctx", forward)
        last_behind = lax.ppermute(behind[half:], "ctx", backward)
        total = add_pair(total, ahead, behind, full_steps)
        from_behind, from_ahead = sources(full_steps + 1)
        cols = jnp.concatenate(
            [
                lax.dynamic_slice_in_dim(tokens, from_behind * rows, half, 1),
                lax.dynamic_slice_in_dim(tokens, from_ahead * rows + half, rows - half, 1),
            ],
            axis=1,
        )
        block = jnp.concatenate([last_ahead, last_behind], axis=0)
        total = plus(total, product(cols, block))
    else:
        total = add_pair(total, ahead, behind, full_steps)
    return total, riders


def tp_bits(count):
    bits = []
    bit = 1
    while bit < count:
        bits.append(bit)
        bit *= 2
    return bits


def spread_weights(out_weight):
    count = lax.axis_size("tp")
    me = lax.axis_index("tp")
    width = out_weight.shape[1] // count
    weights = [lax.dynamic_slice_in_dim(out_weight, me * width, width, 1)]
    for partner in range(1, count):
        pairs = [(k, k ^ partner) for k in range(count)]
        sent = lax.dynamic_slice_in_dim(out_weight, (me ^ partner) * width, width, 1)
        weights.append(lax.ppermute(sent, "tp", pairs))
    return tuple(weights)


def output_projection(gated, weights):
    count = lax.axis_size("tp")
    pieces = {0: gated}
    for bit in reversed(tp_bits(count)):
        pairs = [(k, k ^ bit) for k in range(count)]
        moved = {key ^ bit: lax.ppermute(piece, "tp", pairs) for key, piece in pieces.items()}
        pieces.update(moved)
    total = None
    for key in sorted(pieces):
        part = jnp.dot(pieces[key], weights[key], preferred_element_type=jnp.float32)
        total = part if total is None else total + part
    return total

def halo_rows(tail):
    ctx_count = lax.axis_size("ctx")
    tp_count = lax.axis_size("tp")
    shift = [(k, k + 1) for k in range(ctx_count - 1)]
    if tp_count % 2:
        return lax.ppermute(tail, "ctx", shift)
    width = tail.shape[1] // 2
    side = lax.axis_index("tp") % 2
    mine = lax.ppermute(lax.dynamic_slice_in_dim(tail, side * width, width, 1), "ctx", shift)
    other = lax.ppermute(mine, "tp", [(k, k ^ 1) for k in range(tp_count)])
    return jnp.where(
        side == 0,
        jnp.concatenate([mine, other], axis=1),
        jnp.concatenate([other, mine], axis=1),
    )


def per_device(tokens, in_weight, short_taps, medium_taps, medium_decay, skip_gain, out_weight):
    row_count = tokens.shape[0]
    channel_count = in_weight.shape[2]
    ctx_count = lax.axis_size("ctx")
    medium_count = medium_taps.shape[1]
    short_count = short_taps.shape[2]
    earlier = halo_rows(tokens[row_count - HALO :])
    earlier, in_weight = lax.optimization_barrier((earlier, in_weight))
    widened = jnp.concatenate([earlier, tokens], axis=0)
    features, weights = ring_projection(widened, in_weight, spread_weights(out_weight))
    features = tuple(part.astype(jnp.bfloat16) for part in features)
    lag_values = lax.broadcasted_iota(jnp.float32, (1, medium_count), 1)
    filters = medium_taps * jnp.exp(-medium_decay[:, None] * lag_values)
    taps = jnp.pad(
        jnp.transpose(short_taps, (0, 2, 1)), ((0, 0), (0, 8 - short_count), (0, 0))
    ).reshape(3 * 8, channel_count)
    tiles = channel_count // LANES
    parts = 2 if tiles % 2 == 0 else 1
    share = tiles // parts
    medium = jnp.transpose(filters)
    skip = skip_gain.reshape(1, channel_count)
    total = None
    for part in range(parts):
        gated = channel_filter(features, taps, medium, skip, part * share, share)
        rows = slice(part * share * LANES, (part + 1) * share * LANES)
        piece = output_projection(gated, tuple(w[rows] for w in weights))
        total = piece if total is None else total + piece
    return total.astype(jnp.bfloat16)

def solution(mesh):
    return jax.shard_map(
        per_device,
        mesh=mesh,
        in_specs=(
            P("ctx", None),
            P("ctx", None, "tp"),
            P(None, "tp", None),
            P("tp", None),
            P("tp"),
            P("tp"),
            P("tp", None),
        ),
        out_specs=P("ctx", "tp"),
        check_vma=False,
    )
```

```python
import functools

import jax
import jax.numpy as jnp
from jax import lax
from jax.sharding import PartitionSpec as P


from jax.experimental import pallas as pl
from jax.experimental.pallas import tpu as pltpu

HALO = 136
CHUNK = 64
LANES = 128


def filter_kernel(term_count, *refs):
    fields = refs[: 3 * term_count]
    taps, medium, skip, out, raw, prod, shifted, smooth_q = refs[3 * term_count :]
    ext = fields[0].shape[0]
    local = ext - HALO
    taps_count = 7
    short_count = taps.shape[0] // 3
    for slot in range(3):
        group = fields[slot * term_count : (slot + 1) * term_count]
        total = group[0][...]
        for term in group[1:]:
            total = total + term[...]
        raw[slot] = total.astype(jnp.bfloat16).astype(jnp.float32)

    def smooth(slot, first):
        total = jnp.zeros((ext - first, LANES), jnp.float32)
        for lag in range(taps_count):
            weight = taps[pl.ds(slot * short_count + lag, 1), :]
            total = total + weight * raw[slot, pl.ds(first - lag, ext - first), :]
        return total

    smooth_q[...] = smooth(0, HALO)
    prod[8:ext, :] = smooth(1, 8) * smooth(2, 8)
    for shift in range(8):
        shifted[shift, 16:ext, :] = prod[pl.ds(16 - shift, ext - 16), :]

    def chunk_body(index, carry):
        row = pl.multiple_of(index * CHUNK, CHUNK)
        at = pl.multiple_of(row + HALO, 8)
        total = skip[...] * prod[pl.ds(at, CHUNK), :]
        for group in range(medium.shape[0] // 8):
            base = pl.multiple_of(at - 8 * group, 8)
            for shift in range(8):
                weight = medium[pl.ds(8 * group + shift, 1), :]
                total = total + weight * shifted[shift, pl.ds(base, CHUNK), :]
        out[pl.ds(row, CHUNK), :] = (smooth_q[pl.ds(row, CHUNK), :] * total).astype(out.dtype)
        return carry

    lax.fori_loop(0, local // CHUNK, chunk_body, 0)


def channel_filter(fields, taps, medium, skip, first, tiles):
    term_count = len(fields[0])
    ext = fields[0][0].shape[0]
    local = ext - HALO
    channels = tiles * LANES

    def field_spec(field):
        return pl.BlockSpec((ext, LANES), lambda t: (0, first + t))

    return pl.pallas_call(
        functools.partial(filter_kernel, term_count),
        grid=(tiles,),
        in_specs=[field_spec(0)] * (3 * term_count)
        + [
            pl.BlockSpec((taps.shape[0], LANES), lambda t: (0, first + t)),
            pl.BlockSpec((medium.shape[0], LANES), lambda t: (0, first + t)),
            pl.BlockSpec((1, LANES), lambda t: (0, first + t)),
        ],
        out_specs=pl.BlockSpec((local, LANES), lambda t: (0, t)),
        out_shape=jax.ShapeDtypeStruct((local, channels), jnp.bfloat16),
        scratch_shapes=[
            pltpu.VMEM((3, ext, LANES), jnp.float32),
            pltpu.VMEM((ext, LANES), jnp.float32),
            pltpu.VMEM((8, ext, LANES), jnp.float32),
            pltpu.VMEM((local, LANES), jnp.float32),
        ],
    )(*[term for field in fields for term in field], taps, medium, skip)

def ring_order(count):
    if count % 2:
        return list(range(count))
    return list(range(0, count, 2)) + list(range(count - 1, 0, -2))


def ring_projection(tokens, in_weight, riders):
    count = lax.axis_size("ctx")
    rows = in_weight.shape[0]
    order = ring_order(count)
    place = [0] * count
    for at, member in enumerate(order):
        place[member] = at
    forward = [(order[k], order[(k + 1) % count]) for k in range(count)]
    backward = [(order[k], order[(k - 1) % count]) for k in range(count)]
    me = lax.axis_index("ctx")
    order_table = jnp.array(order, jnp.int32)
    my_place = jnp.array(place, jnp.int32)[me]

    def product(cols, block):
        return tuple(
            jnp.dot(cols, block[:, field, :], preferred_element_type=jnp.float32)
            for field in range(block.shape[1])
        )

    def plus(left, right):
        return tuple(a + b for a, b in zip(left, right))

    def partial(block, source, start, width):
        cols = lax.dynamic_slice_in_dim(tokens, source * rows + start, width, 1)
        return product(cols, block)

    total = partial(in_weight, me, 0, rows)
    full_steps = (count - 1) // 2
    half = rows // 2

    def sources(step):
        return (
            order_table[(my_place - step) % count],
            order_table[(my_place + step) % count],
        )

    def add_pair(total, ahead, behind, step):
        from_behind, from_ahead = sources(step)
        total = plus(total, partial(ahead, from_behind, 0, rows))
        return plus(total, partial(behind, from_ahead, 0, rows))

    def ring_step(step, carry):
        ahead, behind, total = carry
        moved_ahead = lax.ppermute(ahead, "ctx", forward)
        moved_behind = lax.ppermute(behind, "ctx", backward)
        total = add_pair(total, ahead, behind, step - 1)
        return (moved_ahead, moved_behind, total)

    if full_steps == 0:
        return tuple((part,) for part in total), riders
    ahead = lax.ppermute(in_weight, "ctx", forward)
    behind = lax.ppermute(in_weight, "ctx", backward)
    carry = (ahead, behind, total)
    if full_steps >= 2:
        carry = ring_step(2, carry)
    carry, riders = lax.optimization_barrier((carry, riders))

    def carried_step(step, state):
        return (ring_step(step, state[0]), state[1])

    carry, riders = lax.fori_loop(3, full_steps + 1, carried_step, (carry, riders))
    ahead, behind, total = carry
    if count % 2 == 0:
        last_ahead = lax.ppermute(ahead[:half], "ctx", forward)
        last_behind = lax.ppermute(behind[half:], "ctx", backward)
        from_behind_full, from_ahead_full = sources(full_steps)
        first_terms = partial(ahead, from_behind_full, 0, rows)
        second_terms = partial(behind, from_ahead_full, 0, rows)
        from_behind, from_ahead = sources(full_steps + 1)
        cols = jnp.concatenate(
            [
                lax.dynamic_slice_in_dim(tokens, from_behind * rows, half, 1),
                lax.dynamic_slice_in_dim(tokens, from_ahead * rows + half, rows - half, 1),
            ],
            axis=1,
        )
        block = jnp.concatenate([last_ahead, last_behind], axis=0)
        last_terms = product(cols, block)
        terms = tuple(zip(total, first_terms, second_terms, last_terms))
    else:
        from_behind_full, from_ahead_full = sources(full_steps)
        first_terms = partial(ahead, from_behind_full, 0, rows)
        second_terms = partial(behind, from_ahead_full, 0, rows)
        terms = tuple(zip(total, first_terms, second_terms))
    return terms, riders


def tp_bits(count):
    bits = []
    bit = 1
    while bit < count:
        bits.append(bit)
        bit *= 2
    return bits


def spread_weights(out_weight):
    count = lax.axis_size("tp")
    me = lax.axis_index("tp")
    width = out_weight.shape[1] // count
    weights = [lax.dynamic_slice_in_dim(out_weight, me * width, width, 1)]
    for partner in range(1, count):
        pairs = [(k, k ^ partner) for k in range(count)]
        sent = lax.dynamic_slice_in_dim(out_weight, (me ^ partner) * width, width, 1)
        weights.append(lax.ppermute(sent, "tp", pairs))
    return tuple(weights)


def output_projection(gated, weights):
    count = lax.axis_size("tp")
    pieces = {0: gated}
    for bit in reversed(tp_bits(count)):
        pairs = [(k, k ^ bit) for k in range(count)]
        moved = {key ^ bit: lax.ppermute(piece, "tp", pairs) for key, piece in pieces.items()}
        pieces.update(moved)
    total = None
    for key in sorted(pieces):
        part = jnp.dot(pieces[key], weights[key], preferred_element_type=jnp.float32)
        total = part if total is None else total + part
    return total

def halo_rows(tail):
    ctx_count = lax.axis_size("ctx")
    tp_count = lax.axis_size("tp")
    shift = [(k, k + 1) for k in range(ctx_count - 1)]
    if tp_count % 2:
        return lax.ppermute(tail, "ctx", shift)
    width = tail.shape[1] // 2
    side = lax.axis_index("tp") % 2
    mine = lax.ppermute(lax.dynamic_slice_in_dim(tail, side * width, width, 1), "ctx", shift)
    other = lax.ppermute(mine, "tp", [(k, k ^ 1) for k in range(tp_count)])
    return jnp.where(
        side == 0,
        jnp.concatenate([mine, other], axis=1),
        jnp.concatenate([other, mine], axis=1),
    )


def per_device(tokens, in_weight, short_taps, medium_taps, medium_decay, skip_gain, out_weight):
    row_count = tokens.shape[0]
    channel_count = in_weight.shape[2]
    ctx_count = lax.axis_size("ctx")
    medium_count = medium_taps.shape[1]
    short_count = short_taps.shape[2]
    earlier = halo_rows(tokens[row_count - HALO :])
    earlier, in_weight = lax.optimization_barrier((earlier, in_weight))
    widened = jnp.concatenate([earlier, tokens], axis=0)
    features, weights = ring_projection(widened, in_weight, spread_weights(out_weight))
    lag_values = lax.broadcasted_iota(jnp.float32, (1, medium_count), 1)
    filters = medium_taps * jnp.exp(-medium_decay[:, None] * lag_values)
    taps = jnp.pad(
        jnp.transpose(short_taps, (0, 2, 1)), ((0, 0), (0, 8 - short_count), (0, 0))
    ).reshape(3 * 8, channel_count)
    tiles = channel_count // LANES
    parts = 2 if tiles % 2 == 0 else 1
    share = tiles // parts
    medium = jnp.transpose(filters)
    skip = skip_gain.reshape(1, channel_count)
    total = None
    for part in range(parts):
        gated = channel_filter(features, taps, medium, skip, part * share, share)
        rows = slice(part * share * LANES, (part + 1) * share * LANES)
        piece = output_projection(gated, tuple(w[rows] for w in weights))
        total = piece if total is None else total + piece
    return total.astype(jnp.bfloat16)

def solution(mesh):
    return jax.shard_map(
        per_device,
        mesh=mesh,
        in_specs=(
            P("ctx", None),
            P("ctx", None, "tp"),
            P(None, "tp", None),
            P("tp", None),
            P("tp"),
            P("tp"),
            P("tp", None),
        ),
        out_specs=P("ctx", "tp"),
        check_vma=False,
    )
```

```python
import functools

import jax
import jax.numpy as jnp
from jax import lax
from jax.sharding import PartitionSpec as P


from jax.experimental import pallas as pl
from jax.experimental.pallas import tpu as pltpu

HALO = 136
CHUNK = 64
LANES = 128


def filter_kernel(term_count, *refs):
    fields = refs[: 3 * term_count]
    taps, medium, skip, out, raw, prod, shifted, smooth_q = refs[3 * term_count :]
    ext = fields[0].shape[0]
    local = ext - HALO
    taps_count = 7
    short_count = taps.shape[0] // 3
    for slot in range(3):
        group = fields[slot * term_count : (slot + 1) * term_count]
        total = group[0][...]
        for term in group[1:]:
            total = total + term[...]
        raw[slot] = total.astype(jnp.bfloat16).astype(jnp.float32)

    def smooth(slot, first):
        total = jnp.zeros((ext - first, LANES), jnp.float32)
        for lag in range(taps_count):
            weight = taps[pl.ds(slot * short_count + lag, 1), :]
            total = total + weight * raw[slot, pl.ds(first - lag, ext - first), :]
        return total

    smooth_q[...] = smooth(0, HALO)
    prod[8:ext, :] = smooth(1, 8) * smooth(2, 8)
    for shift in range(8):
        shifted[shift, 16:ext, :] = prod[pl.ds(16 - shift, ext - 16), :]

    def chunk_body(index, carry):
        row = pl.multiple_of(index * CHUNK, CHUNK)
        at = pl.multiple_of(row + HALO, 8)
        total = skip[...] * prod[pl.ds(at, CHUNK), :]
        groups = medium.shape[0] // 8
        reach = 8 * (groups - 1)
        start = pl.multiple_of(at - reach, 8)
        for shift in range(8):
            window = shifted[shift, pl.ds(start, CHUNK + reach), :]
            for group in range(groups):
                offset = reach - 8 * group
                weight = medium[pl.ds(8 * group + shift, 1), :]
                total = total + weight * window[offset : offset + CHUNK]
        out[pl.ds(row, CHUNK), :] = (smooth_q[pl.ds(row, CHUNK), :] * total).astype(out.dtype)
        return carry

    lax.fori_loop(0, local // CHUNK, chunk_body, 0)


def channel_filter(fields, taps, medium, skip, first, tiles):
    term_count = len(fields[0])
    ext = fields[0][0].shape[0]
    local = ext - HALO
    channels = tiles * LANES

    def field_spec(field):
        return pl.BlockSpec((ext, LANES), lambda t: (0, first + t))

    return pl.pallas_call(
        functools.partial(filter_kernel, term_count),
        grid=(tiles,),
        in_specs=[field_spec(0)] * (3 * term_count)
        + [
            pl.BlockSpec((taps.shape[0], LANES), lambda t: (0, first + t)),
            pl.BlockSpec((medium.shape[0], LANES), lambda t: (0, first + t)),
            pl.BlockSpec((1, LANES), lambda t: (0, first + t)),
        ],
        out_specs=pl.BlockSpec((local, LANES), lambda t: (0, t)),
        out_shape=jax.ShapeDtypeStruct((local, channels), jnp.bfloat16),
        scratch_shapes=[
            pltpu.VMEM((3, ext, LANES), jnp.float32),
            pltpu.VMEM((ext, LANES), jnp.float32),
            pltpu.VMEM((8, ext, LANES), jnp.float32),
            pltpu.VMEM((local, LANES), jnp.float32),
        ],
    )(*[term for field in fields for term in field], taps, medium, skip)

def ring_order(count):
    if count % 2:
        return list(range(count))
    return list(range(0, count, 2)) + list(range(count - 1, 0, -2))


def ring_projection(tokens, in_weight, riders):
    count = lax.axis_size("ctx")
    rows = in_weight.shape[0]
    order = ring_order(count)
    place = [0] * count
    for at, member in enumerate(order):
        place[member] = at
    forward = [(order[k], order[(k + 1) % count]) for k in range(count)]
    backward = [(order[k], order[(k - 1) % count]) for k in range(count)]
    me = lax.axis_index("ctx")
    order_table = jnp.array(order, jnp.int32)
    my_place = jnp.array(place, jnp.int32)[me]

    def product(cols, block):
        return tuple(
            jnp.dot(cols, block[:, field, :], preferred_element_type=jnp.float32)
            for field in range(block.shape[1])
        )

    def plus(left, right):
        return tuple(a + b for a, b in zip(left, right))

    def partial(block, source, start, width):
        cols = lax.dynamic_slice_in_dim(tokens, source * rows + start, width, 1)
        return product(cols, block)

    total = partial(in_weight, me, 0, rows)
    full_steps = (count - 1) // 2
    half = rows // 2

    def sources(step):
        return (
            order_table[(my_place - step) % count],
            order_table[(my_place + step) % count],
        )

    def add_pair(total, ahead, behind, step):
        from_behind, from_ahead = sources(step)
        total = plus(total, partial(ahead, from_behind, 0, rows))
        return plus(total, partial(behind, from_ahead, 0, rows))

    def ring_step(step, carry):
        ahead, behind, total = carry
        moved_ahead = lax.ppermute(ahead, "ctx", forward)
        moved_behind = lax.ppermute(behind, "ctx", backward)
        total = add_pair(total, ahead, behind, step - 1)
        return (moved_ahead, moved_behind, total)

    if full_steps == 0:
        return tuple((part,) for part in total), riders
    ahead = lax.ppermute(in_weight, "ctx", forward)
    behind = lax.ppermute(in_weight, "ctx", backward)
    carry = (ahead, behind, total)
    if full_steps >= 2:
        carry = ring_step(2, carry)
    carry, riders = lax.optimization_barrier((carry, riders))

    def carried_step(step, state):
        return (ring_step(step, state[0]), state[1])

    carry, riders = lax.fori_loop(3, full_steps + 1, carried_step, (carry, riders))
    ahead, behind, total = carry
    if count % 2 == 0:
        last_ahead = lax.ppermute(ahead[:half], "ctx", forward)
        last_behind = lax.ppermute(behind[half:], "ctx", backward)
        from_behind_full, from_ahead_full = sources(full_steps)
        first_terms = partial(ahead, from_behind_full, 0, rows)
        second_terms = partial(behind, from_ahead_full, 0, rows)
        from_behind, from_ahead = sources(full_steps + 1)
        cols = jnp.concatenate(
            [
                lax.dynamic_slice_in_dim(tokens, from_behind * rows, half, 1),
                lax.dynamic_slice_in_dim(tokens, from_ahead * rows + half, rows - half, 1),
            ],
            axis=1,
        )
        block = jnp.concatenate([last_ahead, last_behind], axis=0)
        last_terms = product(cols, block)
        terms = tuple(zip(total, first_terms, second_terms, last_terms))
    else:
        from_behind_full, from_ahead_full = sources(full_steps)
        first_terms = partial(ahead, from_behind_full, 0, rows)
        second_terms = partial(behind, from_ahead_full, 0, rows)
        terms = tuple(zip(total, first_terms, second_terms))
    return terms, riders


def tp_bits(count):
    bits = []
    bit = 1
    while bit < count:
        bits.append(bit)
        bit *= 2
    return bits


def spread_weights(out_weight):
    count = lax.axis_size("tp")
    me = lax.axis_index("tp")
    width = out_weight.shape[1] // count
    weights = [lax.dynamic_slice_in_dim(out_weight, me * width, width, 1)]
    for partner in range(1, count):
        pairs = [(k, k ^ partner) for k in range(count)]
        sent = lax.dynamic_slice_in_dim(out_weight, (me ^ partner) * width, width, 1)
        weights.append(lax.ppermute(sent, "tp", pairs))
    return tuple(weights)


def output_projection(gated, weights):
    count = lax.axis_size("tp")
    pieces = {0: gated}
    for bit in reversed(tp_bits(count)):
        pairs = [(k, k ^ bit) for k in range(count)]
        moved = {key ^ bit: lax.ppermute(piece, "tp", pairs) for key, piece in pieces.items()}
        pieces.update(moved)
    total = None
    for key in sorted(pieces):
        part = jnp.dot(pieces[key], weights[key], preferred_element_type=jnp.float32)
        total = part if total is None else total + part
    return total

def halo_rows(tail):
    ctx_count = lax.axis_size("ctx")
    tp_count = lax.axis_size("tp")
    shift = [(k, k + 1) for k in range(ctx_count - 1)]
    if tp_count % 2:
        return lax.ppermute(tail, "ctx", shift)
    width = tail.shape[1] // 2
    side = lax.axis_index("tp") % 2
    mine = lax.ppermute(lax.dynamic_slice_in_dim(tail, side * width, width, 1), "ctx", shift)
    other = lax.ppermute(mine, "tp", [(k, k ^ 1) for k in range(tp_count)])
    return jnp.where(
        side == 0,
        jnp.concatenate([mine, other], axis=1),
        jnp.concatenate([other, mine], axis=1),
    )


def per_device(tokens, in_weight, short_taps, medium_taps, medium_decay, skip_gain, out_weight):
    row_count = tokens.shape[0]
    channel_count = in_weight.shape[2]
    ctx_count = lax.axis_size("ctx")
    medium_count = medium_taps.shape[1]
    short_count = short_taps.shape[2]
    earlier = halo_rows(tokens[row_count - HALO :])
    earlier, in_weight = lax.optimization_barrier((earlier, in_weight))
    widened = jnp.concatenate([earlier, tokens], axis=0)
    features, weights = ring_projection(widened, in_weight, spread_weights(out_weight))
    lag_values = lax.broadcasted_iota(jnp.float32, (1, medium_count), 1)
    filters = medium_taps * jnp.exp(-medium_decay[:, None] * lag_values)
    taps = jnp.pad(
        jnp.transpose(short_taps, (0, 2, 1)), ((0, 0), (0, 8 - short_count), (0, 0))
    ).reshape(3 * 8, channel_count)
    tiles = channel_count // LANES
    parts = 2 if tiles % 2 == 0 else 1
    share = tiles // parts
    medium = jnp.transpose(filters)
    skip = skip_gain.reshape(1, channel_count)
    total = None
    for part in range(parts):
        gated = channel_filter(features, taps, medium, skip, part * share, share)
        rows = slice(part * share * LANES, (part + 1) * share * LANES)
        piece = output_projection(gated, tuple(w[rows] for w in weights))
        total = piece if total is None else total + piece
    return total.astype(jnp.bfloat16)

def solution(mesh):
    return jax.shard_map(
        per_device,
        mesh=mesh,
        in_specs=(
            P("ctx", None),
            P("ctx", None, "tp"),
            P(None, "tp", None),
            P("tp", None),
            P("tp"),
            P("tp"),
            P("tp", None),
        ),
        out_specs=P("ctx", "tp"),
        check_vma=False,
    )
```

```python
import functools

import jax
import jax.numpy as jnp
from jax import lax
from jax.sharding import PartitionSpec as P


from jax.experimental import pallas as pl
from jax.experimental.pallas import tpu as pltpu

HALO = 136
CHUNK = 64
LANES = 128


def filter_kernel(term_count, *refs):
    fields = refs[: 3 * term_count]
    taps, medium, skip, out, raw, prod, shifted, smooth_q = refs[3 * term_count :]
    ext = fields[0].shape[0]
    local = ext - HALO
    taps_count = 7
    short_count = taps.shape[0] // 3
    for slot in range(3):
        group = fields[slot * term_count : (slot + 1) * term_count]
        total = group[0][...]
        for term in group[1:]:
            total = total + term[...]
        raw[slot] = total.astype(jnp.bfloat16).astype(jnp.float32)

    def smooth(slot, first):
        total = jnp.zeros((ext - first, LANES), jnp.float32)
        for lag in range(taps_count):
            weight = taps[pl.ds(slot * short_count + lag, 1), :]
            total = total + weight * raw[slot, pl.ds(first - lag, ext - first), :]
        return total

    smooth_q[...] = smooth(0, HALO)
    prod[8:ext, :] = smooth(1, 8) * smooth(2, 8)
    for shift in range(8):
        shifted[shift, 16:ext, :] = prod[pl.ds(16 - shift, ext - 16), :]

    def chunk_body(index, carry):
        row = pl.multiple_of(index * CHUNK, CHUNK)
        at = pl.multiple_of(row + HALO, 8)
        total = skip[...] * prod[pl.ds(at, CHUNK), :]
        groups = medium.shape[0] // 8
        reach = 8 * (groups - 1)
        start = pl.multiple_of(at - reach, 8)
        for shift in range(8):
            window = shifted[shift, pl.ds(start, CHUNK + reach), :]
            for group in range(groups):
                offset = reach - 8 * group
                weight = medium[pl.ds(8 * group + shift, 1), :]
                total = total + weight * window[offset : offset + CHUNK]
        out[pl.ds(row, CHUNK), :] = (smooth_q[pl.ds(row, CHUNK), :] * total).astype(out.dtype)
        return carry

    lax.fori_loop(0, local // CHUNK, chunk_body, 0)


def channel_filter(fields, taps, medium, skip, first, tiles):
    term_count = len(fields[0])
    ext = fields[0][0].shape[0]
    local = ext - HALO
    channels = tiles * LANES

    def field_spec(field):
        return pl.BlockSpec((ext, LANES), lambda t: (0, t))

    return pl.pallas_call(
        functools.partial(filter_kernel, term_count),
        grid=(tiles,),
        in_specs=[field_spec(0)] * (3 * term_count)
        + [
            pl.BlockSpec((taps.shape[0], LANES), lambda t: (0, first + t)),
            pl.BlockSpec((medium.shape[0], LANES), lambda t: (0, first + t)),
            pl.BlockSpec((1, LANES), lambda t: (0, first + t)),
        ],
        out_specs=pl.BlockSpec((local, LANES), lambda t: (0, t)),
        out_shape=jax.ShapeDtypeStruct((local, channels), jnp.bfloat16),
        scratch_shapes=[
            pltpu.VMEM((3, ext, LANES), jnp.float32),
            pltpu.VMEM((ext, LANES), jnp.float32),
            pltpu.VMEM((8, ext, LANES), jnp.float32),
            pltpu.VMEM((local, LANES), jnp.float32),
        ],
    )(*[term for field in fields for term in field], taps, medium, skip)

def ring_order(count):
    if count % 2:
        return list(range(count))
    return list(range(0, count, 2)) + list(range(count - 1, 0, -2))


def ring_projection(tokens, in_weight, riders, follower):
    count = lax.axis_size("ctx")
    rows = in_weight.shape[0]
    order = ring_order(count)
    place = [0] * count
    for at, member in enumerate(order):
        place[member] = at
    forward = [(order[k], order[(k + 1) % count]) for k in range(count)]
    backward = [(order[k], order[(k - 1) % count]) for k in range(count)]
    me = lax.axis_index("ctx")
    order_table = jnp.array(order, jnp.int32)
    my_place = jnp.array(place, jnp.int32)[me]

    def product(cols, block):
        return tuple(
            jnp.dot(cols, block[:, field, :], preferred_element_type=jnp.float32)
            for field in range(block.shape[1])
        )

    def plus(left, right):
        return tuple(a + b for a, b in zip(left, right))

    def partial(block, source, start, width):
        cols = lax.dynamic_slice_in_dim(tokens, source * rows + start, width, 1)
        return product(cols, block)

    total = partial(in_weight, me, 0, rows)
    full_steps = (count - 1) // 2
    half = rows // 2

    def sources(step):
        return (
            order_table[(my_place - step) % count],
            order_table[(my_place + step) % count],
        )

    def add_pair(total, ahead, behind, step):
        from_behind, from_ahead = sources(step)
        total = plus(total, partial(ahead, from_behind, 0, rows))
        return plus(total, partial(behind, from_ahead, 0, rows))

    def ring_step(step, carry):
        ahead, behind, total = carry
        moved_ahead = lax.ppermute(ahead, "ctx", forward)
        moved_behind = lax.ppermute(behind, "ctx", backward)
        total = add_pair(total, ahead, behind, step - 1)
        return (moved_ahead, moved_behind, total)

    if full_steps == 0:
        return tuple((part,) for part in total), riders, follower
    ahead = lax.ppermute(in_weight, "ctx", forward)
    behind = lax.ppermute(in_weight, "ctx", backward)
    carry = (ahead, behind, total)
    if full_steps >= 2:
        carry = ring_step(2, carry)
    carry, riders = lax.optimization_barrier((carry, riders))

    def carried_step(step, state):
        return (ring_step(step, state[0]), state[1])

    carry, riders = lax.fori_loop(3, full_steps + 1, carried_step, (carry, riders))
    ahead, behind, total = carry
    if count % 2 == 0:
        last_ahead = lax.ppermute(ahead[:half], "ctx", forward)
        last_behind = lax.ppermute(behind[half:], "ctx", backward)
        last_ahead, last_behind, follower = lax.optimization_barrier(
            (last_ahead, last_behind, follower)
        )
        from_behind_full, from_ahead_full = sources(full_steps)
        first_terms = partial(ahead, from_behind_full, 0, rows)
        second_terms = partial(behind, from_ahead_full, 0, rows)
        from_behind, from_ahead = sources(full_steps + 1)
        cols = jnp.concatenate(
            [
                lax.dynamic_slice_in_dim(tokens, from_behind * rows, half, 1),
                lax.dynamic_slice_in_dim(tokens, from_ahead * rows + half, rows - half, 1),
            ],
            axis=1,
        )
        block = jnp.concatenate([last_ahead, last_behind], axis=0)
        last_terms = product(cols, block)
        terms = tuple(zip(total, first_terms, second_terms, last_terms))
    else:
        from_behind_full, from_ahead_full = sources(full_steps)
        first_terms = partial(ahead, from_behind_full, 0, rows)
        second_terms = partial(behind, from_ahead_full, 0, rows)
        terms = tuple(zip(total, first_terms, second_terms))
    return terms, riders, follower


def tp_bits(count):
    bits = []
    bit = 1
    while bit < count:
        bits.append(bit)
        bit *= 2
    return bits


def spread_weights(out_weight):
    count = lax.axis_size("tp")
    me = lax.axis_index("tp")
    width = out_weight.shape[1] // count
    weights = [lax.dynamic_slice_in_dim(out_weight, me * width, width, 1)]
    for partner in range(1, count):
        pairs = [(k, k ^ partner) for k in range(count)]
        sent = lax.dynamic_slice_in_dim(out_weight, (me ^ partner) * width, width, 1)
        weights.append(lax.ppermute(sent, "tp", pairs))
    return tuple(weights)


def output_projection(gated, weights):
    count = lax.axis_size("tp")
    pieces = {0: gated}
    for bit in reversed(tp_bits(count)):
        pairs = [(k, k ^ bit) for k in range(count)]
        moved = {key ^ bit: lax.ppermute(piece, "tp", pairs) for key, piece in pieces.items()}
        pieces.update(moved)
    total = None
    for key in sorted(pieces):
        part = jnp.dot(pieces[key], weights[key], preferred_element_type=jnp.float32)
        total = part if total is None else total + part
    return total

def halo_rows(tail):
    ctx_count = lax.axis_size("ctx")
    tp_count = lax.axis_size("tp")
    shift = [(k, k + 1) for k in range(ctx_count - 1)]
    if tp_count % 2:
        return lax.ppermute(tail, "ctx", shift)
    width = tail.shape[1] // 2
    side = lax.axis_index("tp") % 2
    mine = lax.ppermute(lax.dynamic_slice_in_dim(tail, side * width, width, 1), "ctx", shift)
    other = lax.ppermute(mine, "tp", [(k, k ^ 1) for k in range(tp_count)])
    return jnp.where(
        side == 0,
        jnp.concatenate([mine, other], axis=1),
        jnp.concatenate([other, mine], axis=1),
    )


def per_device(tokens, in_weight, short_taps, medium_taps, medium_decay, skip_gain, out_weight):
    row_count = tokens.shape[0]
    channel_count = in_weight.shape[2]
    ctx_count = lax.axis_size("ctx")
    medium_count = medium_taps.shape[1]
    short_count = short_taps.shape[2]
    earlier = halo_rows(tokens[row_count - HALO :])
    earlier, in_weight = lax.optimization_barrier((earlier, in_weight))
    widened = jnp.concatenate([earlier, tokens], axis=0)
    lag_values = lax.broadcasted_iota(jnp.float32, (1, medium_count), 1)
    filters = medium_taps * jnp.exp(-medium_decay[:, None] * lag_values)
    taps = jnp.pad(
        jnp.transpose(short_taps, (0, 2, 1)), ((0, 0), (0, 8 - short_count), (0, 0))
    ).reshape(3 * 8, channel_count)
    tiles = channel_count // LANES
    parts = 2 if tiles % 2 == 0 else 1
    share = tiles // parts
    width = share * LANES
    medium = jnp.transpose(filters)
    skip = skip_gain.reshape(1, channel_count)
    weights = spread_weights(out_weight)
    later = in_weight[:, :, width:]
    total = None
    for part in range(parts):
        block = in_weight[:, :, :width] if part == 0 else later
        features, weights, later = ring_projection(widened, block, weights, later)
        gated = channel_filter(features, taps, medium, skip, part * share, share)
        rows = slice(part * width, (part + 1) * width)
        piece = output_projection(gated, tuple(w[rows] for w in weights))
        total = piece if total is None else total + piece
    return total.astype(jnp.bfloat16)

def solution(mesh):
    return jax.shard_map(
        per_device,
        mesh=mesh,
        in_specs=(
            P("ctx", None),
            P("ctx", None, "tp"),
            P(None, "tp", None),
            P("tp", None),
            P("tp"),
            P("tp"),
            P("tp", None),
        ),
        out_specs=P("ctx", "tp"),
        check_vma=False,
    )
```

```python
import functools

import jax
import jax.numpy as jnp
from jax import lax
from jax.sharding import PartitionSpec as P


from jax.experimental import pallas as pl
from jax.experimental.pallas import tpu as pltpu

HALO = 136
CHUNK = 64
LANES = 128


def filter_kernel(term_count, *refs):
    fields = refs[: 3 * term_count]
    taps, medium, skip, out, raw, prod, shifted, smooth_q = refs[3 * term_count :]
    ext = fields[0].shape[0]
    local = ext - HALO
    taps_count = 7
    short_count = taps.shape[0] // 3
    for slot in range(3):
        group = fields[slot * term_count : (slot + 1) * term_count]
        total = group[0][...]
        for term in group[1:]:
            total = total + term[...]
        raw[slot] = total.astype(jnp.bfloat16).astype(jnp.float32)

    def smooth(slot, first):
        total = jnp.zeros((ext - first, LANES), jnp.float32)
        for lag in range(taps_count):
            weight = taps[pl.ds(slot * short_count + lag, 1), :]
            total = total + weight * raw[slot, pl.ds(first - lag, ext - first), :]
        return total

    smooth_q[...] = smooth(0, HALO)
    prod[8:ext, :] = smooth(1, 8) * smooth(2, 8)
    for shift in range(8):
        shifted[shift, 16:ext, :] = prod[pl.ds(16 - shift, ext - 16), :]

    def chunk_body(index, carry):
        row = pl.multiple_of(index * CHUNK, CHUNK)
        at = pl.multiple_of(row + HALO, 8)
        total = skip[...] * prod[pl.ds(at, CHUNK), :]
        groups = medium.shape[0] // 8
        reach = 8 * (groups - 1)
        start = pl.multiple_of(at - reach, 8)
        for shift in range(8):
            window = shifted[shift, pl.ds(start, CHUNK + reach), :]
            for group in range(groups):
                offset = reach - 8 * group
                weight = medium[pl.ds(8 * group + shift, 1), :]
                total = total + weight * window[offset : offset + CHUNK]
        out[pl.ds(row, CHUNK), :] = (smooth_q[pl.ds(row, CHUNK), :] * total).astype(out.dtype)
        return carry

    lax.fori_loop(0, local // CHUNK, chunk_body, 0)


def channel_filter(fields, taps, medium, skip, first, tiles):
    term_count = len(fields[0])
    ext = fields[0][0].shape[0]
    local = ext - HALO
    channels = tiles * LANES

    def field_spec(field):
        return pl.BlockSpec((ext, LANES), lambda t: (0, first + t))

    return pl.pallas_call(
        functools.partial(filter_kernel, term_count),
        grid=(tiles,),
        in_specs=[field_spec(0)] * (3 * term_count)
        + [
            pl.BlockSpec((taps.shape[0], LANES), lambda t: (0, first + t)),
            pl.BlockSpec((medium.shape[0], LANES), lambda t: (0, first + t)),
            pl.BlockSpec((1, LANES), lambda t: (0, first + t)),
        ],
        out_specs=pl.BlockSpec((local, LANES), lambda t: (0, t)),
        out_shape=jax.ShapeDtypeStruct((local, channels), jnp.bfloat16),
        scratch_shapes=[
            pltpu.VMEM((3, ext, LANES), jnp.float32),
            pltpu.VMEM((ext, LANES), jnp.float32),
            pltpu.VMEM((8, ext, LANES), jnp.float32),
            pltpu.VMEM((local, LANES), jnp.float32),
        ],
    )(*[term for field in fields for term in field], taps, medium, skip)

def ring_order(count):
    if count % 2:
        return list(range(count))
    return list(range(0, count, 2)) + list(range(count - 1, 0, -2))


def ring_projection(tokens, in_weight, riders):
    count = lax.axis_size("ctx")
    rows = in_weight.shape[0]
    order = ring_order(count)
    place = [0] * count
    for at, member in enumerate(order):
        place[member] = at
    forward = [(order[k], order[(k + 1) % count]) for k in range(count)]
    backward = [(order[k], order[(k - 1) % count]) for k in range(count)]
    me = lax.axis_index("ctx")
    order_table = jnp.array(order, jnp.int32)
    my_place = jnp.array(place, jnp.int32)[me]

    def product(cols, block):
        return tuple(
            jnp.dot(cols, block[:, field, :], preferred_element_type=jnp.float32)
            for field in range(block.shape[1])
        )

    def plus(left, right):
        return tuple(a + b for a, b in zip(left, right))

    def partial(block, source, start, width):
        cols = lax.dynamic_slice_in_dim(tokens, source * rows + start, width, 1)
        return product(cols, block)

    total = partial(in_weight, me, 0, rows)
    full_steps = (count - 1) // 2
    half = rows // 2

    def sources(step):
        return (
            order_table[(my_place - step) % count],
            order_table[(my_place + step) % count],
        )

    def add_pair(total, ahead, behind, step):
        from_behind, from_ahead = sources(step)
        total = plus(total, partial(ahead, from_behind, 0, rows))
        return plus(total, partial(behind, from_ahead, 0, rows))

    def ring_step(step, carry):
        ahead, behind, total = carry
        moved_ahead = lax.ppermute(ahead, "ctx", forward)
        moved_behind = lax.ppermute(behind, "ctx", backward)
        total = add_pair(total, ahead, behind, step - 1)
        return (moved_ahead, moved_behind, total)

    if full_steps == 0:
        return tuple((part,) for part in total), riders
    ahead = lax.ppermute(in_weight, "ctx", forward)
    behind = lax.ppermute(in_weight, "ctx", backward)
    carry = (ahead, behind, total)
    if full_steps >= 2:
        carry = ring_step(2, carry)
    carry, riders = lax.optimization_barrier((carry, riders))

    def carried_step(step, state):
        return (ring_step(step, state[0]), state[1])

    carry, riders = lax.fori_loop(3, full_steps + 1, carried_step, (carry, riders))
    ahead, behind, total = carry
    if count % 2 == 0:
        last_ahead = lax.ppermute(ahead[:half], "ctx", forward)
        last_behind = lax.ppermute(behind[half:], "ctx", backward)
        from_behind_full, from_ahead_full = sources(full_steps)
        first_terms = partial(ahead, from_behind_full, 0, rows)
        second_terms = partial(behind, from_ahead_full, 0, rows)
        from_behind, from_ahead = sources(full_steps + 1)
        cols = jnp.concatenate(
            [
                lax.dynamic_slice_in_dim(tokens, from_behind * rows, half, 1),
                lax.dynamic_slice_in_dim(tokens, from_ahead * rows + half, rows - half, 1),
            ],
            axis=1,
        )
        block = jnp.concatenate([last_ahead, last_behind], axis=0)
        last_terms = product(cols, block)
        terms = tuple(zip(total, first_terms, second_terms, last_terms))
    else:
        from_behind_full, from_ahead_full = sources(full_steps)
        first_terms = partial(ahead, from_behind_full, 0, rows)
        second_terms = partial(behind, from_ahead_full, 0, rows)
        terms = tuple(zip(total, first_terms, second_terms))
    return terms, riders


def tp_bits(count):
    bits = []
    bit = 1
    while bit < count:
        bits.append(bit)
        bit *= 2
    return bits


def spread_weights(out_weight):
    count = lax.axis_size("tp")
    me = lax.axis_index("tp")
    width = out_weight.shape[1] // count
    weights = [lax.dynamic_slice_in_dim(out_weight, me * width, width, 1)]
    for partner in range(1, count):
        pairs = [(k, k ^ partner) for k in range(count)]
        sent = lax.dynamic_slice_in_dim(out_weight, (me ^ partner) * width, width, 1)
        weights.append(lax.ppermute(sent, "tp", pairs))
    return tuple(weights)


def output_projection(gated, weights):
    count = lax.axis_size("tp")
    pieces = {0: gated}
    for bit in reversed(tp_bits(count)):
        pairs = [(k, k ^ bit) for k in range(count)]
        moved = {key ^ bit: lax.ppermute(piece, "tp", pairs) for key, piece in pieces.items()}
        pieces.update(moved)
    total = None
    for key in sorted(pieces):
        part = jnp.dot(pieces[key], weights[key], preferred_element_type=jnp.float32)
        total = part if total is None else total + part
    return total

def halo_rows(tail):
    ctx_count = lax.axis_size("ctx")
    tp_count = lax.axis_size("tp")
    shift = [(k, k + 1) for k in range(ctx_count - 1)]
    if tp_count % 2:
        return lax.ppermute(tail, "ctx", shift)
    width = tail.shape[1] // 2
    side = lax.axis_index("tp") % 2
    mine = lax.ppermute(lax.dynamic_slice_in_dim(tail, side * width, width, 1), "ctx", shift)
    other = lax.ppermute(mine, "tp", [(k, k ^ 1) for k in range(tp_count)])
    return jnp.where(
        side == 0,
        jnp.concatenate([mine, other], axis=1),
        jnp.concatenate([other, mine], axis=1),
    )


def per_device(tokens, in_weight, short_taps, medium_taps, medium_decay, skip_gain, out_weight):
    row_count = tokens.shape[0]
    channel_count = in_weight.shape[2]
    ctx_count = lax.axis_size("ctx")
    medium_count = medium_taps.shape[1]
    short_count = short_taps.shape[2]
    earlier = halo_rows(tokens[row_count - HALO :])
    widened = jnp.concatenate([earlier, tokens], axis=0)
    features, weights = ring_projection(widened, in_weight, spread_weights(out_weight))
    lag_values = lax.broadcasted_iota(jnp.float32, (1, medium_count), 1)
    filters = medium_taps * jnp.exp(-medium_decay[:, None] * lag_values)
    taps = jnp.pad(
        jnp.transpose(short_taps, (0, 2, 1)), ((0, 0), (0, 8 - short_count), (0, 0))
    ).reshape(3 * 8, channel_count)
    tiles = channel_count // LANES
    parts = 2 if tiles % 2 == 0 else 1
    share = tiles // parts
    medium = jnp.transpose(filters)
    skip = skip_gain.reshape(1, channel_count)
    total = None
    for part in range(parts):
        gated = channel_filter(features, taps, medium, skip, part * share, share)
        rows = slice(part * share * LANES, (part + 1) * share * LANES)
        piece = output_projection(gated, tuple(w[rows] for w in weights))
        total = piece if total is None else total + piece
    return total.astype(jnp.bfloat16)

def solution(mesh):
    return jax.shard_map(
        per_device,
        mesh=mesh,
        in_specs=(
            P("ctx", None),
            P("ctx", None, "tp"),
            P(None, "tp", None),
            P("tp", None),
            P("tp"),
            P("tp"),
            P("tp", None),
        ),
        out_specs=P("ctx", "tp"),
        check_vma=False,
    )
```

```python
import functools

import jax
import jax.numpy as jnp
from jax import lax
from jax.sharding import PartitionSpec as P


from jax.experimental import pallas as pl
from jax.experimental.pallas import tpu as pltpu

HALO = 136
CHUNK = 64
LANES = 128


def filter_kernel(term_count, *refs):
    fields = refs[: 3 * term_count]
    taps, medium, skip, out, raw, prod, shifted, smooth_q = refs[3 * term_count :]
    ext = fields[0].shape[0]
    local = ext - HALO
    taps_count = 7
    short_count = taps.shape[0] // 3
    for slot in range(3):
        group = fields[slot * term_count : (slot + 1) * term_count]
        total = group[0][0:8, :]
        for term in group[1:]:
            total = total + term[0:8, :]
        raw[slot, 0:8, :] = total.astype(jnp.bfloat16).astype(jnp.float32)

    def gather_body(index, carry):
        row = pl.multiple_of(8 + index * CHUNK, 8)
        for slot in range(3):
            group = fields[slot * term_count : (slot + 1) * term_count]
            total = group[0][pl.ds(row, CHUNK), :]
            for term in group[1:]:
                total = total + term[pl.ds(row, CHUNK), :]
            raw[slot, pl.ds(row, CHUNK), :] = total.astype(jnp.bfloat16).astype(jnp.float32)
        return carry

    lax.fori_loop(0, (ext - 8) // CHUNK, gather_body, 0)

    def smooth(slot, row):
        window = raw[slot, pl.ds(row - 8, CHUNK + 8), :]
        total = jnp.zeros((CHUNK, LANES), jnp.float32)
        for lag in range(taps_count):
            weight = taps[pl.ds(slot * short_count + lag, 1), :]
            total = total + weight * window[8 - lag : 8 - lag + CHUNK]
        return total

    def product_body(index, carry):
        row = pl.multiple_of(8 + index * CHUNK, 8)
        prod[pl.ds(row, CHUNK), :] = smooth(1, row) * smooth(2, row)
        return carry

    lax.fori_loop(0, (ext - 8) // CHUNK, product_body, 0)

    def query_body(index, carry):
        row = pl.multiple_of(index * CHUNK, 8)
        smooth_q[pl.ds(row, CHUNK), :] = smooth(0, row + HALO)
        return carry

    lax.fori_loop(0, local // CHUNK, query_body, 0)

    def shift_body(index, carry):
        row = pl.multiple_of(16 + index * CHUNK, 8)
        window = prod[pl.ds(row - 8, CHUNK + 8), :]
        for shift in range(8):
            shifted[shift, pl.ds(row, CHUNK), :] = window[8 - shift : 8 - shift + CHUNK]
        return carry

    lax.fori_loop(0, (ext - 16) // CHUNK, shift_body, 0)
    tail = 16 + ((ext - 16) // CHUNK) * CHUNK
    if tail < ext:
        window = prod[tail - 8 : ext, :]
        for shift in range(8):
            shifted[shift, tail:ext, :] = window[8 - shift : 8 - shift + ext - tail]

    def chunk_body(index, carry):
        row = pl.multiple_of(index * CHUNK, CHUNK)
        at = pl.multiple_of(row + HALO, 8)
        total = skip[...] * prod[pl.ds(at, CHUNK), :]
        groups = medium.shape[0] // 8
        reach = 8 * (groups - 1)
        start = pl.multiple_of(at - reach, 8)
        for shift in range(8):
            window = shifted[shift, pl.ds(start, CHUNK + reach), :]
            for group in range(groups):
                offset = reach - 8 * group
                weight = medium[pl.ds(8 * group + shift, 1), :]
                total = total + weight * window[offset : offset + CHUNK]
        out[pl.ds(row, CHUNK), :] = (smooth_q[pl.ds(row, CHUNK), :] * total).astype(out.dtype)
        return carry

    lax.fori_loop(0, local // CHUNK, chunk_body, 0)


def channel_filter(fields, taps, medium, skip, first, tiles):
    term_count = len(fields[0])
    ext = fields[0][0].shape[0]
    local = ext - HALO
    channels = tiles * LANES

    def field_spec(field):
        return pl.BlockSpec((ext, LANES), lambda t: (0, first + t))

    return pl.pallas_call(
        functools.partial(filter_kernel, term_count),
        grid=(tiles,),
        in_specs=[field_spec(0)] * (3 * term_count)
        + [
            pl.BlockSpec((taps.shape[0], LANES), lambda t: (0, first + t)),
            pl.BlockSpec((medium.shape[0], LANES), lambda t: (0, first + t)),
            pl.BlockSpec((1, LANES), lambda t: (0, first + t)),
        ],
        out_specs=pl.BlockSpec((local, LANES), lambda t: (0, t)),
        out_shape=jax.ShapeDtypeStruct((local, channels), jnp.bfloat16),
        scratch_shapes=[
            pltpu.VMEM((3, ext, LANES), jnp.float32),
            pltpu.VMEM((ext, LANES), jnp.float32),
            pltpu.VMEM((8, ext, LANES), jnp.float32),
            pltpu.VMEM((local, LANES), jnp.float32),
        ],
    )(*[term for field in fields for term in field], taps, medium, skip)

def ring_order(count):
    if count % 2:
        return list(range(count))
    return list(range(0, count, 2)) + list(range(count - 1, 0, -2))


def ring_projection(tokens, in_weight, riders):
    count = lax.axis_size("ctx")
    rows = in_weight.shape[0]
    order = ring_order(count)
    place = [0] * count
    for at, member in enumerate(order):
        place[member] = at
    forward = [(order[k], order[(k + 1) % count]) for k in range(count)]
    backward = [(order[k], order[(k - 1) % count]) for k in range(count)]
    me = lax.axis_index("ctx")
    order_table = jnp.array(order, jnp.int32)
    my_place = jnp.array(place, jnp.int32)[me]

    def product(cols, block):
        return tuple(
            jnp.dot(cols, block[:, field, :], preferred_element_type=jnp.float32)
            for field in range(block.shape[1])
        )

    def plus(left, right):
        return tuple(a + b for a, b in zip(left, right))

    def partial(block, source, start, width):
        cols = lax.dynamic_slice_in_dim(tokens, source * rows + start, width, 1)
        return product(cols, block)

    total = partial(in_weight, me, 0, rows)
    full_steps = (count - 1) // 2
    half = rows // 2

    def sources(step):
        return (
            order_table[(my_place - step) % count],
            order_table[(my_place + step) % count],
        )

    def add_pair(total, ahead, behind, step):
        from_behind, from_ahead = sources(step)
        total = plus(total, partial(ahead, from_behind, 0, rows))
        return plus(total, partial(behind, from_ahead, 0, rows))

    def ring_step(step, carry):
        ahead, behind, total = carry
        moved_ahead = lax.ppermute(ahead, "ctx", forward)
        moved_behind = lax.ppermute(behind, "ctx", backward)
        total = add_pair(total, ahead, behind, step - 1)
        return (moved_ahead, moved_behind, total)

    if full_steps == 0:
        return tuple((part,) for part in total), riders
    ahead = lax.ppermute(in_weight, "ctx", forward)
    behind = lax.ppermute(in_weight, "ctx", backward)
    carry = (ahead, behind, total)
    if full_steps >= 2:
        carry = ring_step(2, carry)
    carry, riders = lax.optimization_barrier((carry, riders))

    def carried_step(step, state):
        return (ring_step(step, state[0]), state[1])

    carry, riders = lax.fori_loop(3, full_steps + 1, carried_step, (carry, riders))
    ahead, behind, total = carry
    if count % 2 == 0:
        last_ahead = lax.ppermute(ahead[:half], "ctx", forward)
        last_behind = lax.ppermute(behind[half:], "ctx", backward)
        from_behind_full, from_ahead_full = sources(full_steps)
        first_terms = partial(ahead, from_behind_full, 0, rows)
        second_terms = partial(behind, from_ahead_full, 0, rows)
        from_behind, from_ahead = sources(full_steps + 1)
        cols = jnp.concatenate(
            [
                lax.dynamic_slice_in_dim(tokens, from_behind * rows, half, 1),
                lax.dynamic_slice_in_dim(tokens, from_ahead * rows + half, rows - half, 1),
            ],
            axis=1,
        )
        block = jnp.concatenate([last_ahead, last_behind], axis=0)
        last_terms = product(cols, block)
        terms = tuple(zip(total, first_terms, second_terms, last_terms))
    else:
        from_behind_full, from_ahead_full = sources(full_steps)
        first_terms = partial(ahead, from_behind_full, 0, rows)
        second_terms = partial(behind, from_ahead_full, 0, rows)
        terms = tuple(zip(total, first_terms, second_terms))
    return terms, riders


def tp_bits(count):
    bits = []
    bit = 1
    while bit < count:
        bits.append(bit)
        bit *= 2
    return bits


def spread_weights(out_weight):
    count = lax.axis_size("tp")
    me = lax.axis_index("tp")
    width = out_weight.shape[1] // count
    weights = [lax.dynamic_slice_in_dim(out_weight, me * width, width, 1)]
    for partner in range(1, count):
        pairs = [(k, k ^ partner) for k in range(count)]
        sent = lax.dynamic_slice_in_dim(out_weight, (me ^ partner) * width, width, 1)
        weights.append(lax.ppermute(sent, "tp", pairs))
    return tuple(weights)


def output_projection(gated, weights):
    count = lax.axis_size("tp")
    pieces = {0: gated}
    for bit in reversed(tp_bits(count)):
        pairs = [(k, k ^ bit) for k in range(count)]
        moved = {key ^ bit: lax.ppermute(piece, "tp", pairs) for key, piece in pieces.items()}
        pieces.update(moved)
    total = None
    for key in sorted(pieces):
        part = jnp.dot(pieces[key], weights[key], preferred_element_type=jnp.float32)
        total = part if total is None else total + part
    return total

def halo_rows(tail):
    ctx_count = lax.axis_size("ctx")
    tp_count = lax.axis_size("tp")
    shift = [(k, k + 1) for k in range(ctx_count - 1)]
    if tp_count % 2:
        return lax.ppermute(tail, "ctx", shift)
    width = tail.shape[1] // 2
    side = lax.axis_index("tp") % 2
    mine = lax.ppermute(lax.dynamic_slice_in_dim(tail, side * width, width, 1), "ctx", shift)
    other = lax.ppermute(mine, "tp", [(k, k ^ 1) for k in range(tp_count)])
    return jnp.where(
        side == 0,
        jnp.concatenate([mine, other], axis=1),
        jnp.concatenate([other, mine], axis=1),
    )


def per_device(tokens, in_weight, short_taps, medium_taps, medium_decay, skip_gain, out_weight):
    row_count = tokens.shape[0]
    channel_count = in_weight.shape[2]
    ctx_count = lax.axis_size("ctx")
    medium_count = medium_taps.shape[1]
    short_count = short_taps.shape[2]
    earlier = halo_rows(tokens[row_count - HALO :])
    earlier, in_weight = lax.optimization_barrier((earlier, in_weight))
    widened = jnp.concatenate([earlier, tokens], axis=0)
    features, weights = ring_projection(widened, in_weight, spread_weights(out_weight))
    lag_values = lax.broadcasted_iota(jnp.float32, (1, medium_count), 1)
    filters = medium_taps * jnp.exp(-medium_decay[:, None] * lag_values)
    taps = jnp.pad(
        jnp.transpose(short_taps, (0, 2, 1)), ((0, 0), (0, 8 - short_count), (0, 0))
    ).reshape(3 * 8, channel_count)
    tiles = channel_count // LANES
    parts = 2 if tiles % 2 == 0 else 1
    share = tiles // parts
    medium = jnp.transpose(filters)
    skip = skip_gain.reshape(1, channel_count)
    total = None
    for part in range(parts):
        gated = channel_filter(features, taps, medium, skip, part * share, share)
        rows = slice(part * share * LANES, (part + 1) * share * LANES)
        piece = output_projection(gated, tuple(w[rows] for w in weights))
        total = piece if total is None else total + piece
    return total.astype(jnp.bfloat16)

def solution(mesh):
    return jax.shard_map(
        per_device,
        mesh=mesh,
        in_specs=(
            P("ctx", None),
            P("ctx", None, "tp"),
            P(None, "tp", None),
            P("tp", None),
            P("tp"),
            P("tp"),
            P("tp", None),
        ),
        out_specs=P("ctx", "tp"),
        check_vma=False,
    )
```

```python
import functools

import jax
import jax.numpy as jnp
from jax import lax
from jax.sharding import PartitionSpec as P


from jax.experimental import pallas as pl
from jax.experimental.pallas import tpu as pltpu

HALO = 136
CHUNK = 64
LANES = 128


def filter_kernel(term_count, *refs):
    fields = refs[: 3 * term_count]
    taps, medium, skip, out, raw, prod, shifted, smooth_q = refs[3 * term_count :]
    ext = fields[0].shape[0]
    local = ext - HALO
    taps_count = 7
    short_count = taps.shape[0] // 3
    for slot in range(3):
        group = fields[slot * term_count : (slot + 1) * term_count]
        total = group[0][0:8, :]
        for term in group[1:]:
            total = total + term[0:8, :]
        raw[slot, 0:8, :] = total.astype(jnp.bfloat16).astype(jnp.float32)

    def gather_body(index, carry):
        row = pl.multiple_of(8 + index * CHUNK, 8)
        for slot in range(3):
            group = fields[slot * term_count : (slot + 1) * term_count]
            total = group[0][pl.ds(row, CHUNK), :]
            for term in group[1:]:
                total = total + term[pl.ds(row, CHUNK), :]
            raw[slot, pl.ds(row, CHUNK), :] = total.astype(jnp.bfloat16).astype(jnp.float32)
        return carry

    lax.fori_loop(0, (ext - 8) // CHUNK, gather_body, 0)

    def smooth(slot, row):
        window = raw[slot, pl.ds(row - 8, CHUNK + 8), :]
        total = jnp.zeros((CHUNK, LANES), jnp.float32)
        for lag in range(taps_count):
            weight = taps[pl.ds(slot * short_count + lag, 1), :]
            total = total + weight * window[8 - lag : 8 - lag + CHUNK]
        return total

    def product_body(index, carry):
        row = pl.multiple_of(8 + index * CHUNK, 8)
        prod[pl.ds(row, CHUNK), :] = smooth(1, row) * smooth(2, row)
        return carry

    lax.fori_loop(0, (ext - 8) // CHUNK, product_body, 0)

    def query_body(index, carry):
        row = pl.multiple_of(index * CHUNK, 8)
        smooth_q[pl.ds(row, CHUNK), :] = smooth(0, row + HALO)
        return carry

    lax.fori_loop(0, local // CHUNK, query_body, 0)

    def shift_body(index, carry):
        row = pl.multiple_of(16 + index * CHUNK, 8)
        window = prod[pl.ds(row - 8, CHUNK + 8), :]
        for shift in range(8):
            shifted[shift, pl.ds(row, CHUNK), :] = window[8 - shift : 8 - shift + CHUNK]
        return carry

    lax.fori_loop(0, (ext - 16) // CHUNK, shift_body, 0)
    tail = 16 + ((ext - 16) // CHUNK) * CHUNK
    if tail < ext:
        window = prod[tail - 8 : ext, :]
        for shift in range(8):
            shifted[shift, tail:ext, :] = window[8 - shift : 8 - shift + ext - tail]

    def chunk_body(index, carry):
        row = pl.multiple_of(index * CHUNK, CHUNK)
        at = pl.multiple_of(row + HALO, 8)
        total = skip[...] * prod[pl.ds(at, CHUNK), :]
        groups = medium.shape[0] // 8
        reach = 8 * (groups - 1)
        start = pl.multiple_of(at - reach, 8)
        for shift in range(8):
            window = shifted[shift, pl.ds(start, CHUNK + reach), :]
            for group in range(groups):
                offset = reach - 8 * group
                weight = medium[pl.ds(8 * group + shift, 1), :]
                total = total + weight * window[offset : offset + CHUNK]
        out[pl.ds(row, CHUNK), :] = (smooth_q[pl.ds(row, CHUNK), :] * total).astype(out.dtype)
        return carry

    lax.fori_loop(0, local // CHUNK, chunk_body, 0)


def channel_filter(fields, taps, medium, skip, first, tiles):
    term_count = len(fields[0])
    ext = fields[0][0].shape[0]
    local = ext - HALO
    channels = tiles * LANES

    def field_spec(field):
        return pl.BlockSpec((ext, LANES), lambda t: (0, first + t))

    return pl.pallas_call(
        functools.partial(filter_kernel, term_count),
        grid=(tiles,),
        in_specs=[field_spec(0)] * (3 * term_count)
        + [
            pl.BlockSpec((taps.shape[0], LANES), lambda t: (0, first + t)),
            pl.BlockSpec((medium.shape[0], LANES), lambda t: (0, first + t)),
            pl.BlockSpec((1, LANES), lambda t: (0, first + t)),
        ],
        out_specs=pl.BlockSpec((local, LANES), lambda t: (0, t)),
        out_shape=jax.ShapeDtypeStruct((local, channels), jnp.bfloat16),
        scratch_shapes=[
            pltpu.VMEM((3, ext, LANES), jnp.float32),
            pltpu.VMEM((ext, LANES), jnp.float32),
            pltpu.VMEM((8, ext, LANES), jnp.float32),
            pltpu.VMEM((local, LANES), jnp.float32),
        ],
    )(*[term for field in fields for term in field], taps, medium, skip)

def ring_order(count):
    if count % 2:
        return list(range(count))
    return list(range(0, count, 2)) + list(range(count - 1, 0, -2))


def ring_projection(tokens, in_weight, riders):
    count = lax.axis_size("ctx")
    rows = in_weight.shape[0]
    order = ring_order(count)
    place = [0] * count
    for at, member in enumerate(order):
        place[member] = at
    forward = [(order[k], order[(k + 1) % count]) for k in range(count)]
    backward = [(order[k], order[(k - 1) % count]) for k in range(count)]
    me = lax.axis_index("ctx")
    order_table = jnp.array(order, jnp.int32)
    my_place = jnp.array(place, jnp.int32)[me]

    def product(cols, block):
        return tuple(
            jnp.dot(cols, block[:, field, :], preferred_element_type=jnp.float32)
            for field in range(block.shape[1])
        )

    def plus(left, right):
        return tuple(a + b for a, b in zip(left, right))

    def partial(block, source, start, width):
        cols = lax.dynamic_slice_in_dim(tokens, source * rows + start, width, 1)
        return product(cols, block)

    total = partial(in_weight, me, 0, rows)
    full_steps = (count - 1) // 2
    half = rows // 2

    def sources(step):
        return (
            order_table[(my_place - step) % count],
            order_table[(my_place + step) % count],
        )

    def add_pair(total, ahead, behind, step):
        from_behind, from_ahead = sources(step)
        total = plus(total, partial(ahead, from_behind, 0, rows))
        return plus(total, partial(behind, from_ahead, 0, rows))

    def ring_step(step, carry):
        ahead, behind, total = carry
        moved_ahead = lax.ppermute(ahead, "ctx", forward)
        moved_behind = lax.ppermute(behind, "ctx", backward)
        total = add_pair(total, ahead, behind, step - 1)
        return (moved_ahead, moved_behind, total)

    if full_steps == 0:
        return tuple((part,) for part in total), riders
    ahead = lax.ppermute(in_weight, "ctx", forward)
    behind = lax.ppermute(in_weight, "ctx", backward)
    carry = (ahead, behind, total)
    if full_steps >= 2:
        carry = ring_step(2, carry)
    carry, riders = lax.optimization_barrier((carry, riders))

    def carried_step(step, state):
        return (ring_step(step, state[0]), state[1])

    carry, riders = lax.fori_loop(3, full_steps + 1, carried_step, (carry, riders))
    ahead, behind, total = carry
    if count % 2 == 0:
        last_ahead = lax.ppermute(ahead[:half], "ctx", forward)
        last_behind = lax.ppermute(behind[half:], "ctx", backward)
        from_behind_full, from_ahead_full = sources(full_steps)
        first_terms = partial(ahead, from_behind_full, 0, rows)
        second_terms = partial(behind, from_ahead_full, 0, rows)
        from_behind, from_ahead = sources(full_steps + 1)
        cols = jnp.concatenate(
            [
                lax.dynamic_slice_in_dim(tokens, from_behind * rows, half, 1),
                lax.dynamic_slice_in_dim(tokens, from_ahead * rows + half, rows - half, 1),
            ],
            axis=1,
        )
        block = jnp.concatenate([last_ahead, last_behind], axis=0)
        last_terms = product(cols, block)
        terms = tuple(zip(total, first_terms, second_terms, last_terms))
    else:
        from_behind_full, from_ahead_full = sources(full_steps)
        first_terms = partial(ahead, from_behind_full, 0, rows)
        second_terms = partial(behind, from_ahead_full, 0, rows)
        terms = tuple(zip(total, first_terms, second_terms))
    return terms, riders


def tp_bits(count):
    bits = []
    bit = 1
    while bit < count:
        bits.append(bit)
        bit *= 2
    return bits


def spread_weights(out_weight):
    count = lax.axis_size("tp")
    me = lax.axis_index("tp")
    width = out_weight.shape[1] // count
    weights = [lax.dynamic_slice_in_dim(out_weight, me * width, width, 1)]
    for partner in range(1, count):
        pairs = [(k, k ^ partner) for k in range(count)]
        sent = lax.dynamic_slice_in_dim(out_weight, (me ^ partner) * width, width, 1)
        weights.append(lax.ppermute(sent, "tp", pairs))
    return tuple(weights)


def output_projection(gated, weights):
    count = lax.axis_size("tp")
    pieces = {0: gated}
    for bit in reversed(tp_bits(count)):
        pairs = [(k, k ^ bit) for k in range(count)]
        moved = {key ^ bit: lax.ppermute(piece, "tp", pairs) for key, piece in pieces.items()}
        pieces.update(moved)
    stacked = jnp.concatenate([pieces[key] for key in sorted(pieces)], axis=1)
    return jnp.dot(stacked, weights, preferred_element_type=jnp.float32)

def halo_rows(tail):
    ctx_count = lax.axis_size("ctx")
    tp_count = lax.axis_size("tp")
    shift = [(k, k + 1) for k in range(ctx_count - 1)]
    if tp_count % 2:
        return lax.ppermute(tail, "ctx", shift)
    width = tail.shape[1] // 2
    side = lax.axis_index("tp") % 2
    mine = lax.ppermute(lax.dynamic_slice_in_dim(tail, side * width, width, 1), "ctx", shift)
    other = lax.ppermute(mine, "tp", [(k, k ^ 1) for k in range(tp_count)])
    return jnp.where(
        side == 0,
        jnp.concatenate([mine, other], axis=1),
        jnp.concatenate([other, mine], axis=1),
    )


def per_device(tokens, in_weight, short_taps, medium_taps, medium_decay, skip_gain, out_weight):
    row_count = tokens.shape[0]
    channel_count = in_weight.shape[2]
    ctx_count = lax.axis_size("ctx")
    medium_count = medium_taps.shape[1]
    short_count = short_taps.shape[2]
    earlier = halo_rows(tokens[row_count - HALO :])
    earlier, in_weight = lax.optimization_barrier((earlier, in_weight))
    widened = jnp.concatenate([earlier, tokens], axis=0)
    blocks = spread_weights(out_weight)
    tiles = channel_count // LANES
    parts = 2 if tiles % 2 == 0 else 1
    share = tiles // parts
    width = share * LANES
    stacked = tuple(
        jnp.concatenate([w[part * width : (part + 1) * width] for w in blocks], axis=0)
        for part in range(parts)
    )
    features, stacked = ring_projection(widened, in_weight, stacked)
    lag_values = lax.broadcasted_iota(jnp.float32, (1, medium_count), 1)
    filters = medium_taps * jnp.exp(-medium_decay[:, None] * lag_values)
    taps = jnp.pad(
        jnp.transpose(short_taps, (0, 2, 1)), ((0, 0), (0, 8 - short_count), (0, 0))
    ).reshape(3 * 8, channel_count)
    medium = jnp.transpose(filters)
    skip = skip_gain.reshape(1, channel_count)
    total = None
    for part in range(parts):
        gated = channel_filter(features, taps, medium, skip, part * share, share)
        piece = output_projection(gated, stacked[part])
        total = piece if total is None else total + piece
    return total.astype(jnp.bfloat16)

def solution(mesh):
    return jax.shard_map(
        per_device,
        mesh=mesh,
        in_specs=(
            P("ctx", None),
            P("ctx", None, "tp"),
            P(None, "tp", None),
            P("tp", None),
            P("tp"),
            P("tp"),
            P("tp", None),
        ),
        out_specs=P("ctx", "tp"),
        check_vma=False,
    )
```

```python
import functools

import jax
import jax.numpy as jnp
from jax import lax
from jax.sharding import PartitionSpec as P


from jax.experimental import pallas as pl
from jax.experimental.pallas import tpu as pltpu

HALO = 136
CHUNK = 64
LANES = 128


def filter_kernel(term_count, halo, *refs):
    fields = refs[: 3 * term_count]
    taps, medium, skip, out, raw, prod, shifted, smooth_q = refs[3 * term_count :]
    local = fields[0].shape[0]
    ext = local + HALO
    taps_count = 7
    short_count = taps.shape[0] // 3
    for slot in range(3):
        raw[slot, 0:HALO, :] = halo[slot].astype(jnp.float32)

    def gather_body(index, carry):
        row = pl.multiple_of(index * CHUNK, 8)
        for slot in range(3):
            group = fields[slot * term_count : (slot + 1) * term_count]
            total = group[0][pl.ds(row, CHUNK), :]
            for term in group[1:]:
                total = total + term[pl.ds(row, CHUNK), :]
            raw[slot, pl.ds(row + HALO, CHUNK), :] = total.astype(jnp.bfloat16).astype(
                jnp.float32
            )
        return carry

    lax.fori_loop(0, local // CHUNK, gather_body, 0)

    def smooth(slot, row):
        window = raw[slot, pl.ds(row - 8, CHUNK + 8), :]
        total = jnp.zeros((CHUNK, LANES), jnp.float32)
        for lag in range(taps_count):
            weight = taps[pl.ds(slot * short_count + lag, 1), :]
            total = total + weight * window[8 - lag : 8 - lag + CHUNK]
        return total

    def product_body(index, carry):
        row = pl.multiple_of(8 + index * CHUNK, 8)
        prod[pl.ds(row, CHUNK), :] = smooth(1, row) * smooth(2, row)
        return carry

    lax.fori_loop(0, (ext - 8) // CHUNK, product_body, 0)

    def query_body(index, carry):
        row = pl.multiple_of(index * CHUNK, 8)
        smooth_q[pl.ds(row, CHUNK), :] = smooth(0, row + HALO)
        return carry

    lax.fori_loop(0, local // CHUNK, query_body, 0)

    def shift_body(index, carry):
        row = pl.multiple_of(16 + index * CHUNK, 8)
        window = prod[pl.ds(row - 8, CHUNK + 8), :]
        for shift in range(8):
            shifted[shift, pl.ds(row, CHUNK), :] = window[8 - shift : 8 - shift + CHUNK]
        return carry

    lax.fori_loop(0, (ext - 16) // CHUNK, shift_body, 0)
    tail = 16 + ((ext - 16) // CHUNK) * CHUNK
    if tail < ext:
        window = prod[tail - 8 : ext, :]
        for shift in range(8):
            shifted[shift, tail:ext, :] = window[8 - shift : 8 - shift + ext - tail]

    def chunk_body(index, carry):
        row = pl.multiple_of(index * CHUNK, CHUNK)
        at = pl.multiple_of(row + HALO, 8)
        total = skip[...] * prod[pl.ds(at, CHUNK), :]
        groups = medium.shape[0] // 8
        reach = 8 * (groups - 1)
        start = pl.multiple_of(at - reach, 8)
        for shift in range(8):
            window = shifted[shift, pl.ds(start, CHUNK + reach), :]
            for group in range(groups):
                offset = reach - 8 * group
                weight = medium[pl.ds(8 * group + shift, 1), :]
                total = total + weight * window[offset : offset + CHUNK]
        out[pl.ds(row, CHUNK), :] = (smooth_q[pl.ds(row, CHUNK), :] * total).astype(out.dtype)
        return carry

    lax.fori_loop(0, local // CHUNK, chunk_body, 0)


def channel_filter(halo, fields, taps, medium, skip, first, tiles):
    term_count = len(fields[0])
    local = fields[0][0].shape[0]
    ext = local + HALO
    channels = tiles * LANES

    def field_spec(field):
        return pl.BlockSpec((local, LANES), lambda t: (0, first + t))

    return pl.pallas_call(
        functools.partial(filter_kernel, term_count),
        grid=(tiles,),
        in_specs=[pl.BlockSpec((3, HALO, LANES), lambda t: (0, 0, t))]
        + [field_spec(0)] * (3 * term_count)
        + [
            pl.BlockSpec((taps.shape[0], LANES), lambda t: (0, first + t)),
            pl.BlockSpec((medium.shape[0], LANES), lambda t: (0, first + t)),
            pl.BlockSpec((1, LANES), lambda t: (0, first + t)),
        ],
        out_specs=pl.BlockSpec((local, LANES), lambda t: (0, t)),
        out_shape=jax.ShapeDtypeStruct((local, channels), jnp.bfloat16),
        scratch_shapes=[
            pltpu.VMEM((3, ext, LANES), jnp.float32),
            pltpu.VMEM((ext, LANES), jnp.float32),
            pltpu.VMEM((8, ext, LANES), jnp.float32),
            pltpu.VMEM((local, LANES), jnp.float32),
        ],
    )(halo, *[term for field in fields for term in field], taps, medium, skip)

def ring_order(count):
    if count % 2:
        return list(range(count))
    return list(range(0, count, 2)) + list(range(count - 1, 0, -2))


def ring_projection(tokens, in_weight, riders):
    count = lax.axis_size("ctx")
    rows = in_weight.shape[0]
    order = ring_order(count)
    place = [0] * count
    for at, member in enumerate(order):
        place[member] = at
    forward = [(order[k], order[(k + 1) % count]) for k in range(count)]
    backward = [(order[k], order[(k - 1) % count]) for k in range(count)]
    me = lax.axis_index("ctx")
    order_table = jnp.array(order, jnp.int32)
    my_place = jnp.array(place, jnp.int32)[me]

    def product(cols, block):
        return tuple(
            jnp.dot(cols, block[:, field, :], preferred_element_type=jnp.float32)
            for field in range(block.shape[1])
        )

    def plus(left, right):
        return tuple(a + b for a, b in zip(left, right))

    def partial(block, source, start, width):
        cols = lax.dynamic_slice_in_dim(tokens, source * rows + start, width, 1)
        return product(cols, block)

    total = partial(in_weight, me, 0, rows)
    full_steps = (count - 1) // 2
    half = rows // 2

    def sources(step):
        return (
            order_table[(my_place - step) % count],
            order_table[(my_place + step) % count],
        )

    def add_pair(total, ahead, behind, step):
        from_behind, from_ahead = sources(step)
        total = plus(total, partial(ahead, from_behind, 0, rows))
        return plus(total, partial(behind, from_ahead, 0, rows))

    def ring_step(step, carry):
        ahead, behind, total = carry
        moved_ahead = lax.ppermute(ahead, "ctx", forward)
        moved_behind = lax.ppermute(behind, "ctx", backward)
        total = add_pair(total, ahead, behind, step - 1)
        return (moved_ahead, moved_behind, total)

    if full_steps == 0:
        return tuple((part,) for part in total), riders
    ahead = lax.ppermute(in_weight, "ctx", forward)
    behind = lax.ppermute(in_weight, "ctx", backward)
    carry = (ahead, behind, total)
    if full_steps >= 2:
        carry = ring_step(2, carry)
    carry, riders = lax.optimization_barrier((carry, riders))

    def carried_step(step, state):
        return (ring_step(step, state[0]), state[1])

    carry, riders = lax.fori_loop(3, full_steps + 1, carried_step, (carry, riders))
    ahead, behind, total = carry
    if count % 2 == 0:
        last_ahead = lax.ppermute(ahead[:half], "ctx", forward)
        last_behind = lax.ppermute(behind[half:], "ctx", backward)
        from_behind_full, from_ahead_full = sources(full_steps)
        first_terms = partial(ahead, from_behind_full, 0, rows)
        second_terms = partial(behind, from_ahead_full, 0, rows)
        from_behind, from_ahead = sources(full_steps + 1)
        cols = jnp.concatenate(
            [
                lax.dynamic_slice_in_dim(tokens, from_behind * rows, half, 1),
                lax.dynamic_slice_in_dim(tokens, from_ahead * rows + half, rows - half, 1),
            ],
            axis=1,
        )
        block = jnp.concatenate([last_ahead, last_behind], axis=0)
        last_terms = product(cols, block)
        terms = tuple(zip(total, first_terms, second_terms, last_terms))
    else:
        from_behind_full, from_ahead_full = sources(full_steps)
        first_terms = partial(ahead, from_behind_full, 0, rows)
        second_terms = partial(behind, from_ahead_full, 0, rows)
        terms = tuple(zip(total, first_terms, second_terms))
    return terms, riders


def tp_bits(count):
    bits = []
    bit = 1
    while bit < count:
        bits.append(bit)
        bit *= 2
    return bits


def spread_weights(out_weight):
    count = lax.axis_size("tp")
    me = lax.axis_index("tp")
    width = out_weight.shape[1] // count
    weights = [lax.dynamic_slice_in_dim(out_weight, me * width, width, 1)]
    for partner in range(1, count):
        pairs = [(k, k ^ partner) for k in range(count)]
        sent = lax.dynamic_slice_in_dim(out_weight, (me ^ partner) * width, width, 1)
        weights.append(lax.ppermute(sent, "tp", pairs))
    return tuple(weights)


def output_projection(gated, weights):
    count = lax.axis_size("tp")
    pieces = {0: gated}
    for bit in reversed(tp_bits(count)):
        pairs = [(k, k ^ bit) for k in range(count)]
        moved = {key ^ bit: lax.ppermute(piece, "tp", pairs) for key, piece in pieces.items()}
        pieces.update(moved)
    total = None
    for key in sorted(pieces):
        part = jnp.dot(pieces[key], weights[key], preferred_element_type=jnp.float32)
        total = part if total is None else total + part
    return total

def halo_rows(tail):
    ctx_count = lax.axis_size("ctx")
    tp_count = lax.axis_size("tp")
    shift = [(k, k + 1) for k in range(ctx_count - 1)]
    if tp_count % 2:
        return lax.ppermute(tail, "ctx", shift)
    width = tail.shape[1] // 2
    side = lax.axis_index("tp") % 2
    mine = lax.ppermute(lax.dynamic_slice_in_dim(tail, side * width, width, 1), "ctx", shift)
    other = lax.ppermute(mine, "tp", [(k, k ^ 1) for k in range(tp_count)])
    return jnp.where(
        side == 0,
        jnp.concatenate([mine, other], axis=1),
        jnp.concatenate([other, mine], axis=1),
    )


def per_device(tokens, in_weight, short_taps, medium_taps, medium_decay, skip_gain, out_weight):
    row_count = tokens.shape[0]
    channel_count = in_weight.shape[2]
    ctx_count = lax.axis_size("ctx")
    medium_count = medium_taps.shape[1]
    short_count = short_taps.shape[2]
    features, weights = ring_projection(tokens, in_weight, spread_weights(out_weight))
    lag_values = lax.broadcasted_iota(jnp.float32, (1, medium_count), 1)
    filters = medium_taps * jnp.exp(-medium_decay[:, None] * lag_values)
    taps = jnp.pad(
        jnp.transpose(short_taps, (0, 2, 1)), ((0, 0), (0, 8 - short_count), (0, 0))
    ).reshape(3 * 8, channel_count)
    tiles = channel_count // LANES
    parts = 2 if tiles % 2 == 0 else 1
    share = tiles // parts
    medium = jnp.transpose(filters)
    skip = skip_gain.reshape(1, channel_count)
    total = None
    for part in range(parts):
        cols = slice(part * share * LANES, (part + 1) * share * LANES)
        tail = jnp.stack(
            [
                sum(term[row_count - HALO :, cols] for term in field).astype(jnp.bfloat16)
                for field in features
            ]
        )
        halo = lax.ppermute(tail, "ctx", [(k, k + 1) for k in range(ctx_count - 1)])
        gated = channel_filter(halo, features, taps, medium, skip, part * share, share)
        rows = slice(part * share * LANES, (part + 1) * share * LANES)
        piece = output_projection(gated, tuple(w[rows] for w in weights))
        total = piece if total is None else total + piece
    return total.astype(jnp.bfloat16)

def solution(mesh):
    return jax.shard_map(
        per_device,
        mesh=mesh,
        in_specs=(
            P("ctx", None),
            P("ctx", None, "tp"),
            P(None, "tp", None),
            P("tp", None),
            P("tp"),
            P("tp"),
            P("tp", None),
        ),
        out_specs=P("ctx", "tp"),
        check_vma=False,
    )
```

```python
import functools

import jax
import jax.numpy as jnp
from jax import lax
from jax.sharding import PartitionSpec as P


from jax.experimental import pallas as pl
from jax.experimental.pallas import tpu as pltpu

HALO = 136
CHUNK = 64
LANES = 128


def filter_kernel(term_count, halo, *refs):
    fields = refs[: 3 * term_count]
    taps, medium, skip, out, raw, prod, shifted, smooth_q = refs[3 * term_count :]
    local = fields[0].shape[0]
    ext = local + HALO
    taps_count = 7
    short_count = taps.shape[0] // 3
    for slot in range(3):
        raw[slot, 0:HALO, :] = halo[slot].astype(jnp.float32)

    def gather_body(index, carry):
        row = pl.multiple_of(index * CHUNK, 8)
        for slot in range(3):
            group = fields[slot * term_count : (slot + 1) * term_count]
            total = group[0][pl.ds(row, CHUNK), :]
            for term in group[1:]:
                total = total + term[pl.ds(row, CHUNK), :]
            raw[slot, pl.ds(row + HALO, CHUNK), :] = total.astype(jnp.bfloat16).astype(
                jnp.float32
            )
        return carry

    lax.fori_loop(0, local // CHUNK, gather_body, 0)

    def smooth(slot, row):
        window = raw[slot, pl.ds(row - 8, CHUNK + 8), :]
        total = jnp.zeros((CHUNK, LANES), jnp.float32)
        for lag in range(taps_count):
            weight = taps[pl.ds(slot * short_count + lag, 1), :]
            total = total + weight * window[8 - lag : 8 - lag + CHUNK]
        return total

    def product_body(index, carry):
        row = pl.multiple_of(8 + index * CHUNK, 8)
        prod[pl.ds(row, CHUNK), :] = smooth(1, row) * smooth(2, row)
        return carry

    lax.fori_loop(0, (ext - 8) // CHUNK, product_body, 0)

    def query_body(index, carry):
        row = pl.multiple_of(index * CHUNK, 8)
        smooth_q[pl.ds(row, CHUNK), :] = smooth(0, row + HALO)
        return carry

    lax.fori_loop(0, local // CHUNK, query_body, 0)

    def shift_body(index, carry):
        row = pl.multiple_of(16 + index * CHUNK, 8)
        window = prod[pl.ds(row - 8, CHUNK + 8), :]
        for shift in range(8):
            shifted[shift, pl.ds(row, CHUNK), :] = window[8 - shift : 8 - shift + CHUNK]
        return carry

    lax.fori_loop(0, (ext - 16) // CHUNK, shift_body, 0)
    tail = 16 + ((ext - 16) // CHUNK) * CHUNK
    if tail < ext:
        window = prod[tail - 8 : ext, :]
        for shift in range(8):
            shifted[shift, tail:ext, :] = window[8 - shift : 8 - shift + ext - tail]

    def chunk_body(index, carry):
        row = pl.multiple_of(index * CHUNK, CHUNK)
        at = pl.multiple_of(row + HALO, 8)
        total = skip[...] * prod[pl.ds(at, CHUNK), :]
        groups = medium.shape[0] // 8
        reach = 8 * (groups - 1)
        start = pl.multiple_of(at - reach, 8)
        for shift in range(8):
            window = shifted[shift, pl.ds(start, CHUNK + reach), :]
            for group in range(groups):
                offset = reach - 8 * group
                weight = medium[pl.ds(8 * group + shift, 1), :]
                total = total + weight * window[offset : offset + CHUNK]
        out[pl.ds(row, CHUNK), :] = (smooth_q[pl.ds(row, CHUNK), :] * total).astype(out.dtype)
        return carry

    lax.fori_loop(0, local // CHUNK, chunk_body, 0)


def channel_filter(halo, fields, taps, medium, skip, first, tiles):
    term_count = len(fields[0])
    local = fields[0][0][0].shape[0]
    ext = local + HALO
    channels = tiles * LANES

    def field_spec(shift):
        return pl.BlockSpec((local, LANES), lambda t: (0, shift + t))

    return pl.pallas_call(
        functools.partial(filter_kernel, term_count),
        grid=(tiles,),
        in_specs=[pl.BlockSpec((3, HALO, LANES), lambda t: (0, 0, t))]
        + [field_spec(shift) for field in fields for _, shift in field]
        + [
            pl.BlockSpec((taps.shape[0], LANES), lambda t: (0, first + t)),
            pl.BlockSpec((medium.shape[0], LANES), lambda t: (0, first + t)),
            pl.BlockSpec((1, LANES), lambda t: (0, first + t)),
        ],
        out_specs=pl.BlockSpec((local, LANES), lambda t: (0, t)),
        out_shape=jax.ShapeDtypeStruct((local, channels), jnp.bfloat16),
        scratch_shapes=[
            pltpu.VMEM((3, ext, LANES), jnp.float32),
            pltpu.VMEM((ext, LANES), jnp.float32),
            pltpu.VMEM((8, ext, LANES), jnp.float32),
            pltpu.VMEM((local, LANES), jnp.float32),
        ],
    )(halo, *[term for field in fields for term, _ in field], taps, medium, skip)

def ring_order(count):
    if count % 2:
        return list(range(count))
    return list(range(0, count, 2)) + list(range(count - 1, 0, -2))


def ring_projection(tokens, in_weight, riders, parts):
    count = lax.axis_size("ctx")
    rows = in_weight.shape[0]
    order = ring_order(count)
    place = [0] * count
    for at, member in enumerate(order):
        place[member] = at
    forward = [(order[k], order[(k + 1) % count]) for k in range(count)]
    backward = [(order[k], order[(k - 1) % count]) for k in range(count)]
    me = lax.axis_index("ctx")
    order_table = jnp.array(order, jnp.int32)
    my_place = jnp.array(place, jnp.int32)[me]

    def product(cols, block):
        return tuple(
            jnp.dot(cols, block[:, field, :], preferred_element_type=jnp.float32)
            for field in range(block.shape[1])
        )

    def plus(left, right):
        return tuple(a + b for a, b in zip(left, right))

    def partial(block, source, start, width):
        cols = lax.dynamic_slice_in_dim(tokens, source * rows + start, width, 1)
        return product(cols, block)

    total = partial(in_weight, me, 0, rows)
    full_steps = (count - 1) // 2
    half = rows // 2

    def sources(step):
        return (
            order_table[(my_place - step) % count],
            order_table[(my_place + step) % count],
        )

    def add_pair(total, ahead, behind, step):
        from_behind, from_ahead = sources(step)
        total = plus(total, partial(ahead, from_behind, 0, rows))
        return plus(total, partial(behind, from_ahead, 0, rows))

    def ring_step(step, carry):
        ahead, behind, total = carry
        moved_ahead = lax.ppermute(ahead, "ctx", forward)
        moved_behind = lax.ppermute(behind, "ctx", backward)
        total = add_pair(total, ahead, behind, step - 1)
        return (moved_ahead, moved_behind, total)

    if full_steps == 0:
        return tuple(((part, None),) for part in total), riders, None
    ahead = lax.ppermute(in_weight, "ctx", forward)
    behind = lax.ppermute(in_weight, "ctx", backward)
    carry = (ahead, behind, total)
    if full_steps >= 2:
        carry = ring_step(2, carry)
    carry, riders = lax.optimization_barrier((carry, riders))

    def carried_step(step, state):
        return (ring_step(step, state[0]), state[1])

    carry, riders = lax.fori_loop(3, full_steps + 1, carried_step, (carry, riders))
    ahead, behind, total = carry
    if count % 2 == 0:
        last_ahead = lax.ppermute(ahead[:half], "ctx", forward)
        last_behind = lax.ppermute(behind[half:], "ctx", backward)
        from_behind_full, from_ahead_full = sources(full_steps)
        first_terms = partial(ahead, from_behind_full, 0, rows)
        second_terms = partial(behind, from_ahead_full, 0, rows)
        from_behind, from_ahead = sources(full_steps + 1)
        cols = jnp.concatenate(
            [
                lax.dynamic_slice_in_dim(tokens, from_behind * rows, half, 1),
                lax.dynamic_slice_in_dim(tokens, from_ahead * rows + half, rows - half, 1),
            ],
            axis=1,
        )
        block = jnp.concatenate([last_ahead, last_behind], axis=0)
        terms = tuple(
            tuple((term, None) for term in group)
            for group in zip(total, first_terms, second_terms)
        )
        return terms, riders, (cols, block)
    else:
        from_behind_full, from_ahead_full = sources(full_steps)
        first_terms = partial(ahead, from_behind_full, 0, rows)
        second_terms = partial(behind, from_ahead_full, 0, rows)
        terms = tuple(
            tuple((term, None) for term in group)
            for group in zip(total, first_terms, second_terms)
        )
    return terms, riders, None


def tp_bits(count):
    bits = []
    bit = 1
    while bit < count:
        bits.append(bit)
        bit *= 2
    return bits


def spread_weights(out_weight):
    count = lax.axis_size("tp")
    me = lax.axis_index("tp")
    width = out_weight.shape[1] // count
    weights = [lax.dynamic_slice_in_dim(out_weight, me * width, width, 1)]
    for partner in range(1, count):
        pairs = [(k, k ^ partner) for k in range(count)]
        sent = lax.dynamic_slice_in_dim(out_weight, (me ^ partner) * width, width, 1)
        weights.append(lax.ppermute(sent, "tp", pairs))
    return tuple(weights)


def output_projection(gated, weights):
    count = lax.axis_size("tp")
    pieces = {0: gated}
    for bit in reversed(tp_bits(count)):
        pairs = [(k, k ^ bit) for k in range(count)]
        moved = {key ^ bit: lax.ppermute(piece, "tp", pairs) for key, piece in pieces.items()}
        pieces.update(moved)
    total = None
    for key in sorted(pieces):
        part = jnp.dot(pieces[key], weights[key], preferred_element_type=jnp.float32)
        total = part if total is None else total + part
    return total

def halo_rows(tail):
    ctx_count = lax.axis_size("ctx")
    tp_count = lax.axis_size("tp")
    shift = [(k, k + 1) for k in range(ctx_count - 1)]
    if tp_count % 2:
        return lax.ppermute(tail, "ctx", shift)
    width = tail.shape[1] // 2
    side = lax.axis_index("tp") % 2
    mine = lax.ppermute(lax.dynamic_slice_in_dim(tail, side * width, width, 1), "ctx", shift)
    other = lax.ppermute(mine, "tp", [(k, k ^ 1) for k in range(tp_count)])
    return jnp.where(
        side == 0,
        jnp.concatenate([mine, other], axis=1),
        jnp.concatenate([other, mine], axis=1),
    )


def per_device(tokens, in_weight, short_taps, medium_taps, medium_decay, skip_gain, out_weight):
    row_count = tokens.shape[0]
    channel_count = in_weight.shape[2]
    ctx_count = lax.axis_size("ctx")
    medium_count = medium_taps.shape[1]
    short_count = short_taps.shape[2]
    lag_values = lax.broadcasted_iota(jnp.float32, (1, medium_count), 1)
    filters = medium_taps * jnp.exp(-medium_decay[:, None] * lag_values)
    taps = jnp.pad(
        jnp.transpose(short_taps, (0, 2, 1)), ((0, 0), (0, 8 - short_count), (0, 0))
    ).reshape(3 * 8, channel_count)
    tiles = channel_count // LANES
    parts = 2 if tiles % 2 == 0 else 1
    share = tiles // parts
    medium = jnp.transpose(filters)
    features, weights, last = ring_projection(tokens, in_weight, spread_weights(out_weight), parts)
    tail = None
    skip = skip_gain.reshape(1, channel_count)
    total = None
    for part in range(parts):
        cols = slice(part * share * LANES, (part + 1) * share * LANES)
        chosen = tuple(tuple((term, part * share) for term, _ in field) for field in features)
        if last is not None:
            cols_in, block = last
            if tail is not None:
                cols_in, block, _ = lax.optimization_barrier((cols_in, block, tail))
            chosen = tuple(
                field
                + (
                    (
                        jnp.dot(
                            cols_in,
                            block[:, index, cols],
                            preferred_element_type=jnp.float32,
                        ),
                        0,
                    ),
                )
                for index, field in enumerate(chosen)
            )
        tail = jnp.stack(
            [
                sum(
                    term[row_count - HALO :, cols] if shift else term[row_count - HALO :, : cols.stop - cols.start]
                    for term, shift in field
                ).astype(jnp.bfloat16)
                for field in chosen
            ]
        )
        halo = lax.ppermute(tail, "ctx", [(k, k + 1) for k in range(ctx_count - 1)])
        gated = channel_filter(halo, chosen, taps, medium, skip, part * share, share)
        rows = slice(part * share * LANES, (part + 1) * share * LANES)
        piece = output_projection(gated, tuple(w[rows] for w in weights))
        total = piece if total is None else total + piece
    return total.astype(jnp.bfloat16)

def solution(mesh):
    return jax.shard_map(
        per_device,
        mesh=mesh,
        in_specs=(
            P("ctx", None),
            P("ctx", None, "tp"),
            P(None, "tp", None),
            P("tp", None),
            P("tp"),
            P("tp"),
            P("tp", None),
        ),
        out_specs=P("ctx", "tp"),
        check_vma=False,
    )
```

```python
import functools

import jax
import jax.numpy as jnp
from jax import lax
from jax.sharding import PartitionSpec as P


from jax.experimental import pallas as pl
from jax.experimental.pallas import tpu as pltpu

HALO = 136
CHUNK = 64
LANES = 128


def filter_kernel(term_count, halo, *refs):
    fields = refs[: 3 * term_count]
    taps, medium, skip, out, raw, prod, shifted, smooth_q = refs[3 * term_count :]
    local = fields[0].shape[0]
    ext = local + HALO
    taps_count = 7
    short_count = taps.shape[0] // 3
    for slot in range(3):
        raw[slot, 0:HALO, :] = halo[slot].astype(jnp.float32)

    def gather_body(index, carry):
        row = pl.multiple_of(index * CHUNK, 8)
        for slot in range(3):
            group = fields[slot * term_count : (slot + 1) * term_count]
            total = group[0][pl.ds(row, CHUNK), :]
            for term in group[1:]:
                total = total + term[pl.ds(row, CHUNK), :]
            raw[slot, pl.ds(row + HALO, CHUNK), :] = total.astype(jnp.bfloat16).astype(
                jnp.float32
            )
        return carry

    lax.fori_loop(0, local // CHUNK, gather_body, 0)

    def smooth(slot, row):
        window = raw[slot, pl.ds(row - 8, CHUNK + 8), :]
        total = jnp.zeros((CHUNK, LANES), jnp.float32)
        for lag in range(taps_count):
            weight = taps[pl.ds(slot * short_count + lag, 1), :]
            total = total + weight * window[8 - lag : 8 - lag + CHUNK]
        return total

    def product_body(index, carry):
        row = pl.multiple_of(8 + index * CHUNK, 8)
        prod[pl.ds(row, CHUNK), :] = smooth(1, row) * smooth(2, row)
        return carry

    lax.fori_loop(0, (ext - 8) // CHUNK, product_body, 0)

    def query_body(index, carry):
        row = pl.multiple_of(index * CHUNK, 8)
        smooth_q[pl.ds(row, CHUNK), :] = smooth(0, row + HALO)
        return carry

    lax.fori_loop(0, local // CHUNK, query_body, 0)

    def shift_body(index, carry):
        row = pl.multiple_of(16 + index * CHUNK, 8)
        window = prod[pl.ds(row - 8, CHUNK + 8), :]
        for shift in range(8):
            shifted[shift, pl.ds(row, CHUNK), :] = window[8 - shift : 8 - shift + CHUNK]
        return carry

    lax.fori_loop(0, (ext - 16) // CHUNK, shift_body, 0)
    tail = 16 + ((ext - 16) // CHUNK) * CHUNK
    if tail < ext:
        window = prod[tail - 8 : ext, :]
        for shift in range(8):
            shifted[shift, tail:ext, :] = window[8 - shift : 8 - shift + ext - tail]

    def chunk_body(index, carry):
        row = pl.multiple_of(index * CHUNK, CHUNK)
        at = pl.multiple_of(row + HALO, 8)
        total = skip[...] * prod[pl.ds(at, CHUNK), :]
        groups = medium.shape[0] // 8
        reach = 8 * (groups - 1)
        start = pl.multiple_of(at - reach, 8)
        for shift in range(8):
            window = shifted[shift, pl.ds(start, CHUNK + reach), :]
            for group in range(groups):
                offset = reach - 8 * group
                weight = medium[pl.ds(8 * group + shift, 1), :]
                total = total + weight * window[offset : offset + CHUNK]
        out[pl.ds(row, CHUNK), :] = (smooth_q[pl.ds(row, CHUNK), :] * total).astype(out.dtype)
        return carry

    lax.fori_loop(0, local // CHUNK, chunk_body, 0)


def channel_filter(halo, fields, taps, medium, skip, first, tiles):
    term_count = len(fields[0])
    local = fields[0][0][0].shape[0]
    ext = local + HALO
    channels = tiles * LANES

    def field_spec(shift):
        return pl.BlockSpec((local, LANES), lambda t: (0, shift + t))

    return pl.pallas_call(
        functools.partial(filter_kernel, term_count),
        grid=(tiles,),
        in_specs=[pl.BlockSpec((3, HALO, LANES), lambda t: (0, 0, t))]
        + [field_spec(shift) for field in fields for _, shift in field]
        + [
            pl.BlockSpec((taps.shape[0], LANES), lambda t: (0, first + t)),
            pl.BlockSpec((medium.shape[0], LANES), lambda t: (0, first + t)),
            pl.BlockSpec((1, LANES), lambda t: (0, first + t)),
        ],
        out_specs=pl.BlockSpec((local, LANES), lambda t: (0, t)),
        out_shape=jax.ShapeDtypeStruct((local, channels), jnp.bfloat16),
        scratch_shapes=[
            pltpu.VMEM((3, ext, LANES), jnp.float32),
            pltpu.VMEM((ext, LANES), jnp.float32),
            pltpu.VMEM((8, ext, LANES), jnp.float32),
            pltpu.VMEM((local, LANES), jnp.float32),
        ],
    )(halo, *[term for field in fields for term, _ in field], taps, medium, skip)

def ring_order(count):
    if count % 2:
        return list(range(count))
    return list(range(0, count, 2)) + list(range(count - 1, 0, -2))


def ring_projection(tokens, in_weight, riders, parts):
    count = lax.axis_size("ctx")
    rows = in_weight.shape[0]
    order = ring_order(count)
    place = [0] * count
    for at, member in enumerate(order):
        place[member] = at
    forward = [(order[k], order[(k + 1) % count]) for k in range(count)]
    backward = [(order[k], order[(k - 1) % count]) for k in range(count)]
    me = lax.axis_index("ctx")
    order_table = jnp.array(order, jnp.int32)
    my_place = jnp.array(place, jnp.int32)[me]

    def product(cols, block):
        return tuple(
            jnp.dot(cols, block[:, field, :], preferred_element_type=jnp.float32)
            for field in range(block.shape[1])
        )

    def plus(left, right):
        return tuple(a + b for a, b in zip(left, right))

    def partial(block, source, start, width):
        cols = lax.dynamic_slice_in_dim(tokens, source * rows + start, width, 1)
        return product(cols, block)

    total = partial(in_weight, me, 0, rows)
    full_steps = (count - 1) // 2
    half = rows // 2

    def sources(step):
        return (
            order_table[(my_place - step) % count],
            order_table[(my_place + step) % count],
        )

    def add_pair(total, ahead, behind, step):
        from_behind, from_ahead = sources(step)
        total = plus(total, partial(ahead, from_behind, 0, rows))
        return plus(total, partial(behind, from_ahead, 0, rows))

    def ring_step(step, carry):
        ahead, behind, total = carry
        moved_ahead = lax.ppermute(ahead, "ctx", forward)
        moved_behind = lax.ppermute(behind, "ctx", backward)
        total = add_pair(total, ahead, behind, step - 1)
        return (moved_ahead, moved_behind, total)

    if full_steps == 0:
        return tuple(((part, None),) for part in total), riders, None
    ahead = lax.ppermute(in_weight, "ctx", forward)
    behind = lax.ppermute(in_weight, "ctx", backward)
    carry = (ahead, behind, total)
    if full_steps >= 2:
        carry = ring_step(2, carry)
    carry, riders = lax.optimization_barrier((carry, riders))

    def carried_step(step, state):
        return (ring_step(step, state[0]), state[1])

    carry, riders = lax.fori_loop(3, full_steps + 1, carried_step, (carry, riders))
    ahead, behind, total = carry
    if count % 2 == 0:
        last_ahead = lax.ppermute(ahead[:half], "ctx", forward)
        last_behind = lax.ppermute(behind[half:], "ctx", backward)
        from_behind_full, from_ahead_full = sources(full_steps)
        first_terms = partial(ahead, from_behind_full, 0, rows)
        second_terms = partial(behind, from_ahead_full, 0, rows)
        from_behind, from_ahead = sources(full_steps + 1)
        cols = jnp.concatenate(
            [
                lax.dynamic_slice_in_dim(tokens, from_behind * rows, half, 1),
                lax.dynamic_slice_in_dim(tokens, from_ahead * rows + half, rows - half, 1),
            ],
            axis=1,
        )
        block = jnp.concatenate([last_ahead, last_behind], axis=0)
        terms = tuple(
            tuple((term, None) for term in group)
            for group in zip(total, first_terms, second_terms)
        )
        return terms, riders, (cols, block)
    else:
        from_behind_full, from_ahead_full = sources(full_steps)
        first_terms = partial(ahead, from_behind_full, 0, rows)
        second_terms = partial(behind, from_ahead_full, 0, rows)
        terms = tuple(
            tuple((term, None) for term in group)
            for group in zip(total, first_terms, second_terms)
        )
    return terms, riders, None


def tp_bits(count):
    bits = []
    bit = 1
    while bit < count:
        bits.append(bit)
        bit *= 2
    return bits


def spread_weights(out_weight):
    count = lax.axis_size("tp")
    me = lax.axis_index("tp")
    width = out_weight.shape[1] // count
    weights = [lax.dynamic_slice_in_dim(out_weight, me * width, width, 1)]
    for partner in range(1, count):
        pairs = [(k, k ^ partner) for k in range(count)]
        sent = lax.dynamic_slice_in_dim(out_weight, (me ^ partner) * width, width, 1)
        weights.append(lax.ppermute(sent, "tp", pairs))
    return tuple(weights)


def output_projection(gated, weights):
    count = lax.axis_size("tp")
    pieces = {0: gated}
    for bit in reversed(tp_bits(count)):
        pairs = [(k, k ^ bit) for k in range(count)]
        moved = {key ^ bit: lax.ppermute(piece, "tp", pairs) for key, piece in pieces.items()}
        pieces.update(moved)
    total = None
    for key in sorted(pieces):
        part = jnp.dot(pieces[key], weights[key], preferred_element_type=jnp.float32)
        total = part if total is None else total + part
    return total

def halo_rows(tail):
    ctx_count = lax.axis_size("ctx")
    tp_count = lax.axis_size("tp")
    shift = [(k, k + 1) for k in range(ctx_count - 1)]
    if tp_count % 2:
        return lax.ppermute(tail, "ctx", shift)
    width = tail.shape[1] // 2
    side = lax.axis_index("tp") % 2
    mine = lax.ppermute(lax.dynamic_slice_in_dim(tail, side * width, width, 1), "ctx", shift)
    other = lax.ppermute(mine, "tp", [(k, k ^ 1) for k in range(tp_count)])
    return jnp.where(
        side == 0,
        jnp.concatenate([mine, other], axis=1),
        jnp.concatenate([other, mine], axis=1),
    )


def per_device(tokens, in_weight, short_taps, medium_taps, medium_decay, skip_gain, out_weight):
    row_count = tokens.shape[0]
    channel_count = in_weight.shape[2]
    ctx_count = lax.axis_size("ctx")
    medium_count = medium_taps.shape[1]
    short_count = short_taps.shape[2]
    lag_values = lax.broadcasted_iota(jnp.float32, (1, medium_count), 1)
    filters = medium_taps * jnp.exp(-medium_decay[:, None] * lag_values)
    taps = jnp.pad(
        jnp.transpose(short_taps, (0, 2, 1)), ((0, 0), (0, 8 - short_count), (0, 0))
    ).reshape(3 * 8, channel_count)
    tiles = channel_count // LANES
    split = (tiles * 5 + 7) // 8
    bounds = [0, split, tiles] if 0 < split < tiles else [0, tiles]
    parts = len(bounds) - 1
    medium = jnp.transpose(filters)
    features, weights, last = ring_projection(tokens, in_weight, spread_weights(out_weight), parts)
    tail = None
    skip = skip_gain.reshape(1, channel_count)
    total = None
    for part in range(parts):
        first, share = bounds[part], bounds[part + 1] - bounds[part]
        cols = slice(first * LANES, (first + share) * LANES)
        chosen = tuple(tuple((term, first) for term, _ in field) for field in features)
        if last is not None:
            cols_in, block = last
            if tail is not None:
                cols_in, block, _ = lax.optimization_barrier((cols_in, block, tail))
            chosen = tuple(
                field
                + (
                    (
                        jnp.dot(
                            cols_in,
                            block[:, index, cols],
                            preferred_element_type=jnp.float32,
                        ),
                        0,
                    ),
                )
                for index, field in enumerate(chosen)
            )
        tail = jnp.stack(
            [
                sum(
                    term[row_count - HALO :, cols] if shift else term[row_count - HALO :, : cols.stop - cols.start]
                    for term, shift in field
                ).astype(jnp.bfloat16)
                for field in chosen
            ]
        )
        halo = lax.ppermute(tail, "ctx", [(k, k + 1) for k in range(ctx_count - 1)])
        gated = channel_filter(halo, chosen, taps, medium, skip, first, share)
        piece = output_projection(gated, tuple(w[cols] for w in weights))
        total = piece if total is None else total + piece
    return total.astype(jnp.bfloat16)

def solution(mesh):
    return jax.shard_map(
        per_device,
        mesh=mesh,
        in_specs=(
            P("ctx", None),
            P("ctx", None, "tp"),
            P(None, "tp", None),
            P("tp", None),
            P("tp"),
            P("tp"),
            P("tp", None),
        ),
        out_specs=P("ctx", "tp"),
        check_vma=False,
    )
```

```python
import functools

import jax
import jax.numpy as jnp
from jax import lax
from jax.sharding import PartitionSpec as P


from jax.experimental import pallas as pl
from jax.experimental.pallas import tpu as pltpu

HALO = 136
CHUNK = 64
LANES = 128


def filter_kernel(term_count, halo, *refs):
    fields = refs[: 3 * term_count]
    taps, medium, skip, out, raw, prod, shifted, smooth_q = refs[3 * term_count :]
    local = fields[0].shape[0]
    ext = local + HALO
    taps_count = 7
    short_count = taps.shape[0] // 3
    for slot in range(3):
        raw[slot, 0:HALO, :] = halo[slot].astype(jnp.float32)

    def gather_body(index, carry):
        row = pl.multiple_of(index * CHUNK, 8)
        for slot in range(3):
            group = fields[slot * term_count : (slot + 1) * term_count]
            total = group[0][pl.ds(row, CHUNK), :]
            for term in group[1:]:
                total = total + term[pl.ds(row, CHUNK), :]
            raw[slot, pl.ds(row + HALO, CHUNK), :] = total.astype(jnp.bfloat16).astype(
                jnp.float32
            )
        return carry

    lax.fori_loop(0, local // CHUNK, gather_body, 0)

    def smooth(slot, row):
        window = raw[slot, pl.ds(row - 8, CHUNK + 8), :]
        total = jnp.zeros((CHUNK, LANES), jnp.float32)
        for lag in range(taps_count):
            weight = taps[pl.ds(slot * short_count + lag, 1), :]
            total = total + weight * window[8 - lag : 8 - lag + CHUNK]
        return total

    def product_body(index, carry):
        row = pl.multiple_of(8 + index * CHUNK, 8)
        prod[pl.ds(row, CHUNK), :] = smooth(1, row) * smooth(2, row)
        return carry

    lax.fori_loop(0, (ext - 8) // CHUNK, product_body, 0)

    def query_body(index, carry):
        row = pl.multiple_of(index * CHUNK, 8)
        smooth_q[pl.ds(row, CHUNK), :] = smooth(0, row + HALO)
        return carry

    lax.fori_loop(0, local // CHUNK, query_body, 0)

    def shift_body(index, carry):
        row = pl.multiple_of(16 + index * CHUNK, 8)
        window = prod[pl.ds(row - 8, CHUNK + 8), :]
        for shift in range(8):
            shifted[shift, pl.ds(row, CHUNK), :] = window[8 - shift : 8 - shift + CHUNK]
        return carry

    lax.fori_loop(0, (ext - 16) // CHUNK, shift_body, 0)
    tail = 16 + ((ext - 16) // CHUNK) * CHUNK
    if tail < ext:
        window = prod[tail - 8 : ext, :]
        for shift in range(8):
            shifted[shift, tail:ext, :] = window[8 - shift : 8 - shift + ext - tail]

    def chunk_body(index, carry):
        row = pl.multiple_of(index * CHUNK, CHUNK)
        at = pl.multiple_of(row + HALO, 8)
        total = (skip[...] * prod[pl.ds(at, CHUNK), :]).reshape(CHUNK // 8, 8, LANES)
        groups = medium.shape[0] // 64
        reach = 8 * (groups - 1)
        start = pl.multiple_of(at - reach, 8)
        for shift in range(8):
            window = shifted[shift, pl.ds(start, CHUNK + reach), :]
            for group in range(groups):
                offset = reach - 8 * group
                lag = 8 * group + shift
                weight = medium[8 * lag : 8 * lag + 8, :]
                part = window[offset : offset + CHUNK].reshape(CHUNK // 8, 8, LANES)
                total = total + weight[None] * part
        total = total.reshape(CHUNK, LANES)
        out[pl.ds(row, CHUNK), :] = (smooth_q[pl.ds(row, CHUNK), :] * total).astype(out.dtype)
        return carry

    lax.fori_loop(0, local // CHUNK, chunk_body, 0)


def channel_filter(halo, fields, taps, medium, skip, first, tiles):
    term_count = len(fields[0])
    local = fields[0][0][0].shape[0]
    ext = local + HALO
    channels = tiles * LANES

    def field_spec(shift):
        return pl.BlockSpec((local, LANES), lambda t: (0, shift + t))

    return pl.pallas_call(
        functools.partial(filter_kernel, term_count),
        grid=(tiles,),
        in_specs=[pl.BlockSpec((3, HALO, LANES), lambda t: (0, 0, t))]
        + [field_spec(shift) for field in fields for _, shift in field]
        + [
            pl.BlockSpec((taps.shape[0], LANES), lambda t: (0, first + t)),
            pl.BlockSpec((medium.shape[0], LANES), lambda t: (0, first + t)),
            pl.BlockSpec((1, LANES), lambda t: (0, first + t)),
        ],
        out_specs=pl.BlockSpec((local, LANES), lambda t: (0, t)),
        out_shape=jax.ShapeDtypeStruct((local, channels), jnp.bfloat16),
        scratch_shapes=[
            pltpu.VMEM((3, ext, LANES), jnp.float32),
            pltpu.VMEM((ext, LANES), jnp.float32),
            pltpu.VMEM((8, ext, LANES), jnp.float32),
            pltpu.VMEM((local, LANES), jnp.float32),
        ],
    )(halo, *[term for field in fields for term, _ in field], taps, medium, skip)

def ring_order(count):
    if count % 2:
        return list(range(count))
    return list(range(0, count, 2)) + list(range(count - 1, 0, -2))


def ring_projection(tokens, in_weight, riders, parts):
    count = lax.axis_size("ctx")
    rows = in_weight.shape[0]
    order = ring_order(count)
    place = [0] * count
    for at, member in enumerate(order):
        place[member] = at
    forward = [(order[k], order[(k + 1) % count]) for k in range(count)]
    backward = [(order[k], order[(k - 1) % count]) for k in range(count)]
    me = lax.axis_index("ctx")
    order_table = jnp.array(order, jnp.int32)
    my_place = jnp.array(place, jnp.int32)[me]

    def product(cols, block):
        return tuple(
            jnp.dot(cols, block[:, field, :], preferred_element_type=jnp.float32)
            for field in range(block.shape[1])
        )

    def plus(left, right):
        return tuple(a + b for a, b in zip(left, right))

    def partial(block, source, start, width):
        cols = lax.dynamic_slice_in_dim(tokens, source * rows + start, width, 1)
        return product(cols, block)

    total = partial(in_weight, me, 0, rows)
    full_steps = (count - 1) // 2
    half = rows // 2

    def sources(step):
        return (
            order_table[(my_place - step) % count],
            order_table[(my_place + step) % count],
        )

    def add_pair(total, ahead, behind, step):
        from_behind, from_ahead = sources(step)
        total = plus(total, partial(ahead, from_behind, 0, rows))
        return plus(total, partial(behind, from_ahead, 0, rows))

    def ring_step(step, carry):
        ahead, behind, total = carry
        moved_ahead = lax.ppermute(ahead, "ctx", forward)
        moved_behind = lax.ppermute(behind, "ctx", backward)
        total = add_pair(total, ahead, behind, step - 1)
        return (moved_ahead, moved_behind, total)

    if full_steps == 0:
        return tuple(((part, None),) for part in total), riders, None
    ahead = lax.ppermute(in_weight, "ctx", forward)
    behind = lax.ppermute(in_weight, "ctx", backward)
    carry = (ahead, behind, total)
    if full_steps >= 2:
        carry = ring_step(2, carry)
    carry, riders = lax.optimization_barrier((carry, riders))

    def carried_step(step, state):
        return (ring_step(step, state[0]), state[1])

    carry, riders = lax.fori_loop(3, full_steps + 1, carried_step, (carry, riders))
    ahead, behind, total = carry
    if count % 2 == 0:
        last_ahead = lax.ppermute(ahead[:half], "ctx", forward)
        last_behind = lax.ppermute(behind[half:], "ctx", backward)
        from_behind_full, from_ahead_full = sources(full_steps)
        first_terms = partial(ahead, from_behind_full, 0, rows)
        second_terms = partial(behind, from_ahead_full, 0, rows)
        from_behind, from_ahead = sources(full_steps + 1)
        cols = jnp.concatenate(
            [
                lax.dynamic_slice_in_dim(tokens, from_behind * rows, half, 1),
                lax.dynamic_slice_in_dim(tokens, from_ahead * rows + half, rows - half, 1),
            ],
            axis=1,
        )
        block = jnp.concatenate([last_ahead, last_behind], axis=0)
        terms = tuple(
            tuple((term, None) for term in group)
            for group in zip(total, first_terms, second_terms)
        )
        return terms, riders, (cols, block)
    else:
        from_behind_full, from_ahead_full = sources(full_steps)
        first_terms = partial(ahead, from_behind_full, 0, rows)
        second_terms = partial(behind, from_ahead_full, 0, rows)
        terms = tuple(
            tuple((term, None) for term in group)
            for group in zip(total, first_terms, second_terms)
        )
    return terms, riders, None


def tp_bits(count):
    bits = []
    bit = 1
    while bit < count:
        bits.append(bit)
        bit *= 2
    return bits


def spread_weights(out_weight):
    count = lax.axis_size("tp")
    me = lax.axis_index("tp")
    width = out_weight.shape[1] // count
    weights = [lax.dynamic_slice_in_dim(out_weight, me * width, width, 1)]
    for partner in range(1, count):
        pairs = [(k, k ^ partner) for k in range(count)]
        sent = lax.dynamic_slice_in_dim(out_weight, (me ^ partner) * width, width, 1)
        weights.append(lax.ppermute(sent, "tp", pairs))
    return tuple(weights)


def output_projection(gated, weights):
    count = lax.axis_size("tp")
    pieces = {0: gated}
    for bit in reversed(tp_bits(count)):
        pairs = [(k, k ^ bit) for k in range(count)]
        moved = {key ^ bit: lax.ppermute(piece, "tp", pairs) for key, piece in pieces.items()}
        pieces.update(moved)
    total = None
    for key in sorted(pieces):
        part = jnp.dot(pieces[key], weights[key], preferred_element_type=jnp.float32)
        total = part if total is None else total + part
    return total

def halo_rows(tail):
    ctx_count = lax.axis_size("ctx")
    tp_count = lax.axis_size("tp")
    shift = [(k, k + 1) for k in range(ctx_count - 1)]
    if tp_count % 2:
        return lax.ppermute(tail, "ctx", shift)
    width = tail.shape[1] // 2
    side = lax.axis_index("tp") % 2
    mine = lax.ppermute(lax.dynamic_slice_in_dim(tail, side * width, width, 1), "ctx", shift)
    other = lax.ppermute(mine, "tp", [(k, k ^ 1) for k in range(tp_count)])
    return jnp.where(
        side == 0,
        jnp.concatenate([mine, other], axis=1),
        jnp.concatenate([other, mine], axis=1),
    )


def per_device(tokens, in_weight, short_taps, medium_taps, medium_decay, skip_gain, out_weight):
    row_count = tokens.shape[0]
    channel_count = in_weight.shape[2]
    ctx_count = lax.axis_size("ctx")
    medium_count = medium_taps.shape[1]
    short_count = short_taps.shape[2]
    lag_values = lax.broadcasted_iota(jnp.float32, (1, medium_count), 1)
    filters = medium_taps * jnp.exp(-medium_decay[:, None] * lag_values)
    taps = jnp.pad(
        jnp.transpose(short_taps, (0, 2, 1)), ((0, 0), (0, 8 - short_count), (0, 0))
    ).reshape(3 * 8, channel_count)
    tiles = channel_count // LANES
    parts = 2 if tiles % 2 == 0 else 1
    share = tiles // parts
    medium = jnp.repeat(jnp.transpose(filters), 8, axis=0)
    features, weights, last = ring_projection(tokens, in_weight, spread_weights(out_weight), parts)
    tail = None
    skip = skip_gain.reshape(1, channel_count)
    total = None
    for part in range(parts):
        cols = slice(part * share * LANES, (part + 1) * share * LANES)
        chosen = tuple(tuple((term, part * share) for term, _ in field) for field in features)
        if last is not None:
            cols_in, block = last
            if tail is not None:
                cols_in, block, _ = lax.optimization_barrier((cols_in, block, tail))
            chosen = tuple(
                field
                + (
                    (
                        jnp.dot(
                            cols_in,
                            block[:, index, cols],
                            preferred_element_type=jnp.float32,
                        ),
                        0,
                    ),
                )
                for index, field in enumerate(chosen)
            )
        tail = jnp.stack(
            [
                sum(
                    term[row_count - HALO :, cols] if shift else term[row_count - HALO :, : cols.stop - cols.start]
                    for term, shift in field
                ).astype(jnp.bfloat16)
                for field in chosen
            ]
        )
        halo = lax.ppermute(tail, "ctx", [(k, k + 1) for k in range(ctx_count - 1)])
        gated = channel_filter(halo, chosen, taps, medium, skip, part * share, share)
        rows = slice(part * share * LANES, (part + 1) * share * LANES)
        piece = output_projection(gated, tuple(w[rows] for w in weights))
        total = piece if total is None else total + piece
    return total.astype(jnp.bfloat16)

def solution(mesh):
    return jax.shard_map(
        per_device,
        mesh=mesh,
        in_specs=(
            P("ctx", None),
            P("ctx", None, "tp"),
            P(None, "tp", None),
            P("tp", None),
            P("tp"),
            P("tp"),
            P("tp", None),
        ),
        out_specs=P("ctx", "tp"),
        check_vma=False,
    )
```

```python
import functools

import jax
import jax.numpy as jnp
from jax import lax
from jax.sharding import PartitionSpec as P


from jax.experimental import pallas as pl
from jax.experimental.pallas import tpu as pltpu

HALO = 136
CHUNK = 64
LANES = 128


def filter_kernel(term_count, halo, *refs):
    fields = refs[: 3 * term_count]
    taps, medium, skip, out, raw, prod, shifted, smooth_q = refs[3 * term_count :]
    local = fields[0].shape[0]
    ext = local + HALO
    taps_count = 7
    short_count = taps.shape[0] // 3
    for slot in range(3):
        raw[slot, 0:HALO, :] = halo[slot].astype(jnp.float32)

    def gather_body(index, carry):
        row = pl.multiple_of(index * CHUNK, 8)
        for slot in range(3):
            group = fields[slot * term_count : (slot + 1) * term_count]
            total = group[0][pl.ds(row, CHUNK), :]
            for term in group[1:]:
                total = total + term[pl.ds(row, CHUNK), :]
            raw[slot, pl.ds(row + HALO, CHUNK), :] = total.astype(jnp.bfloat16).astype(
                jnp.float32
            )
        return carry

    lax.fori_loop(0, local // CHUNK, gather_body, 0)

    def smooth(slot, row):
        window = raw[slot, pl.ds(row - 8, CHUNK + 8), :]
        total = jnp.zeros((CHUNK, LANES), jnp.float32)
        for lag in range(taps_count):
            weight = taps[pl.ds(slot * short_count + lag, 1), :]
            total = total + weight * window[8 - lag : 8 - lag + CHUNK]
        return total

    def product_body(index, carry):
        row = pl.multiple_of(8 + index * CHUNK, 8)
        prod[pl.ds(row, CHUNK), :] = smooth(1, row) * smooth(2, row)
        return carry

    lax.fori_loop(0, (ext - 8) // CHUNK, product_body, 0)

    def query_body(index, carry):
        row = pl.multiple_of(index * CHUNK, 8)
        smooth_q[pl.ds(row, CHUNK), :] = smooth(0, row + HALO)
        return carry

    lax.fori_loop(0, local // CHUNK, query_body, 0)

    def shift_body(index, carry):
        row = pl.multiple_of(16 + index * CHUNK, 8)
        window = prod[pl.ds(row - 8, CHUNK + 8), :]
        for shift in range(8):
            shifted[shift, pl.ds(row, CHUNK), :] = window[8 - shift : 8 - shift + CHUNK]
        return carry

    lax.fori_loop(0, (ext - 16) // CHUNK, shift_body, 0)
    tail = 16 + ((ext - 16) // CHUNK) * CHUNK
    if tail < ext:
        window = prod[tail - 8 : ext, :]
        for shift in range(8):
            shifted[shift, tail:ext, :] = window[8 - shift : 8 - shift + ext - tail]

    def chunk_body(index, carry):
        row = pl.multiple_of(index * CHUNK, CHUNK)
        at = pl.multiple_of(row + HALO, 8)
        total = skip[...] * prod[pl.ds(at, CHUNK), :]
        groups = medium.shape[0] // 8
        reach = 8 * (groups - 1)
        start = pl.multiple_of(at - reach, 8)
        for shift in range(8):
            window = shifted[shift, pl.ds(start, CHUNK + reach), :]
            for group in range(groups):
                offset = reach - 8 * group
                weight = medium[pl.ds(8 * group + shift, 1), :]
                total = total + weight * window[offset : offset + CHUNK]
        out[pl.ds(row, CHUNK), :] = (smooth_q[pl.ds(row, CHUNK), :] * total).astype(out.dtype)
        return carry

    lax.fori_loop(0, local // CHUNK, chunk_body, 0)


def channel_filter(halo, fields, taps, medium, skip, first, tiles):
    term_count = len(fields[0])
    local = fields[0][0][0].shape[0]
    ext = local + HALO
    channels = tiles * LANES

    def field_spec(shift):
        return pl.BlockSpec((local, LANES), lambda t: (0, shift + t))

    return pl.pallas_call(
        functools.partial(filter_kernel, term_count),
        grid=(tiles,),
        in_specs=[pl.BlockSpec((3, HALO, LANES), lambda t: (0, 0, t))]
        + [field_spec(shift) for field in fields for _, shift in field]
        + [
            pl.BlockSpec((taps.shape[0], LANES), lambda t: (0, first + t)),
            pl.BlockSpec((medium.shape[0], LANES), lambda t: (0, first + t)),
            pl.BlockSpec((1, LANES), lambda t: (0, first + t)),
        ],
        out_specs=pl.BlockSpec((local, LANES), lambda t: (0, t)),
        out_shape=jax.ShapeDtypeStruct((local, channels), jnp.bfloat16),
        scratch_shapes=[
            pltpu.VMEM((3, ext, LANES), jnp.float32),
            pltpu.VMEM((ext, LANES), jnp.float32),
            pltpu.VMEM((8, ext, LANES), jnp.float32),
            pltpu.VMEM((local, LANES), jnp.float32),
        ],
    )(halo, *[term for field in fields for term, _ in field], taps, medium, skip)

def ring_order(count):
    if count % 2:
        return list(range(count))
    return list(range(0, count, 2)) + list(range(count - 1, 0, -2))


def ring_projection(tokens, in_weight, riders, parts):
    count = lax.axis_size("ctx")
    rows = in_weight.shape[0]
    order = ring_order(count)
    place = [0] * count
    for at, member in enumerate(order):
        place[member] = at
    forward = [(order[k], order[(k + 1) % count]) for k in range(count)]
    backward = [(order[k], order[(k - 1) % count]) for k in range(count)]
    me = lax.axis_index("ctx")
    order_table = jnp.array(order, jnp.int32)
    my_place = jnp.array(place, jnp.int32)[me]

    def product(cols, block):
        return tuple(
            jnp.dot(cols, block[:, field, :], preferred_element_type=jnp.float32)
            for field in range(block.shape[1])
        )

    def plus(left, right):
        return tuple(a + b for a, b in zip(left, right))

    def partial(block, source, start, width):
        cols = lax.dynamic_slice_in_dim(tokens, source * rows + start, width, 1)
        return product(cols, block)

    total = partial(in_weight, me, 0, rows)
    full_steps = (count - 1) // 2
    half = rows // 2

    def sources(step):
        return (
            order_table[(my_place - step) % count],
            order_table[(my_place + step) % count],
        )

    def add_pair(total, ahead, behind, step):
        from_behind, from_ahead = sources(step)
        total = plus(total, partial(ahead, from_behind, 0, rows))
        return plus(total, partial(behind, from_ahead, 0, rows))

    def ring_step(step, carry):
        ahead, behind, total = carry
        moved_ahead = lax.ppermute(ahead, "ctx", forward)
        moved_behind = lax.ppermute(behind, "ctx", backward)
        total = add_pair(total, ahead, behind, step - 1)
        return (moved_ahead, moved_behind, total)

    if full_steps == 0:
        return tuple(((part, None),) for part in total), riders, None
    ahead = lax.ppermute(in_weight, "ctx", forward)
    behind = lax.ppermute(in_weight, "ctx", backward)
    carry = (ahead, behind, total)
    if full_steps >= 2:
        carry = ring_step(2, carry)
    carry, riders = lax.optimization_barrier((carry, riders))

    def carried_step(step, state):
        return (ring_step(step, state[0]), state[1])

    carry, riders = lax.fori_loop(3, full_steps + 1, carried_step, (carry, riders))
    ahead, behind, total = carry
    if count % 2 == 0:
        last_ahead = lax.ppermute(ahead[:half], "ctx", forward)
        last_behind = lax.ppermute(behind[half:], "ctx", backward)
        from_behind_full, from_ahead_full = sources(full_steps)
        first_terms = partial(ahead, from_behind_full, 0, rows)
        second_terms = partial(behind, from_ahead_full, 0, rows)
        from_behind, from_ahead = sources(full_steps + 1)
        cols = jnp.concatenate(
            [
                lax.dynamic_slice_in_dim(tokens, from_behind * rows, half, 1),
                lax.dynamic_slice_in_dim(tokens, from_ahead * rows + half, rows - half, 1),
            ],
            axis=1,
        )
        block = jnp.concatenate([last_ahead, last_behind], axis=0)
        terms = tuple(
            tuple((term, None) for term in group)
            for group in zip(total, first_terms, second_terms)
        )
        return terms, riders, (cols, block)
    else:
        from_behind_full, from_ahead_full = sources(full_steps)
        first_terms = partial(ahead, from_behind_full, 0, rows)
        second_terms = partial(behind, from_ahead_full, 0, rows)
        terms = tuple(
            tuple((term, None) for term in group)
            for group in zip(total, first_terms, second_terms)
        )
    return terms, riders, None


def tp_bits(count):
    bits = []
    bit = 1
    while bit < count:
        bits.append(bit)
        bit *= 2
    return bits


def spread_weights(out_weight):
    count = lax.axis_size("tp")
    me = lax.axis_index("tp")
    width = out_weight.shape[1] // count
    weights = [lax.dynamic_slice_in_dim(out_weight, me * width, width, 1)]
    for partner in range(1, count):
        pairs = [(k, k ^ partner) for k in range(count)]
        sent = lax.dynamic_slice_in_dim(out_weight, (me ^ partner) * width, width, 1)
        weights.append(lax.ppermute(sent, "tp", pairs))
    return tuple(weights)


def output_projection(gated, weights, earlier):
    count = lax.axis_size("tp")
    pieces = {0: gated}
    for bit in reversed(tp_bits(count)):
        pairs = [(k, k ^ bit) for k in range(count)]
        moved = {key ^ bit: lax.ppermute(piece, "tp", pairs) for key, piece in pieces.items()}
        if earlier is not None:
            moved, earlier = lax.optimization_barrier((moved, earlier))
        pieces.update(moved)
    total = earlier
    for key in sorted(pieces):
        part = jnp.dot(pieces[key], weights[key], preferred_element_type=jnp.float32)
        total = part if total is None else total + part
    return total

def halo_rows(tail):
    ctx_count = lax.axis_size("ctx")
    tp_count = lax.axis_size("tp")
    shift = [(k, k + 1) for k in range(ctx_count - 1)]
    if tp_count % 2:
        return lax.ppermute(tail, "ctx", shift)
    width = tail.shape[1] // 2
    side = lax.axis_index("tp") % 2
    mine = lax.ppermute(lax.dynamic_slice_in_dim(tail, side * width, width, 1), "ctx", shift)
    other = lax.ppermute(mine, "tp", [(k, k ^ 1) for k in range(tp_count)])
    return jnp.where(
        side == 0,
        jnp.concatenate([mine, other], axis=1),
        jnp.concatenate([other, mine], axis=1),
    )


def per_device(tokens, in_weight, short_taps, medium_taps, medium_decay, skip_gain, out_weight):
    row_count = tokens.shape[0]
    channel_count = in_weight.shape[2]
    ctx_count = lax.axis_size("ctx")
    medium_count = medium_taps.shape[1]
    short_count = short_taps.shape[2]
    lag_values = lax.broadcasted_iota(jnp.float32, (1, medium_count), 1)
    filters = medium_taps * jnp.exp(-medium_decay[:, None] * lag_values)
    taps = jnp.pad(
        jnp.transpose(short_taps, (0, 2, 1)), ((0, 0), (0, 8 - short_count), (0, 0))
    ).reshape(3 * 8, channel_count)
    tiles = channel_count // LANES
    parts = 2 if tiles % 2 == 0 else 1
    share = tiles // parts
    medium = jnp.transpose(filters)
    features, weights, last = ring_projection(tokens, in_weight, spread_weights(out_weight), parts)
    tail = None
    skip = skip_gain.reshape(1, channel_count)
    total = None
    for part in range(parts):
        cols = slice(part * share * LANES, (part + 1) * share * LANES)
        chosen = tuple(tuple((term, part * share) for term, _ in field) for field in features)
        if last is not None:
            cols_in, block = last
            if tail is not None:
                cols_in, block, _ = lax.optimization_barrier((cols_in, block, tail))
            chosen = tuple(
                field
                + (
                    (
                        jnp.dot(
                            cols_in,
                            block[:, index, cols],
                            preferred_element_type=jnp.float32,
                        ),
                        0,
                    ),
                )
                for index, field in enumerate(chosen)
            )
        tail = jnp.stack(
            [
                sum(
                    term[row_count - HALO :, cols] if shift else term[row_count - HALO :, : cols.stop - cols.start]
                    for term, shift in field
                ).astype(jnp.bfloat16)
                for field in chosen
            ]
        )
        halo = lax.ppermute(tail, "ctx", [(k, k + 1) for k in range(ctx_count - 1)])
        gated = channel_filter(halo, chosen, taps, medium, skip, part * share, share)
        rows = slice(part * share * LANES, (part + 1) * share * LANES)
        total = output_projection(gated, tuple(w[rows] for w in weights), total)
    return total.astype(jnp.bfloat16)

def solution(mesh):
    return jax.shard_map(
        per_device,
        mesh=mesh,
        in_specs=(
            P("ctx", None),
            P("ctx", None, "tp"),
            P(None, "tp", None),
            P("tp", None),
            P("tp"),
            P("tp"),
            P("tp", None),
        ),
        out_specs=P("ctx", "tp"),
        check_vma=False,
    )
```

```python
import functools

import jax
import jax.numpy as jnp
from jax import lax
from jax.sharding import PartitionSpec as P


from jax.experimental import pallas as pl
from jax.experimental.pallas import tpu as pltpu

HALO = 136
CHUNK = 64
MAIN = 128
LANES = 128


def filter_kernel(term_count, halo, *refs):
    fields = refs[: 3 * term_count]
    taps, medium, skip, out, raw, prod, shifted, smooth_q = refs[3 * term_count :]
    local = fields[0].shape[0]
    ext = local + HALO
    taps_count = 7
    short_count = taps.shape[0] // 3
    for slot in range(3):
        raw[slot, 0:HALO, :] = halo[slot].astype(jnp.float32)

    def gather_body(index, carry):
        row = pl.multiple_of(index * CHUNK, 8)
        for slot in range(3):
            group = fields[slot * term_count : (slot + 1) * term_count]
            total = group[0][pl.ds(row, CHUNK), :]
            for term in group[1:]:
                total = total + term[pl.ds(row, CHUNK), :]
            raw[slot, pl.ds(row + HALO, CHUNK), :] = total.astype(jnp.bfloat16).astype(
                jnp.float32
            )
        return carry

    lax.fori_loop(0, local // CHUNK, gather_body, 0)

    def smooth(slot, row):
        window = raw[slot, pl.ds(row - 8, CHUNK + 8), :]
        total = jnp.zeros((CHUNK, LANES), jnp.float32)
        for lag in range(taps_count):
            weight = taps[pl.ds(slot * short_count + lag, 1), :]
            total = total + weight * window[8 - lag : 8 - lag + CHUNK]
        return total

    def product_body(index, carry):
        row = pl.multiple_of(8 + index * CHUNK, 8)
        prod[pl.ds(row, CHUNK), :] = smooth(1, row) * smooth(2, row)
        return carry

    lax.fori_loop(0, (ext - 8) // CHUNK, product_body, 0)

    def query_body(index, carry):
        row = pl.multiple_of(index * CHUNK, 8)
        smooth_q[pl.ds(row, CHUNK), :] = smooth(0, row + HALO)
        return carry

    lax.fori_loop(0, local // CHUNK, query_body, 0)

    def shift_body(index, carry):
        row = pl.multiple_of(16 + index * CHUNK, 8)
        window = prod[pl.ds(row - 8, CHUNK + 8), :]
        for shift in range(8):
            shifted[shift, pl.ds(row, CHUNK), :] = window[8 - shift : 8 - shift + CHUNK]
        return carry

    lax.fori_loop(0, (ext - 16) // CHUNK, shift_body, 0)
    tail = 16 + ((ext - 16) // CHUNK) * CHUNK
    if tail < ext:
        window = prod[tail - 8 : ext, :]
        for shift in range(8):
            shifted[shift, tail:ext, :] = window[8 - shift : 8 - shift + ext - tail]

    def chunk_body(index, carry):
        row = pl.multiple_of(index * MAIN, MAIN)
        at = pl.multiple_of(row + HALO, 8)
        total = skip[...] * prod[pl.ds(at, MAIN), :]
        groups = medium.shape[0] // 8
        reach = 8 * (groups - 1)
        start = pl.multiple_of(at - reach, 8)
        for shift in range(8):
            window = shifted[shift, pl.ds(start, MAIN + reach), :]
            for group in range(groups):
                offset = reach - 8 * group
                weight = medium[pl.ds(8 * group + shift, 1), :]
                total = total + weight * window[offset : offset + MAIN]
        out[pl.ds(row, MAIN), :] = (smooth_q[pl.ds(row, MAIN), :] * total).astype(out.dtype)
        return carry

    lax.fori_loop(0, local // MAIN, chunk_body, 0)


def channel_filter(halo, fields, taps, medium, skip, first, tiles):
    term_count = len(fields[0])
    local = fields[0][0][0].shape[0]
    ext = local + HALO
    channels = tiles * LANES

    def field_spec(shift):
        return pl.BlockSpec((local, LANES), lambda t: (0, shift + t))

    return pl.pallas_call(
        functools.partial(filter_kernel, term_count),
        grid=(tiles,),
        in_specs=[pl.BlockSpec((3, HALO, LANES), lambda t: (0, 0, t))]
        + [field_spec(shift) for field in fields for _, shift in field]
        + [
            pl.BlockSpec((taps.shape[0], LANES), lambda t: (0, first + t)),
            pl.BlockSpec((medium.shape[0], LANES), lambda t: (0, first + t)),
            pl.BlockSpec((1, LANES), lambda t: (0, first + t)),
        ],
        out_specs=pl.BlockSpec((local, LANES), lambda t: (0, t)),
        out_shape=jax.ShapeDtypeStruct((local, channels), jnp.bfloat16),
        scratch_shapes=[
            pltpu.VMEM((3, ext, LANES), jnp.float32),
            pltpu.VMEM((ext, LANES), jnp.float32),
            pltpu.VMEM((8, ext, LANES), jnp.float32),
            pltpu.VMEM((local, LANES), jnp.float32),
        ],
    )(halo, *[term for field in fields for term, _ in field], taps, medium, skip)

def ring_order(count):
    if count % 2:
        return list(range(count))
    return list(range(0, count, 2)) + list(range(count - 1, 0, -2))


def ring_projection(tokens, in_weight, riders, parts):
    count = lax.axis_size("ctx")
    rows = in_weight.shape[0]
    order = ring_order(count)
    place = [0] * count
    for at, member in enumerate(order):
        place[member] = at
    forward = [(order[k], order[(k + 1) % count]) for k in range(count)]
    backward = [(order[k], order[(k - 1) % count]) for k in range(count)]
    me = lax.axis_index("ctx")
    order_table = jnp.array(order, jnp.int32)
    my_place = jnp.array(place, jnp.int32)[me]

    def product(cols, block):
        return tuple(
            jnp.dot(cols, block[:, field, :], preferred_element_type=jnp.float32)
            for field in range(block.shape[1])
        )

    def plus(left, right):
        return tuple(a + b for a, b in zip(left, right))

    def partial(block, source, start, width):
        cols = lax.dynamic_slice_in_dim(tokens, source * rows + start, width, 1)
        return product(cols, block)

    total = partial(in_weight, me, 0, rows)
    full_steps = (count - 1) // 2
    half = rows // 2

    def sources(step):
        return (
            order_table[(my_place - step) % count],
            order_table[(my_place + step) % count],
        )

    def add_pair(total, ahead, behind, step):
        from_behind, from_ahead = sources(step)
        total = plus(total, partial(ahead, from_behind, 0, rows))
        return plus(total, partial(behind, from_ahead, 0, rows))

    def ring_step(step, carry):
        ahead, behind, total = carry
        moved_ahead = lax.ppermute(ahead, "ctx", forward)
        moved_behind = lax.ppermute(behind, "ctx", backward)
        total = add_pair(total, ahead, behind, step - 1)
        return (moved_ahead, moved_behind, total)

    if full_steps == 0:
        return tuple(((part, None),) for part in total), riders, None
    ahead = lax.ppermute(in_weight, "ctx", forward)
    behind = lax.ppermute(in_weight, "ctx", backward)
    carry = (ahead, behind, total)
    if full_steps >= 2:
        carry = ring_step(2, carry)
    carry, riders = lax.optimization_barrier((carry, riders))

    def carried_step(step, state):
        return (ring_step(step, state[0]), state[1])

    carry, riders = lax.fori_loop(3, full_steps + 1, carried_step, (carry, riders))
    ahead, behind, total = carry
    if count % 2 == 0:
        last_ahead = lax.ppermute(ahead[:half], "ctx", forward)
        last_behind = lax.ppermute(behind[half:], "ctx", backward)
        from_behind_full, from_ahead_full = sources(full_steps)
        first_terms = partial(ahead, from_behind_full, 0, rows)
        second_terms = partial(behind, from_ahead_full, 0, rows)
        from_behind, from_ahead = sources(full_steps + 1)
        cols = jnp.concatenate(
            [
                lax.dynamic_slice_in_dim(tokens, from_behind * rows, half, 1),
                lax.dynamic_slice_in_dim(tokens, from_ahead * rows + half, rows - half, 1),
            ],
            axis=1,
        )
        block = jnp.concatenate([last_ahead, last_behind], axis=0)
        terms = tuple(
            tuple((term, None) for term in group)
            for group in zip(total, first_terms, second_terms)
        )
        return terms, riders, (cols, block)
    else:
        from_behind_full, from_ahead_full = sources(full_steps)
        first_terms = partial(ahead, from_behind_full, 0, rows)
        second_terms = partial(behind, from_ahead_full, 0, rows)
        terms = tuple(
            tuple((term, None) for term in group)
            for group in zip(total, first_terms, second_terms)
        )
    return terms, riders, None


def tp_bits(count):
    bits = []
    bit = 1
    while bit < count:
        bits.append(bit)
        bit *= 2
    return bits


def spread_weights(out_weight):
    count = lax.axis_size("tp")
    me = lax.axis_index("tp")
    width = out_weight.shape[1] // count
    weights = [lax.dynamic_slice_in_dim(out_weight, me * width, width, 1)]
    for partner in range(1, count):
        pairs = [(k, k ^ partner) for k in range(count)]
        sent = lax.dynamic_slice_in_dim(out_weight, (me ^ partner) * width, width, 1)
        weights.append(lax.ppermute(sent, "tp", pairs))
    return tuple(weights)


def output_projection(gated, weights):
    count = lax.axis_size("tp")
    pieces = {0: gated}
    for bit in reversed(tp_bits(count)):
        pairs = [(k, k ^ bit) for k in range(count)]
        moved = {key ^ bit: lax.ppermute(piece, "tp", pairs) for key, piece in pieces.items()}
        pieces.update(moved)
    total = None
    for key in sorted(pieces):
        part = jnp.dot(pieces[key], weights[key], preferred_element_type=jnp.float32)
        total = part if total is None else total + part
    return total

def halo_rows(tail):
    ctx_count = lax.axis_size("ctx")
    tp_count = lax.axis_size("tp")
    shift = [(k, k + 1) for k in range(ctx_count - 1)]
    if tp_count % 2:
        return lax.ppermute(tail, "ctx", shift)
    width = tail.shape[1] // 2
    side = lax.axis_index("tp") % 2
    mine = lax.ppermute(lax.dynamic_slice_in_dim(tail, side * width, width, 1), "ctx", shift)
    other = lax.ppermute(mine, "tp", [(k, k ^ 1) for k in range(tp_count)])
    return jnp.where(
        side == 0,
        jnp.concatenate([mine, other], axis=1),
        jnp.concatenate([other, mine], axis=1),
    )


def per_device(tokens, in_weight, short_taps, medium_taps, medium_decay, skip_gain, out_weight):
    row_count = tokens.shape[0]
    channel_count = in_weight.shape[2]
    ctx_count = lax.axis_size("ctx")
    medium_count = medium_taps.shape[1]
    short_count = short_taps.shape[2]
    lag_values = lax.broadcasted_iota(jnp.float32, (1, medium_count), 1)
    filters = medium_taps * jnp.exp(-medium_decay[:, None] * lag_values)
    taps = jnp.pad(
        jnp.transpose(short_taps, (0, 2, 1)), ((0, 0), (0, 8 - short_count), (0, 0))
    ).reshape(3 * 8, channel_count)
    tiles = channel_count // LANES
    parts = 2 if tiles % 2 == 0 else 1
    share = tiles // parts
    medium = jnp.transpose(filters)
    features, weights, last = ring_projection(tokens, in_weight, spread_weights(out_weight), parts)
    tail = None
    skip = skip_gain.reshape(1, channel_count)
    total = None
    for part in range(parts):
        cols = slice(part * share * LANES, (part + 1) * share * LANES)
        chosen = tuple(tuple((term, part * share) for term, _ in field) for field in features)
        if last is not None:
            cols_in, block = last
            if tail is not None:
                cols_in, block, _ = lax.optimization_barrier((cols_in, block, tail))
            chosen = tuple(
                field
                + (
                    (
                        jnp.dot(
                            cols_in,
                            block[:, index, cols],
                            preferred_element_type=jnp.float32,
                        ),
                        0,
                    ),
                )
                for index, field in enumerate(chosen)
            )
        tail = jnp.stack(
            [
                sum(
                    term[row_count - HALO :, cols] if shift else term[row_count - HALO :, : cols.stop - cols.start]
                    for term, shift in field
                ).astype(jnp.bfloat16)
                for field in chosen
            ]
        )
        halo = lax.ppermute(tail, "ctx", [(k, k + 1) for k in range(ctx_count - 1)])
        gated = channel_filter(halo, chosen, taps, medium, skip, part * share, share)
        rows = slice(part * share * LANES, (part + 1) * share * LANES)
        piece = output_projection(gated, tuple(w[rows] for w in weights))
        total = piece if total is None else total + piece
    return total.astype(jnp.bfloat16)

def solution(mesh):
    return jax.shard_map(
        per_device,
        mesh=mesh,
        in_specs=(
            P("ctx", None),
            P("ctx", None, "tp"),
            P(None, "tp", None),
            P("tp", None),
            P("tp"),
            P("tp"),
            P("tp", None),
        ),
        out_specs=P("ctx", "tp"),
        check_vma=False,
    )
```
